512 devices in a mesh: gx: 32 (over z, y_hi, core), gy: 16 (over x, y_lo).
Axes of the slice: x: 4, y: 8 (y_hi: 2, y_lo: 4; y = y_hi * 4 + y_lo), z: 8, core: 2. Of those that a mesh axis runs over, the one named last changes fastest.
Arguments:
- design: float32 [256, 128, 128], P('gx', 'gy'), may hold values from 0.06 to 0.9
- passive: int32 [256, 128, 128], P('gx', 'gy'), may hold values 0 or 1
- basis_pairs: float32 [4, 2, 3, 256, 128, 128], P(None, None, None, 'gx', 'gy'), may hold values from -6 to 6
- supports: int32 [256, 128, 128], P('gx', 'gy'), may hold values 0 or 1
- stiffness: float32 [24, 24], replicated, may hold values from -1.25 to 1.25
- mass_matrix: float32 [24, 24], replicated, may hold values from -1.25 to 1.25
- volume_fraction: float32 [64], replicated, may hold values from 0.26 to 0.36
Outputs:
- sensitivity: float32 [256, 128, 128], P('gx', 'gy')
- design_next: float32 [256, 128, 128], P('gx', 'gy')
The draws below stay inside these ranges and needn't reach their ends.
All inputs are finite; a program needn't handle non-finite values. No bound on the sum of `passive` or of `supports` on one device may be relied on, other than what follows from the above.
Results may differ from the reference program's by a relative error of at most 0.0003.
Values sent between devices are 32-bit elements; how exact they have to be, the bound alone decides.
No kernel may reach another device: no remote copies, remote signals or barrier semaphores. Data moves between devices by JAX's collectives and lax.ppermute only.
A program may use at most 64 MiB of HBM per device.

```python
import math
import jax
import jax.numpy as jnp
from jax import lax

EX = 8
NB = 4
BISECT = 6
REGIONS = 64
NX = 256
NY = 128
NZ = 128
N_GX = 32


def draw_design(key, part):
    across = jnp.arange(NX, dtype=jnp.float32) / max(NX - 1, 1)
    ramp = 0.3 + 0.6 * across
    base = jax.random.uniform(key, (NX, NY, NZ), jnp.float32, 0.2, 1.0)
    return (ramp[:, None, None] * base).astype(jnp.float32)


def plant(values, rng, least, largest):
    extent = values.shape
    index_at = [jax.random.randint(jax.random.fold_in(rng, axis), (), 0, extent[axis]) for axis in range(len(extent))]
    values = values.at[tuple(index_at)].set(least)
    longest = extent.index(max(extent))
    index_at[longest] = (index_at[longest] + 1) % extent[longest]
    return values.at[tuple(index_at)].set(largest)


def block_levels(key, extent, split, low, high):
    gain, own = 1.0, jax.random.fold_in(key, 6)
    for dim, blocks in split:
        steps = jnp.exp(jax.random.uniform(jax.random.fold_in(own, dim), (blocks,), jnp.float32, low / len(split), high / len(split)))
        gain = gain * jnp.repeat(steps, extent[dim] // blocks).reshape([-1 if axis == dim else 1 for axis in range(len(extent))])
    return gain


def bell_draw(rng, dims, deviation, bound, split=(), kind=jnp.bfloat16):
    level = block_levels(rng, dims, split, -0.22, 0.18) if split else 1.0
    entries = jax.random.normal(rng, dims, jnp.float32) * deviation * level
    return jnp.minimum(jnp.maximum(entries, -bound), bound).astype(kind)


def setup_inputs(seed: int = 0) -> dict:
    key_of = jax.random.split(jax.random.key(seed), 8)
    return {
        "design": draw_design(jax.random.fold_in(key_of[7], 71), 0),
        "passive": plant((jax.random.randint(key_of[1], (NX, NY, NZ), 0, 16) < 1).astype(jnp.int32), jax.random.fold_in(key_of[1], 1), 0, 1),
        "basis_pairs": bell_draw(key_of[2], (NB, 2, 3, NX, NY, NZ), 1.0, 6.0, ((3, 32), (4, 16)), jnp.float32),
        "supports": plant((jax.random.randint(key_of[3], (NX, NY, NZ), 0, 16) < 1).astype(jnp.int32), jax.random.fold_in(key_of[3], 1), 0, 1),
        "stiffness": bell_draw(key_of[4], (24, 24), 24 ** -0.5, 1.25, (), jnp.float32),
        "mass_matrix": bell_draw(key_of[5], (24, 24), 24 ** -0.5, 1.25, (), jnp.float32),
        "volume_fraction": jnp.clip(jax.random.uniform(key_of[6], (REGIONS,), jnp.float32, 0.26, 0.36), 0.26, 0.36),
    }


PENALTY_SCALE = 3.0 * (1.0 - 0.001)
OMEGA_SQUARED = 0.5
MOVE_LIMIT = 0.2

def filter_taps():
    tap_list = []
    for offset_x in range(-2, 3):
        for offset_y in range(-2, 3):
            for offset_z in range(-2, 3):
                weight = 3.0 - math.sqrt(offset_x * offset_x + offset_y * offset_y + offset_z * offset_z)
                if weight > 0.0:
                    tap_list.append((offset_x, offset_y, offset_z, weight))
    return tap_list

def stencil(padded, block_shape):
    result = jnp.zeros(block_shape, jnp.float32)
    for offset_x, offset_y, offset_z, weight in filter_taps():
        result = result + weight * padded[2 + offset_x:2 + offset_x + block_shape[0], 2 + offset_y:2 + offset_y + block_shape[1], 2 + offset_z:2 + offset_z + block_shape[2]]
    return result

def element_terms(extended, stiffness, mass_matrix):
    pair_count = extended.shape[0]
    cells_x = extended.shape[3] - 1
    cells_y = extended.shape[4] - 1
    cells_z = extended.shape[5] - 1
    stiff_energy = jnp.zeros((cells_x * cells_y * cells_z,), jnp.float32)
    mass_energy = jnp.zeros((cells_x * cells_y * cells_z,), jnp.float32)
    for pair_index in range(pair_count):
        vectors = []
        for member in range(2):
            row_list = []
            for corner_x in (0, 1):
                for corner_y in (0, 1):
                    for corner_z in (0, 1):
                        for component in range(3):
                            row_list.append(extended[pair_index, member, component, corner_x:corner_x + cells_x, corner_y:corner_y + cells_y, corner_z:corner_z + cells_z].reshape(-1))
            vectors.append(jnp.stack(row_list))
        state_rows, adjoint_rows = vectors
        stiff_energy = stiff_energy + lax.optimization_barrier(jnp.sum(state_rows * jnp.dot(stiffness, adjoint_rows, precision=lax.Precision.HIGHEST), axis=0))
        mass_energy = mass_energy + lax.optimization_barrier(jnp.sum(state_rows * jnp.dot(mass_matrix, adjoint_rows, precision=lax.Precision.HIGHEST), axis=0))
    return (stiff_energy.reshape(cells_x, cells_y, cells_z), mass_energy.reshape(cells_x, cells_y, cells_z))

def reference(design, passive, basis_pairs, supports, stiffness, mass_matrix, volume_fraction):
    block_shape = design.shape
    weight_sum = stencil(jnp.pad(jnp.ones(block_shape, jnp.float32), 2), block_shape)
    physical = jnp.where(passive == 1, 1.0, stencil(jnp.pad(design, 2), block_shape) / weight_sum)
    fields = basis_pairs * (1 - supports).astype(jnp.float32)
    extended = jnp.pad(fields, ((0, 0), (0, 0), (0, 0), (0, 1), (0, 1), (0, 1)))

    def block_terms(block_index):
        block_piece = lax.dynamic_slice_in_dim(extended, block_index * EX, EX + 1, axis=3)
        return element_terms(block_piece, stiffness, mass_matrix)
    stiff_parts, mass_parts = lax.map(block_terms, jnp.arange(N_GX, dtype=jnp.int32))
    stiff_energy = stiff_parts.reshape(block_shape)
    mass_energy = mass_parts.reshape(block_shape)
    raw_sensitivity = -(PENALTY_SCALE * physical * physical * stiff_energy - OMEGA_SQUARED * mass_energy)
    raw_sensitivity = jnp.where(passive == 1, 0.0, raw_sensitivity)
    sensitivity = stencil(jnp.pad(raw_sensitivity / weight_sum, 2), block_shape)
    benefit = jnp.maximum(-sensitivity, 0.0)
    floor_value = jnp.maximum(design - MOVE_LIMIT, 0.0)
    ceiling = jnp.minimum(design + MOVE_LIMIT, 1.0)
    band_cells = NZ // REGIONS
    target = volume_fraction * float(NX * NY * band_cells)

    def candidate(multiplier):
        per_cell = jnp.repeat(multiplier, band_cells)[None, None, :]
        trial = design * jnp.sqrt(benefit / per_cell)
        return jnp.where(passive == 1, 1.0, jnp.minimum(ceiling, jnp.maximum(floor_value, trial)))

    def region_sum(field):
        return lax.optimization_barrier(jnp.sum(field, axis=(0, 1))).reshape(REGIONS, band_cells).sum(axis=1)

    def bisect_step(step_index, bracket):
        low_end, high_end = bracket
        middle = jnp.sqrt(low_end * high_end)
        heavier = region_sum(candidate(middle)) > target
        return (jnp.where(heavier, middle, low_end), jnp.where(heavier, high_end, middle))
    start = (jnp.full((REGIONS,), 0.0001, jnp.float32), jnp.full((REGIONS,), 10000.0, jnp.float32))
    low_end, high_end = lax.fori_loop(0, BISECT, bisect_step, start)
    design_next = candidate(jnp.sqrt(low_end * high_end))
    return (sensitivity, design_next)
```

```python
import math

import jax
import jax.numpy as jnp
from jax import lax
from jax.sharding import PartitionSpec as P

BISECT = 6
REGIONS = 64


PENALTY_SCALE = 3.0 * (1.0 - 0.001)
OMEGA_SQUARED = 0.5
MOVE_LIMIT = 0.2


def with_halo(cells, sides, width):
    for axis, dim in sides:
        count = lax.axis_size(axis)
        ends = count - 1
        head = lax.slice_in_dim(cells, 0, width, axis=dim)
        tail = lax.slice_in_dim(cells, cells.shape[dim] - width, cells.shape[dim], axis=dim)
        cells = jnp.concatenate(
            [
                lax.ppermute(tail, axis, [(i, (i + 1) % count) for i in range(ends)]),
                cells,
                lax.ppermute(head, axis, [((i + 1) % count, i) for i in range(ends)]),
            ],
            axis=dim,
        )
    return cells


def from_behind(value, axis, steps):
    count = lax.axis_size(axis)
    initial, last = (max(0, -steps), min(count, count - steps))
    return lax.ppermute(value, axis, [(source, source + steps) for source in range(initial, last)])


def filter_taps():
    tap_list = []
    for offset_x in range(-2, 3):
        for offset_y in range(-2, 3):
            for offset_z in range(-2, 3):
                weight = 3.0 - math.sqrt(
                    offset_x * offset_x + offset_y * offset_y + offset_z * offset_z
                )
                if weight > 0.0:
                    tap_list.append((offset_x, offset_y, offset_z, weight))
    return tap_list


def stencil(padded, block_shape):
    result = jnp.zeros(block_shape, jnp.float32)
    for offset_x, offset_y, offset_z, weight in filter_taps():
        result = (
            result
            + weight
            * padded[
                2 + offset_x : 2 + offset_x + block_shape[0],
                2 + offset_y : 2 + offset_y + block_shape[1],
                2 + offset_z : 2 + offset_z + block_shape[2],
            ]
        )
    return result


def element_terms(extended, stiffness, mass_matrix):
    pair_count = extended.shape[0]
    cells_x = extended.shape[3] - 1
    cells_y = extended.shape[4] - 1
    cells_z = extended.shape[5] - 1
    stiff_energy = jnp.zeros((cells_x * cells_y * cells_z,), jnp.float32)
    mass_energy = jnp.zeros((cells_x * cells_y * cells_z,), jnp.float32)
    for pair_index in range(pair_count):
        vectors = []
        for member in range(2):
            row_list = []
            for corner_x in (0, 1):
                for corner_y in (0, 1):
                    for corner_z in (0, 1):
                        for component in range(3):
                            row_list.append(
                                extended[
                                    pair_index,
                                    member,
                                    component,
                                    corner_x : corner_x + cells_x,
                                    corner_y : corner_y + cells_y,
                                    corner_z : corner_z + cells_z,
                                ].reshape(-1)
                            )
            vectors.append(jnp.stack(row_list))
        state_rows, adjoint_rows = vectors
        stiff_energy = stiff_energy + jnp.sum(
            state_rows * jnp.dot(stiffness, adjoint_rows, precision=lax.Precision.HIGHEST), axis=0
        )
        mass_energy = mass_energy + jnp.sum(
            state_rows * jnp.dot(mass_matrix, adjoint_rows, precision=lax.Precision.HIGHEST), axis=0
        )
    return (
        stiff_energy.reshape(cells_x, cells_y, cells_z),
        mass_energy.reshape(cells_x, cells_y, cells_z),
    )


def shards(design, passive, basis_pairs, supports, stiffness, mass_matrix, volume_fraction):
    block_shape = design.shape
    size_x, size_y, size_z = block_shape
    devices_x = lax.axis_size("gx")
    devices_y = lax.axis_size("gy")
    index_x = lax.axis_index("gx")
    index_y = lax.axis_index("gy")
    grid_x = size_x * devices_x
    grid_y = size_y * devices_y
    spread_x = jnp.arange(size_x + 4, dtype=jnp.int32) + index_x * size_x - 2
    spread_y = jnp.arange(size_y + 4, dtype=jnp.int32) + index_y * size_y - 2
    valid_x = ((spread_x >= 0) & (spread_x < grid_x)).astype(jnp.float32)
    valid_y = ((spread_y >= 0) & (spread_y < grid_y)).astype(jnp.float32)
    valid_z = jnp.pad(jnp.ones((size_z,), jnp.float32), 2)
    inside = valid_x[:, None, None] * valid_y[None, :, None] * valid_z[None, None, :]
    weight_sum = stencil(inside, block_shape)
    design_wide = with_halo(design, (("gx", 0), ("gy", 1)), 2)
    design_wide = jnp.pad(design_wide, ((0, 0), (0, 0), (2, 2)))
    physical = jnp.where(passive == 1, 1.0, stencil(design_wide, block_shape) / weight_sum)
    fields = basis_pairs * (1 - supports).astype(jnp.float32)
    rim_first = from_behind(fields[:, :, :, :1], "gx", -1)
    widened = jnp.concatenate([fields, rim_first], axis=3)
    rim_second = from_behind(widened[:, :, :, :, :1], "gy", -1)
    extended = jnp.concatenate([widened, rim_second], axis=4)
    extended = jnp.pad(extended, ((0, 0), (0, 0), (0, 0), (0, 0), (0, 0), (0, 1)))
    stiff_energy, mass_energy = element_terms(extended, stiffness, mass_matrix)
    raw_sensitivity = -(
        PENALTY_SCALE * physical * physical * stiff_energy - OMEGA_SQUARED * mass_energy
    )
    raw_sensitivity = jnp.where(passive == 1, 0.0, raw_sensitivity)
    scaled_wide = with_halo(raw_sensitivity / weight_sum, (("gx", 0), ("gy", 1)), 2)
    scaled_wide = jnp.pad(scaled_wide, ((0, 0), (0, 0), (2, 2)))
    sensitivity = stencil(scaled_wide, block_shape)
    benefit = jnp.maximum(-sensitivity, 0.0)
    floor_value = jnp.maximum(design - MOVE_LIMIT, 0.0)
    ceiling = jnp.minimum(design + MOVE_LIMIT, 1.0)
    band_cells = size_z // REGIONS
    target = volume_fraction * float(grid_x * grid_y * band_cells)

    def candidate(multiplier):
        per_cell = jnp.repeat(multiplier, band_cells)[None, None, :]
        trial = design * jnp.sqrt(benefit / per_cell)
        return jnp.where(passive == 1, 1.0, jnp.minimum(ceiling, jnp.maximum(floor_value, trial)))

    def region_sum(field):
        return jnp.sum(field, axis=(0, 1)).reshape(REGIONS, band_cells).sum(axis=1)

    levels = BISECT

    def bisect_round(round_index, bracket):
        low_end, high_end = bracket
        level_nodes = [(low_end, high_end)]
        midpoints = []
        for depth in range(levels):
            next_nodes = []
            for node_low, node_high in level_nodes:
                middle = jnp.sqrt(node_low * node_high)
                midpoints.append(middle)
                next_nodes.append((node_low, middle))
                next_nodes.append((middle, node_high))
            level_nodes = next_nodes
        trial_multipliers = jnp.stack(midpoints)
        per_cell = jnp.repeat(trial_multipliers, band_cells, axis=1)[:, None, None, :]
        trial = design[None] * jnp.sqrt(benefit[None] / per_cell)
        fields_of = jnp.where(
            passive[None] == 1, 1.0, jnp.minimum(ceiling[None], jnp.maximum(floor_value[None], trial))
        )
        partial_volumes = (
            jnp.sum(fields_of, axis=(1, 2)).reshape(len(midpoints), REGIONS, band_cells).sum(axis=2)
        )
        volumes = lax.psum(partial_volumes, ("gx", "gy"))
        position = jnp.zeros((REGIONS,), jnp.int32)
        for depth in range(levels):
            middle = jnp.sqrt(low_end * high_end)
            heap_index = position + (2**depth - 1)
            chosen = jnp.take_along_axis(volumes, heap_index[None, :], axis=0)[0]
            heavier = chosen > target
            low_end = jnp.where(heavier, middle, low_end)
            high_end = jnp.where(heavier, high_end, middle)
            position = 2 * position + heavier.astype(jnp.int32)
        return (low_end, high_end)

    start = (jnp.full((REGIONS,), 0.0001, jnp.float32), jnp.full((REGIONS,), 10000.0, jnp.float32))
    low_end, high_end = bisect_round(0, start)
    design_next = candidate(jnp.sqrt(low_end * high_end))
    return (sensitivity, design_next)


def solution(mesh):
    placed = (
        P("gx", "gy", None),
        P("gx", "gy", None),
        P(None, None, None, "gx", "gy", None),
        P("gx", "gy", None),
        P(),
        P(),
        P(),
    )
    return jax.shard_map(
        shards,
        mesh=mesh,
        in_specs=placed,
        out_specs=(P("gx", "gy", None), P("gx", "gy", None)),
        check_vma=False,
    )
```

```python
import math

import jax
import jax.numpy as jnp
from jax import lax
from jax.sharding import PartitionSpec as P

BISECT = 6
REGIONS = 64


PENALTY_SCALE = 3.0 * (1.0 - 0.001)
OMEGA_SQUARED = 0.5
MOVE_LIMIT = 0.2


def with_halo(cells, sides, width):
    for axis, dim in sides:
        count = lax.axis_size(axis)
        ends = count - 1
        head = lax.slice_in_dim(cells, 0, width, axis=dim)
        tail = lax.slice_in_dim(cells, cells.shape[dim] - width, cells.shape[dim], axis=dim)
        cells = jnp.concatenate(
            [
                lax.ppermute(tail, axis, [(i, (i + 1) % count) for i in range(ends)]),
                cells,
                lax.ppermute(head, axis, [((i + 1) % count, i) for i in range(ends)]),
            ],
            axis=dim,
        )
    return cells


def from_behind(value, axis, steps):
    count = lax.axis_size(axis)
    initial, last = (max(0, -steps), min(count, count - steps))
    return lax.ppermute(value, axis, [(source, source + steps) for source in range(initial, last)])


def butterfly_sum(value, axis):
    count = lax.axis_size(axis)
    stride = 1
    while stride < count:
        value = value + lax.ppermute(value, axis, [(i, i ^ stride) for i in range(count)])
        stride *= 2
    return value


def filter_taps():
    tap_list = []
    for offset_x in range(-2, 3):
        for offset_y in range(-2, 3):
            for offset_z in range(-2, 3):
                weight = 3.0 - math.sqrt(
                    offset_x * offset_x + offset_y * offset_y + offset_z * offset_z
                )
                if weight > 0.0:
                    tap_list.append((offset_x, offset_y, offset_z, weight))
    return tap_list


def stencil(padded, block_shape):
    result = jnp.zeros(block_shape, jnp.float32)
    for offset_x, offset_y, offset_z, weight in filter_taps():
        result = (
            result
            + weight
            * padded[
                2 + offset_x : 2 + offset_x + block_shape[0],
                2 + offset_y : 2 + offset_y + block_shape[1],
                2 + offset_z : 2 + offset_z + block_shape[2],
            ]
        )
    return result


def element_terms(extended, stiffness, mass_matrix):
    pair_count = extended.shape[0]
    cells_x = extended.shape[3] - 1
    cells_y = extended.shape[4] - 1
    cells_z = extended.shape[5] - 1
    stiff_energy = jnp.zeros((cells_x * cells_y * cells_z,), jnp.float32)
    mass_energy = jnp.zeros((cells_x * cells_y * cells_z,), jnp.float32)
    for pair_index in range(pair_count):
        vectors = []
        for member in range(2):
            row_list = []
            for corner_x in (0, 1):
                for corner_y in (0, 1):
                    for corner_z in (0, 1):
                        for component in range(3):
                            row_list.append(
                                extended[
                                    pair_index,
                                    member,
                                    component,
                                    corner_x : corner_x + cells_x,
                                    corner_y : corner_y + cells_y,
                                    corner_z : corner_z + cells_z,
                                ].reshape(-1)
                            )
            vectors.append(jnp.stack(row_list))
        state_rows, adjoint_rows = vectors
        stiff_energy = stiff_energy + jnp.sum(
            state_rows * jnp.dot(stiffness, adjoint_rows, precision=lax.Precision.HIGHEST), axis=0
        )
        mass_energy = mass_energy + jnp.sum(
            state_rows * jnp.dot(mass_matrix, adjoint_rows, precision=lax.Precision.HIGHEST), axis=0
        )
    return (
        stiff_energy.reshape(cells_x, cells_y, cells_z),
        mass_energy.reshape(cells_x, cells_y, cells_z),
    )


def shards(design, passive, basis_pairs, supports, stiffness, mass_matrix, volume_fraction):
    block_shape = design.shape
    size_x, size_y, size_z = block_shape
    devices_x = lax.axis_size("gx")
    devices_y = lax.axis_size("gy")
    index_x = lax.axis_index("gx")
    index_y = lax.axis_index("gy")
    grid_x = size_x * devices_x
    grid_y = size_y * devices_y
    spread_x = jnp.arange(size_x + 4, dtype=jnp.int32) + index_x * size_x - 2
    spread_y = jnp.arange(size_y + 4, dtype=jnp.int32) + index_y * size_y - 2
    valid_x = ((spread_x >= 0) & (spread_x < grid_x)).astype(jnp.float32)
    valid_y = ((spread_y >= 0) & (spread_y < grid_y)).astype(jnp.float32)
    valid_z = jnp.pad(jnp.ones((size_z,), jnp.float32), 2)
    inside = valid_x[:, None, None] * valid_y[None, :, None] * valid_z[None, None, :]
    weight_sum = stencil(inside, block_shape)
    design_wide = with_halo(design, (("gx", 0), ("gy", 1)), 2)
    design_wide = jnp.pad(design_wide, ((0, 0), (0, 0), (2, 2)))
    physical = jnp.where(passive == 1, 1.0, stencil(design_wide, block_shape) / weight_sum)
    fields = basis_pairs * (1 - supports).astype(jnp.float32)
    rim_first = from_behind(fields[:, :, :, :1], "gx", -1)
    widened = jnp.concatenate([fields, rim_first], axis=3)
    rim_second = from_behind(widened[:, :, :, :, :1], "gy", -1)
    extended = jnp.concatenate([widened, rim_second], axis=4)
    extended = jnp.pad(extended, ((0, 0), (0, 0), (0, 0), (0, 0), (0, 0), (0, 1)))
    stiff_energy, mass_energy = element_terms(extended, stiffness, mass_matrix)
    raw_sensitivity = -(
        PENALTY_SCALE * physical * physical * stiff_energy - OMEGA_SQUARED * mass_energy
    )
    raw_sensitivity = jnp.where(passive == 1, 0.0, raw_sensitivity)
    scaled_wide = with_halo(raw_sensitivity / weight_sum, (("gx", 0), ("gy", 1)), 2)
    scaled_wide = jnp.pad(scaled_wide, ((0, 0), (0, 0), (2, 2)))
    sensitivity = stencil(scaled_wide, block_shape)
    benefit = jnp.maximum(-sensitivity, 0.0)
    floor_value = jnp.maximum(design - MOVE_LIMIT, 0.0)
    ceiling = jnp.minimum(design + MOVE_LIMIT, 1.0)
    band_cells = size_z // REGIONS
    target = volume_fraction * float(grid_x * grid_y * band_cells)

    def candidate(multiplier):
        per_cell = jnp.repeat(multiplier, band_cells)[None, None, :]
        trial = design * jnp.sqrt(benefit / per_cell)
        return jnp.where(passive == 1, 1.0, jnp.minimum(ceiling, jnp.maximum(floor_value, trial)))

    def region_sum(field):
        return jnp.sum(field, axis=(0, 1)).reshape(REGIONS, band_cells).sum(axis=1)

    levels = BISECT

    def bisect_round(round_index, bracket):
        low_end, high_end = bracket
        level_nodes = [(low_end, high_end)]
        midpoints = []
        for depth in range(levels):
            next_nodes = []
            for node_low, node_high in level_nodes:
                middle = jnp.sqrt(node_low * node_high)
                midpoints.append(middle)
                next_nodes.append((node_low, middle))
                next_nodes.append((middle, node_high))
            level_nodes = next_nodes
        trial_multipliers = jnp.stack(midpoints)
        per_cell = jnp.repeat(trial_multipliers, band_cells, axis=1)[:, None, None, :]
        trial = design[None] * jnp.sqrt(benefit[None] / per_cell)
        fields_of = jnp.where(
            passive[None] == 1, 1.0, jnp.minimum(ceiling[None], jnp.maximum(floor_value[None], trial))
        )
        partial_volumes = (
            jnp.sum(fields_of, axis=(1, 2)).reshape(len(midpoints), REGIONS, band_cells).sum(axis=2)
        )
        volumes = butterfly_sum(butterfly_sum(partial_volumes, "gy"), "gx")
        position = jnp.zeros((REGIONS,), jnp.int32)
        for depth in range(levels):
            middle = jnp.sqrt(low_end * high_end)
            heap_index = position + (2**depth - 1)
            chosen = jnp.take_along_axis(volumes, heap_index[None, :], axis=0)[0]
            heavier = chosen > target
            low_end = jnp.where(heavier, middle, low_end)
            high_end = jnp.where(heavier, high_end, middle)
            position = 2 * position + heavier.astype(jnp.int32)
        return (low_end, high_end)

    start = (jnp.full((REGIONS,), 0.0001, jnp.float32), jnp.full((REGIONS,), 10000.0, jnp.float32))
    low_end, high_end = bisect_round(0, start)
    design_next = candidate(jnp.sqrt(low_end * high_end))
    return (sensitivity, design_next)


def solution(mesh):
    placed = (
        P("gx", "gy", None),
        P("gx", "gy", None),
        P(None, None, None, "gx", "gy", None),
        P("gx", "gy", None),
        P(),
        P(),
        P(),
    )
    return jax.shard_map(
        shards,
        mesh=mesh,
        in_specs=placed,
        out_specs=(P("gx", "gy", None), P("gx", "gy", None)),
        check_vma=False,
    )
```

```python
import math

import jax
import jax.numpy as jnp
from jax import lax
from jax.sharding import PartitionSpec as P
from jax.experimental import pallas as pl
from jax.experimental.pallas import tpu as pltpu

BISECT = 6
REGIONS = 64


PENALTY_SCALE = 3.0 * (1.0 - 0.001)
OMEGA_SQUARED = 0.5
MOVE_LIMIT = 0.2


def with_halo(cells, sides, width):
    for axis, dim in sides:
        count = lax.axis_size(axis)
        ends = count - 1
        head = lax.slice_in_dim(cells, 0, width, axis=dim)
        tail = lax.slice_in_dim(cells, cells.shape[dim] - width, cells.shape[dim], axis=dim)
        cells = jnp.concatenate(
            [
                lax.ppermute(tail, axis, [(i, (i + 1) % count) for i in range(ends)]),
                cells,
                lax.ppermute(head, axis, [((i + 1) % count, i) for i in range(ends)]),
            ],
            axis=dim,
        )
    return cells


def from_behind(value, axis, steps):
    count = lax.axis_size(axis)
    initial, last = (max(0, -steps), min(count, count - steps))
    return lax.ppermute(value, axis, [(source, source + steps) for source in range(initial, last)])


def butterfly_sum(value, axis):
    count = lax.axis_size(axis)
    stride = 1
    while stride < count:
        value = value + lax.ppermute(value, axis, [(i, i ^ stride) for i in range(count)])
        stride *= 2
    return value


def filter_taps():
    tap_list = []
    for offset_x in range(-2, 3):
        for offset_y in range(-2, 3):
            for offset_z in range(-2, 3):
                weight = 3.0 - math.sqrt(
                    offset_x * offset_x + offset_y * offset_y + offset_z * offset_z
                )
                if weight > 0.0:
                    tap_list.append((offset_x, offset_y, offset_z, weight))
    return tap_list


def stencil(padded, block_shape):
    result = jnp.zeros(block_shape, jnp.float32)
    for offset_x, offset_y, offset_z, weight in filter_taps():
        result = (
            result
            + weight
            * padded[
                2 + offset_x : 2 + offset_x + block_shape[0],
                2 + offset_y : 2 + offset_y + block_shape[1],
                2 + offset_z : 2 + offset_z + block_shape[2],
            ]
        )
    return result


def element_terms(extended, stiffness, mass_matrix):
    pair_count = extended.shape[0]
    cells_x = extended.shape[3] - 1
    cells_y = extended.shape[4] - 1
    cells_z = extended.shape[5] - 1
    stiff_energy = jnp.zeros((cells_x * cells_y * cells_z,), jnp.float32)
    mass_energy = jnp.zeros((cells_x * cells_y * cells_z,), jnp.float32)
    for pair_index in range(pair_count):
        vectors = []
        for member in range(2):
            row_list = []
            for corner_x in (0, 1):
                for corner_y in (0, 1):
                    for corner_z in (0, 1):
                        for component in range(3):
                            row_list.append(
                                extended[
                                    pair_index,
                                    member,
                                    component,
                                    corner_x : corner_x + cells_x,
                                    corner_y : corner_y + cells_y,
                                    corner_z : corner_z + cells_z,
                                ].reshape(-1)
                            )
            vectors.append(jnp.stack(row_list))
        state_rows, adjoint_rows = vectors
        stiff_energy = stiff_energy + jnp.sum(
            state_rows * jnp.dot(stiffness, adjoint_rows, precision=lax.Precision.HIGHEST), axis=0
        )
        mass_energy = mass_energy + jnp.sum(
            state_rows * jnp.dot(mass_matrix, adjoint_rows, precision=lax.Precision.HIGHEST), axis=0
        )
    return (
        stiff_energy.reshape(cells_x, cells_y, cells_z),
        mass_energy.reshape(cells_x, cells_y, cells_z),
    )


CORNERS = [(a, b, d) for a in (0, 1) for b in (0, 1) for d in (0, 1)]


def energy_kernel(extended_ref, stiffness_ref, mass_ref, stiff_out, mass_out):
    pair_count = extended_ref.shape[0]
    cells_x, cells_y, cells_z = stiff_out.shape
    lane = lax.broadcasted_iota(jnp.int32, (cells_y, cells_z), 1)
    inside = lane < cells_z - 1

    def node_view(pair, member, component, x, corner):
        corner_x, corner_y, corner_z = corner
        value = extended_ref[pair, member, component, x + corner_x, pl.ds(corner_y, cells_y), :]
        if corner_z:
            value = jnp.where(inside, pltpu.roll(value, cells_z - 1, 1), 0.0)
        return value

    def over_pairs(pair, energies):
        stiff_sum, mass_sum, x = energies
        adjoint = [
            node_view(pair, 1, component, x, corner) for corner in CORNERS for component in range(3)
        ]
        for row in range(len(adjoint)):
            state = node_view(pair, 0, row % 3, x, CORNERS[row // 3])
            stiff_row = stiffness_ref[row, 0] * adjoint[0]
            mass_row = mass_ref[row, 0] * adjoint[0]
            for column in range(1, len(adjoint)):
                stiff_row = stiff_row + stiffness_ref[row, column] * adjoint[column]
                mass_row = mass_row + mass_ref[row, column] * adjoint[column]
            stiff_sum = stiff_sum + state * stiff_row
            mass_sum = mass_sum + state * mass_row
        return stiff_sum, mass_sum, x

    def over_x(x, carry):
        zero = jnp.zeros((cells_y, cells_z), jnp.float32)
        stiff_sum, mass_sum, _ = lax.fori_loop(0, pair_count, over_pairs, (zero, zero, x))
        stiff_out[x] = stiff_sum
        mass_out[x] = mass_sum
        return carry

    lax.fori_loop(0, cells_x, over_x, 0)


def element_energies(extended, stiffness, mass_matrix):
    pair_count = extended.shape[0]
    cells = (extended.shape[3] - 1, extended.shape[4] - 1, extended.shape[5])
    voxels = cells[0] * cells[1] * cells[2]
    vmem = pl.BlockSpec(memory_space=pltpu.VMEM)
    smem = pl.BlockSpec(memory_space=pltpu.SMEM)
    return pl.pallas_call(
        energy_kernel,
        out_shape=(
            jax.ShapeDtypeStruct(cells, jnp.float32),
            jax.ShapeDtypeStruct(cells, jnp.float32),
        ),
        in_specs=[vmem, smem, smem],
        out_specs=(vmem, vmem),
        cost_estimate=pl.CostEstimate(
            flops=pair_count * voxels * 2400,
            bytes_accessed=extended.size * 4 + 2 * voxels * 4,
            transcendentals=0,
        ),
    )(extended, stiffness, mass_matrix)


def shards(design, passive, basis_pairs, supports, stiffness, mass_matrix, volume_fraction):
    block_shape = design.shape
    size_x, size_y, size_z = block_shape
    devices_x = lax.axis_size("gx")
    devices_y = lax.axis_size("gy")
    index_x = lax.axis_index("gx")
    index_y = lax.axis_index("gy")
    grid_x = size_x * devices_x
    grid_y = size_y * devices_y
    spread_x = jnp.arange(size_x + 4, dtype=jnp.int32) + index_x * size_x - 2
    spread_y = jnp.arange(size_y + 4, dtype=jnp.int32) + index_y * size_y - 2
    valid_x = ((spread_x >= 0) & (spread_x < grid_x)).astype(jnp.float32)
    valid_y = ((spread_y >= 0) & (spread_y < grid_y)).astype(jnp.float32)
    valid_z = jnp.pad(jnp.ones((size_z,), jnp.float32), 2)
    inside = valid_x[:, None, None] * valid_y[None, :, None] * valid_z[None, None, :]
    weight_sum = stencil(inside, block_shape)
    design_wide = with_halo(design, (("gx", 0), ("gy", 1)), 2)
    design_wide = jnp.pad(design_wide, ((0, 0), (0, 0), (2, 2)))
    physical = jnp.where(passive == 1, 1.0, stencil(design_wide, block_shape) / weight_sum)
    fields = basis_pairs * (1 - supports).astype(jnp.float32)
    rim_first = from_behind(fields[:, :, :, :1], "gx", -1)
    widened = jnp.concatenate([fields, rim_first], axis=3)
    rim_second = from_behind(widened[:, :, :, :, :1], "gy", -1)
    extended = jnp.concatenate([widened, rim_second], axis=4)
    stiff_energy, mass_energy = element_energies(extended, stiffness, mass_matrix)
    raw_sensitivity = -(
        PENALTY_SCALE * physical * physical * stiff_energy - OMEGA_SQUARED * mass_energy
    )
    raw_sensitivity = jnp.where(passive == 1, 0.0, raw_sensitivity)
    scaled_wide = with_halo(raw_sensitivity / weight_sum, (("gx", 0), ("gy", 1)), 2)
    scaled_wide = jnp.pad(scaled_wide, ((0, 0), (0, 0), (2, 2)))
    sensitivity = stencil(scaled_wide, block_shape)
    benefit = jnp.maximum(-sensitivity, 0.0)
    floor_value = jnp.maximum(design - MOVE_LIMIT, 0.0)
    ceiling = jnp.minimum(design + MOVE_LIMIT, 1.0)
    band_cells = size_z // REGIONS
    target = volume_fraction * float(grid_x * grid_y * band_cells)

    def candidate(multiplier):
        per_cell = jnp.repeat(multiplier, band_cells)[None, None, :]
        trial = design * jnp.sqrt(benefit / per_cell)
        return jnp.where(passive == 1, 1.0, jnp.minimum(ceiling, jnp.maximum(floor_value, trial)))

    def region_sum(field):
        return jnp.sum(field, axis=(0, 1)).reshape(REGIONS, band_cells).sum(axis=1)

    levels = BISECT

    def bisect_round(round_index, bracket):
        low_end, high_end = bracket
        level_nodes = [(low_end, high_end)]
        midpoints = []
        for depth in range(levels):
            next_nodes = []
            for node_low, node_high in level_nodes:
                middle = jnp.sqrt(node_low * node_high)
                midpoints.append(middle)
                next_nodes.append((node_low, middle))
                next_nodes.append((middle, node_high))
            level_nodes = next_nodes
        trial_multipliers = jnp.stack(midpoints)
        per_cell = jnp.repeat(trial_multipliers, band_cells, axis=1)[:, None, None, :]
        trial = design[None] * jnp.sqrt(benefit[None] / per_cell)
        fields_of = jnp.where(
            passive[None] == 1, 1.0, jnp.minimum(ceiling[None], jnp.maximum(floor_value[None], trial))
        )
        partial_volumes = (
            jnp.sum(fields_of, axis=(1, 2)).reshape(len(midpoints), REGIONS, band_cells).sum(axis=2)
        )
        volumes = butterfly_sum(butterfly_sum(partial_volumes, "gy"), "gx")
        position = jnp.zeros((REGIONS,), jnp.int32)
        for depth in range(levels):
            middle = jnp.sqrt(low_end * high_end)
            heap_index = position + (2**depth - 1)
            chosen = jnp.take_along_axis(volumes, heap_index[None, :], axis=0)[0]
            heavier = chosen > target
            low_end = jnp.where(heavier, middle, low_end)
            high_end = jnp.where(heavier, high_end, middle)
            position = 2 * position + heavier.astype(jnp.int32)
        return (low_end, high_end)

    start = (jnp.full((REGIONS,), 0.0001, jnp.float32), jnp.full((REGIONS,), 10000.0, jnp.float32))
    low_end, high_end = bisect_round(0, start)
    design_next = candidate(jnp.sqrt(low_end * high_end))
    return (sensitivity, design_next)


def solution(mesh):
    placed = (
        P("gx", "gy", None),
        P("gx", "gy", None),
        P(None, None, None, "gx", "gy", None),
        P("gx", "gy", None),
        P(),
        P(),
        P(),
    )
    return jax.shard_map(
        shards,
        mesh=mesh,
        in_specs=placed,
        out_specs=(P("gx", "gy", None), P("gx", "gy", None)),
        check_vma=False,
    )
```

```python
import math

import jax
import jax.numpy as jnp
from jax import lax
from jax.sharding import PartitionSpec as P
from jax.experimental import pallas as pl
from jax.experimental.pallas import tpu as pltpu

BISECT = 6
REGIONS = 64


PENALTY_SCALE = 3.0 * (1.0 - 0.001)
OMEGA_SQUARED = 0.5
MOVE_LIMIT = 0.2


def with_halo(cells, sides, width):
    for axis, dim in sides:
        count = lax.axis_size(axis)
        ends = count - 1
        head = lax.slice_in_dim(cells, 0, width, axis=dim)
        tail = lax.slice_in_dim(cells, cells.shape[dim] - width, cells.shape[dim], axis=dim)
        cells = jnp.concatenate(
            [
                lax.ppermute(tail, axis, [(i, (i + 1) % count) for i in range(ends)]),
                cells,
                lax.ppermute(head, axis, [((i + 1) % count, i) for i in range(ends)]),
            ],
            axis=dim,
        )
    return cells


def front_exchange(cells, fields, width):
    for axis, dim in (("gx", 0), ("gy", 1)):
        count = lax.axis_size(axis)
        ends = count - 1
        field_dim = dim + 3
        head = lax.slice_in_dim(cells, 0, width, axis=dim)
        tail = lax.slice_in_dim(cells, cells.shape[dim] - width, cells.shape[dim], axis=dim)
        rim = lax.slice_in_dim(fields, 0, 1, axis=field_dim)
        lanes = cells.shape[-1]
        packed = jnp.concatenate([head.reshape(-1, lanes), rim.reshape(-1, lanes)], axis=0)
        packed = lax.ppermute(packed, axis, [((i + 1) % count, i) for i in range(ends)])
        split = head.size // lanes
        head = packed[:split].reshape(head.shape)
        rim = packed[split:].reshape(rim.shape)
        tail = lax.ppermute(tail, axis, [(i, (i + 1) % count) for i in range(ends)])
        cells = jnp.concatenate([tail, cells, head], axis=dim)
        fields = jnp.concatenate([fields, rim], axis=field_dim)
    return cells, fields


def from_behind(value, axis, steps):
    count = lax.axis_size(axis)
    initial, last = (max(0, -steps), min(count, count - steps))
    return lax.ppermute(value, axis, [(source, source + steps) for source in range(initial, last)])


def butterfly_sum(value, axis):
    count = lax.axis_size(axis)
    stride = 1
    while stride < count:
        value = value + lax.ppermute(value, axis, [(i, i ^ stride) for i in range(count)])
        stride *= 2
    return value


def filter_taps():
    tap_list = []
    for offset_x in range(-2, 3):
        for offset_y in range(-2, 3):
            for offset_z in range(-2, 3):
                weight = 3.0 - math.sqrt(
                    offset_x * offset_x + offset_y * offset_y + offset_z * offset_z
                )
                if weight > 0.0:
                    tap_list.append((offset_x, offset_y, offset_z, weight))
    return tap_list


def stencil(padded, block_shape):
    result = jnp.zeros(block_shape, jnp.float32)
    for offset_x, offset_y, offset_z, weight in filter_taps():
        result = (
            result
            + weight
            * padded[
                2 + offset_x : 2 + offset_x + block_shape[0],
                2 + offset_y : 2 + offset_y + block_shape[1],
                2 + offset_z : 2 + offset_z + block_shape[2],
            ]
        )
    return result


def element_terms(extended, stiffness, mass_matrix):
    pair_count = extended.shape[0]
    cells_x = extended.shape[3] - 1
    cells_y = extended.shape[4] - 1
    cells_z = extended.shape[5] - 1
    stiff_energy = jnp.zeros((cells_x * cells_y * cells_z,), jnp.float32)
    mass_energy = jnp.zeros((cells_x * cells_y * cells_z,), jnp.float32)
    for pair_index in range(pair_count):
        vectors = []
        for member in range(2):
            row_list = []
            for corner_x in (0, 1):
                for corner_y in (0, 1):
                    for corner_z in (0, 1):
                        for component in range(3):
                            row_list.append(
                                extended[
                                    pair_index,
                                    member,
                                    component,
                                    corner_x : corner_x + cells_x,
                                    corner_y : corner_y + cells_y,
                                    corner_z : corner_z + cells_z,
                                ].reshape(-1)
                            )
            vectors.append(jnp.stack(row_list))
        state_rows, adjoint_rows = vectors
        stiff_energy = stiff_energy + jnp.sum(
            state_rows * jnp.dot(stiffness, adjoint_rows, precision=lax.Precision.HIGHEST), axis=0
        )
        mass_energy = mass_energy + jnp.sum(
            state_rows * jnp.dot(mass_matrix, adjoint_rows, precision=lax.Precision.HIGHEST), axis=0
        )
    return (
        stiff_energy.reshape(cells_x, cells_y, cells_z),
        mass_energy.reshape(cells_x, cells_y, cells_z),
    )


CORNERS = [(a, b, d) for a in (0, 1) for b in (0, 1) for d in (0, 1)]


def energy_kernel(extended_ref, stiffness_ref, mass_ref, stiff_out, mass_out):
    pair_count = extended_ref.shape[0]
    cells_x, cells_y, cells_z = stiff_out.shape
    lane = lax.broadcasted_iota(jnp.int32, (cells_y, cells_z), 1)
    inside = lane < cells_z - 1

    def node_view(pair, member, component, x, corner):
        corner_x, corner_y, corner_z = corner
        value = extended_ref[pair, member, component, x + corner_x, pl.ds(corner_y, cells_y), :]
        if corner_z:
            value = jnp.where(inside, pltpu.roll(value, cells_z - 1, 1), 0.0)
        return value

    def over_pairs(pair, energies):
        stiff_sum, mass_sum, x = energies
        adjoint = [
            node_view(pair, 1, component, x, corner) for corner in CORNERS for component in range(3)
        ]
        for row in range(len(adjoint)):
            state = node_view(pair, 0, row % 3, x, CORNERS[row // 3])
            stiff_row = stiffness_ref[row, 0] * adjoint[0]
            mass_row = mass_ref[row, 0] * adjoint[0]
            for column in range(1, len(adjoint)):
                stiff_row = stiff_row + stiffness_ref[row, column] * adjoint[column]
                mass_row = mass_row + mass_ref[row, column] * adjoint[column]
            stiff_sum = stiff_sum + state * stiff_row
            mass_sum = mass_sum + state * mass_row
        return stiff_sum, mass_sum, x

    def over_x(x, carry):
        zero = jnp.zeros((cells_y, cells_z), jnp.float32)
        stiff_sum, mass_sum, _ = lax.fori_loop(0, pair_count, over_pairs, (zero, zero, x))
        stiff_out[x] = stiff_sum
        mass_out[x] = mass_sum
        return carry

    lax.fori_loop(0, cells_x, over_x, 0)


def element_energies(extended, stiffness, mass_matrix):
    pair_count = extended.shape[0]
    cells = (extended.shape[3] - 1, extended.shape[4] - 1, extended.shape[5])
    voxels = cells[0] * cells[1] * cells[2]
    vmem = pl.BlockSpec(memory_space=pltpu.VMEM)
    smem = pl.BlockSpec(memory_space=pltpu.SMEM)
    return pl.pallas_call(
        energy_kernel,
        out_shape=(
            jax.ShapeDtypeStruct(cells, jnp.float32),
            jax.ShapeDtypeStruct(cells, jnp.float32),
        ),
        in_specs=[vmem, smem, smem],
        out_specs=(vmem, vmem),
        cost_estimate=pl.CostEstimate(
            flops=pair_count * voxels * 2400,
            bytes_accessed=extended.size * 4 + 2 * voxels * 4,
            transcendentals=0,
        ),
    )(extended, stiffness, mass_matrix)


def shards(design, passive, basis_pairs, supports, stiffness, mass_matrix, volume_fraction):
    block_shape = design.shape
    size_x, size_y, size_z = block_shape
    devices_x = lax.axis_size("gx")
    devices_y = lax.axis_size("gy")
    index_x = lax.axis_index("gx")
    index_y = lax.axis_index("gy")
    grid_x = size_x * devices_x
    grid_y = size_y * devices_y
    spread_x = jnp.arange(size_x + 4, dtype=jnp.int32) + index_x * size_x - 2
    spread_y = jnp.arange(size_y + 4, dtype=jnp.int32) + index_y * size_y - 2
    valid_x = ((spread_x >= 0) & (spread_x < grid_x)).astype(jnp.float32)
    valid_y = ((spread_y >= 0) & (spread_y < grid_y)).astype(jnp.float32)
    valid_z = jnp.pad(jnp.ones((size_z,), jnp.float32), 2)
    inside = valid_x[:, None, None] * valid_y[None, :, None] * valid_z[None, None, :]
    weight_sum = stencil(inside, block_shape)
    fields = basis_pairs * (1 - supports).astype(jnp.float32)
    design_wide, extended = front_exchange(design, fields, 2)
    design_wide = jnp.pad(design_wide, ((0, 0), (0, 0), (2, 2)))
    physical = jnp.where(passive == 1, 1.0, stencil(design_wide, block_shape) / weight_sum)
    stiff_energy, mass_energy = element_energies(extended, stiffness, mass_matrix)
    raw_sensitivity = -(
        PENALTY_SCALE * physical * physical * stiff_energy - OMEGA_SQUARED * mass_energy
    )
    raw_sensitivity = jnp.where(passive == 1, 0.0, raw_sensitivity)
    scaled_wide = with_halo(raw_sensitivity / weight_sum, (("gx", 0), ("gy", 1)), 2)
    scaled_wide = jnp.pad(scaled_wide, ((0, 0), (0, 0), (2, 2)))
    sensitivity = stencil(scaled_wide, block_shape)
    benefit = jnp.maximum(-sensitivity, 0.0)
    floor_value = jnp.maximum(design - MOVE_LIMIT, 0.0)
    ceiling = jnp.minimum(design + MOVE_LIMIT, 1.0)
    band_cells = size_z // REGIONS
    target = volume_fraction * float(grid_x * grid_y * band_cells)

    def candidate(multiplier):
        per_cell = jnp.repeat(multiplier, band_cells)[None, None, :]
        trial = design * jnp.sqrt(benefit / per_cell)
        return jnp.where(passive == 1, 1.0, jnp.minimum(ceiling, jnp.maximum(floor_value, trial)))

    def region_sum(field):
        return jnp.sum(field, axis=(0, 1)).reshape(REGIONS, band_cells).sum(axis=1)

    levels = BISECT

    def bisect_round(round_index, bracket):
        low_end, high_end = bracket
        level_nodes = [(low_end, high_end)]
        midpoints = []
        for depth in range(levels):
            next_nodes = []
            for node_low, node_high in level_nodes:
                middle = jnp.sqrt(node_low * node_high)
                midpoints.append(middle)
                next_nodes.append((node_low, middle))
                next_nodes.append((middle, node_high))
            level_nodes = next_nodes
        trial_multipliers = jnp.stack(midpoints)
        per_cell = jnp.repeat(trial_multipliers, band_cells, axis=1)[:, None, None, :]
        trial = design[None] * jnp.sqrt(benefit[None] / per_cell)
        fields_of = jnp.where(
            passive[None] == 1, 1.0, jnp.minimum(ceiling[None], jnp.maximum(floor_value[None], trial))
        )
        partial_volumes = (
            jnp.sum(fields_of, axis=(1, 2)).reshape(len(midpoints), REGIONS, band_cells).sum(axis=2)
        )
        volumes = butterfly_sum(butterfly_sum(partial_volumes, "gy"), "gx")
        heavier_all = volumes > target[None, :]
        position = jnp.zeros((REGIONS,), jnp.int32)
        for depth in range(levels):
            middle = jnp.sqrt(low_end * high_end)
            nodes = lax.slice_in_dim(heavier_all, 2**depth - 1, 2 ** (depth + 1) - 1, axis=0)
            slots = lax.broadcasted_iota(jnp.int32, nodes.shape, 0)
            heavier = jnp.any(nodes & (slots == position[None, :]), axis=0)
            low_end = jnp.where(heavier, middle, low_end)
            high_end = jnp.where(heavier, high_end, middle)
            position = 2 * position + heavier.astype(jnp.int32)
        return (low_end, high_end)

    start = (jnp.full((REGIONS,), 0.0001, jnp.float32), jnp.full((REGIONS,), 10000.0, jnp.float32))
    low_end, high_end = bisect_round(0, start)
    design_next = candidate(jnp.sqrt(low_end * high_end))
    return (sensitivity, design_next)


def solution(mesh):
    placed = (
        P("gx", "gy", None),
        P("gx", "gy", None),
        P(None, None, None, "gx", "gy", None),
        P("gx", "gy", None),
        P(),
        P(),
        P(),
    )
    return jax.shard_map(
        shards,
        mesh=mesh,
        in_specs=placed,
        out_specs=(P("gx", "gy", None), P("gx", "gy", None)),
        check_vma=False,
    )
```

```python
import math

import jax
import jax.numpy as jnp
from jax import lax
from jax.sharding import PartitionSpec as P
from jax.experimental import pallas as pl
from jax.experimental.pallas import tpu as pltpu

BISECT = 6
REGIONS = 64


PENALTY_SCALE = 3.0 * (1.0 - 0.001)
OMEGA_SQUARED = 0.5
MOVE_LIMIT = 0.2


def with_halo(cells, sides, width):
    for axis, dim in sides:
        count = lax.axis_size(axis)
        ends = count - 1
        head = lax.slice_in_dim(cells, 0, width, axis=dim)
        tail = lax.slice_in_dim(cells, cells.shape[dim] - width, cells.shape[dim], axis=dim)
        cells = jnp.concatenate(
            [
                lax.ppermute(tail, axis, [(i, (i + 1) % count) for i in range(ends)]),
                cells,
                lax.ppermute(head, axis, [((i + 1) % count, i) for i in range(ends)]),
            ],
            axis=dim,
        )
    return cells


def front_exchange(cells, fields, width):
    for axis, dim in (("gx", 0), ("gy", 1)):
        count = lax.axis_size(axis)
        ends = count - 1
        field_dim = dim + 3
        head = lax.slice_in_dim(cells, 0, width, axis=dim)
        tail = lax.slice_in_dim(cells, cells.shape[dim] - width, cells.shape[dim], axis=dim)
        rim = lax.slice_in_dim(fields, 0, 1, axis=field_dim)
        lanes = cells.shape[-1]
        packed = jnp.concatenate([head.reshape(-1, lanes), rim.reshape(-1, lanes)], axis=0)
        packed = lax.ppermute(packed, axis, [((i + 1) % count, i) for i in range(ends)])
        split = head.size // lanes
        head = packed[:split].reshape(head.shape)
        rim = packed[split:].reshape(rim.shape)
        tail = lax.ppermute(tail, axis, [(i, (i + 1) % count) for i in range(ends)])
        cells = jnp.concatenate([tail, cells, head], axis=dim)
        fields = jnp.concatenate([fields, rim], axis=field_dim)
    return cells, fields


def from_behind(value, axis, steps):
    count = lax.axis_size(axis)
    initial, last = (max(0, -steps), min(count, count - steps))
    return lax.ppermute(value, axis, [(source, source + steps) for source in range(initial, last)])


def butterfly_sum(value, axis):
    count = lax.axis_size(axis)
    stride = 1
    while stride < count:
        value = value + lax.ppermute(value, axis, [(i, i ^ stride) for i in range(count)])
        stride *= 2
    return value


def filter_taps():
    tap_list = []
    for offset_x in range(-2, 3):
        for offset_y in range(-2, 3):
            for offset_z in range(-2, 3):
                weight = 3.0 - math.sqrt(
                    offset_x * offset_x + offset_y * offset_y + offset_z * offset_z
                )
                if weight > 0.0:
                    tap_list.append((offset_x, offset_y, offset_z, weight))
    return tap_list


def stencil(padded, block_shape):
    result = jnp.zeros(block_shape, jnp.float32)
    for offset_x, offset_y, offset_z, weight in filter_taps():
        result = (
            result
            + weight
            * padded[
                2 + offset_x : 2 + offset_x + block_shape[0],
                2 + offset_y : 2 + offset_y + block_shape[1],
                2 + offset_z : 2 + offset_z + block_shape[2],
            ]
        )
    return result


def element_terms(extended, stiffness, mass_matrix):
    pair_count = extended.shape[0]
    cells_x = extended.shape[3] - 1
    cells_y = extended.shape[4] - 1
    cells_z = extended.shape[5] - 1
    stiff_energy = jnp.zeros((cells_x * cells_y * cells_z,), jnp.float32)
    mass_energy = jnp.zeros((cells_x * cells_y * cells_z,), jnp.float32)
    for pair_index in range(pair_count):
        vectors = []
        for member in range(2):
            row_list = []
            for corner_x in (0, 1):
                for corner_y in (0, 1):
                    for corner_z in (0, 1):
                        for component in range(3):
                            row_list.append(
                                extended[
                                    pair_index,
                                    member,
                                    component,
                                    corner_x : corner_x + cells_x,
                                    corner_y : corner_y + cells_y,
                                    corner_z : corner_z + cells_z,
                                ].reshape(-1)
                            )
            vectors.append(jnp.stack(row_list))
        state_rows, adjoint_rows = vectors
        stiff_energy = stiff_energy + jnp.sum(
            state_rows * jnp.dot(stiffness, adjoint_rows, precision=lax.Precision.HIGHEST), axis=0
        )
        mass_energy = mass_energy + jnp.sum(
            state_rows * jnp.dot(mass_matrix, adjoint_rows, precision=lax.Precision.HIGHEST), axis=0
        )
    return (
        stiff_energy.reshape(cells_x, cells_y, cells_z),
        mass_energy.reshape(cells_x, cells_y, cells_z),
    )


CORNERS = [(a, b, d) for a in (0, 1) for b in (0, 1) for d in (0, 1)]


def energy_kernel(extended_ref, stiffness_ref, mass_ref, stiff_out, mass_out):
    pair_count = extended_ref.shape[0]
    cells_x, cells_y, cells_z = stiff_out.shape
    lane = lax.broadcasted_iota(jnp.int32, (cells_y, cells_z), 1)
    inside = lane < cells_z - 1

    def node_view(pair, member, component, x, corner):
        corner_x, corner_y, corner_z = corner
        value = extended_ref[pair, member, component, x + corner_x, pl.ds(corner_y, cells_y), :]
        if corner_z:
            value = jnp.where(inside, pltpu.roll(value, cells_z - 1, 1), 0.0)
        return value

    def over_pairs(pair, energies):
        stiff_sum, mass_sum, x = energies
        adjoint = [
            node_view(pair, 1, component, x, corner) for corner in CORNERS for component in range(3)
        ]
        for row in range(len(adjoint)):
            state = node_view(pair, 0, row % 3, x, CORNERS[row // 3])
            stiff_row = stiffness_ref[row, 0] * adjoint[0]
            mass_row = mass_ref[row, 0] * adjoint[0]
            for column in range(1, len(adjoint)):
                stiff_row = stiff_row + stiffness_ref[row, column] * adjoint[column]
                mass_row = mass_row + mass_ref[row, column] * adjoint[column]
            stiff_sum = stiff_sum + state * stiff_row
            mass_sum = mass_sum + state * mass_row
        return stiff_sum, mass_sum, x

    def over_x(x, carry):
        zero = jnp.zeros((cells_y, cells_z), jnp.float32)
        stiff_sum, mass_sum, _ = lax.fori_loop(0, pair_count, over_pairs, (zero, zero, x))
        stiff_out[x] = stiff_sum
        mass_out[x] = mass_sum
        return carry

    lax.fori_loop(0, cells_x, over_x, 0)


def mxu_energy_kernel(extended_ref, coupling_ref, stiff_out, mass_out, adjoint_rows, products):
    pair_count = extended_ref.shape[0]
    cells_x, cells_y, cells_z = stiff_out.shape
    dofs = 3 * len(CORNERS)
    lane = lax.broadcasted_iota(jnp.int32, (cells_y, cells_z), 1)
    inside = lane < cells_z - 1
    stiff_out[...] = jnp.zeros(stiff_out.shape, jnp.float32)
    mass_out[...] = jnp.zeros(mass_out.shape, jnp.float32)

    def node_view(pair, member, row, x):
        corner_x, corner_y, corner_z = CORNERS[row // 3]
        value = extended_ref[pair, member, row % 3, x + corner_x, pl.ds(corner_y, cells_y), :]
        if corner_z:
            value = jnp.where(inside, pltpu.roll(value, cells_z - 1, 1), 0.0)
        return value

    def over_pairs(pair, carry):
        def gather_x(x, inner):
            columns = pl.ds(pl.multiple_of(x * cells_z, cells_z), cells_z)
            for row in range(dofs):
                adjoint_rows[pl.ds(row * cells_y, cells_y), columns] = node_view(pair, 1, row, x)
            return inner

        lax.fori_loop(0, cells_x, gather_x, 0)
        products[...] = jnp.dot(
            coupling_ref[...],
            adjoint_rows[...],
            precision=lax.Precision.HIGHEST,
            preferred_element_type=jnp.float32,
        )

        def reduce_x(x, inner):
            columns = pl.ds(pl.multiple_of(x * cells_z, cells_z), cells_z)
            stiff_sum = stiff_out[x]
            mass_sum = mass_out[x]
            for row in range(dofs):
                state = node_view(pair, 0, row, x)
                stiff_sum = stiff_sum + state * products[pl.ds(row * cells_y, cells_y), columns]
                mass_sum = mass_sum + state * products[pl.ds((dofs + row) * cells_y, cells_y), columns]
            stiff_out[x] = stiff_sum
            mass_out[x] = mass_sum
            return inner

        lax.fori_loop(0, cells_x, reduce_x, 0)
        return carry

    lax.fori_loop(0, pair_count, over_pairs, 0)


def element_energies(extended, stiffness, mass_matrix):
    pair_count = extended.shape[0]
    cells = (extended.shape[3] - 1, extended.shape[4] - 1, extended.shape[5])
    voxels = cells[0] * cells[1] * cells[2]
    dofs = stiffness.shape[0]
    coupling = jnp.kron(
        jnp.concatenate([stiffness, mass_matrix], axis=0), jnp.eye(cells[1], dtype=jnp.float32)
    )
    vmem = pl.BlockSpec(memory_space=pltpu.VMEM)
    return pl.pallas_call(
        mxu_energy_kernel,
        out_shape=(
            jax.ShapeDtypeStruct(cells, jnp.float32),
            jax.ShapeDtypeStruct(cells, jnp.float32),
        ),
        in_specs=[vmem, vmem],
        out_specs=(vmem, vmem),
        scratch_shapes=[
            pltpu.VMEM((dofs * cells[1], cells[0] * cells[2]), jnp.float32),
            pltpu.VMEM((2 * dofs * cells[1], cells[0] * cells[2]), jnp.float32),
        ],
        cost_estimate=pl.CostEstimate(
            flops=pair_count * (2 * coupling.size * cells[0] * cells[2] + 4 * dofs * voxels),
            bytes_accessed=extended.size * 4 + coupling.size * 4 + 2 * voxels * 4,
            transcendentals=0,
        ),
    )(extended, coupling)


def shards(design, passive, basis_pairs, supports, stiffness, mass_matrix, volume_fraction):
    block_shape = design.shape
    size_x, size_y, size_z = block_shape
    devices_x = lax.axis_size("gx")
    devices_y = lax.axis_size("gy")
    index_x = lax.axis_index("gx")
    index_y = lax.axis_index("gy")
    grid_x = size_x * devices_x
    grid_y = size_y * devices_y
    spread_x = jnp.arange(size_x + 4, dtype=jnp.int32) + index_x * size_x - 2
    spread_y = jnp.arange(size_y + 4, dtype=jnp.int32) + index_y * size_y - 2
    valid_x = ((spread_x >= 0) & (spread_x < grid_x)).astype(jnp.float32)
    valid_y = ((spread_y >= 0) & (spread_y < grid_y)).astype(jnp.float32)
    valid_z = jnp.pad(jnp.ones((size_z,), jnp.float32), 2)
    inside = valid_x[:, None, None] * valid_y[None, :, None] * valid_z[None, None, :]
    weight_sum = stencil(inside, block_shape)
    fields = basis_pairs * (1 - supports).astype(jnp.float32)
    design_wide, extended = front_exchange(design, fields, 2)
    design_wide = jnp.pad(design_wide, ((0, 0), (0, 0), (2, 2)))
    physical = jnp.where(passive == 1, 1.0, stencil(design_wide, block_shape) / weight_sum)
    stiff_energy, mass_energy = element_energies(extended, stiffness, mass_matrix)
    raw_sensitivity = -(
        PENALTY_SCALE * physical * physical * stiff_energy - OMEGA_SQUARED * mass_energy
    )
    raw_sensitivity = jnp.where(passive == 1, 0.0, raw_sensitivity)
    scaled_wide = with_halo(raw_sensitivity / weight_sum, (("gx", 0), ("gy", 1)), 2)
    scaled_wide = jnp.pad(scaled_wide, ((0, 0), (0, 0), (2, 2)))
    sensitivity = stencil(scaled_wide, block_shape)
    benefit = jnp.maximum(-sensitivity, 0.0)
    floor_value = jnp.maximum(design - MOVE_LIMIT, 0.0)
    ceiling = jnp.minimum(design + MOVE_LIMIT, 1.0)
    band_cells = size_z // REGIONS
    target = volume_fraction * float(grid_x * grid_y * band_cells)

    def candidate(multiplier):
        per_cell = jnp.repeat(multiplier, band_cells)[None, None, :]
        trial = design * jnp.sqrt(benefit / per_cell)
        return jnp.where(passive == 1, 1.0, jnp.minimum(ceiling, jnp.maximum(floor_value, trial)))

    def region_sum(field):
        return jnp.sum(field, axis=(0, 1)).reshape(REGIONS, band_cells).sum(axis=1)

    levels = BISECT

    def bisect_round(round_index, bracket):
        low_end, high_end = bracket
        level_nodes = [(low_end, high_end)]
        midpoints = []
        for depth in range(levels):
            next_nodes = []
            for node_low, node_high in level_nodes:
                middle = jnp.sqrt(node_low * node_high)
                midpoints.append(middle)
                next_nodes.append((node_low, middle))
                next_nodes.append((middle, node_high))
            level_nodes = next_nodes
        trial_multipliers = jnp.stack(midpoints)
        per_cell = jnp.repeat(trial_multipliers, band_cells, axis=1)[:, None, None, :]
        trial = design[None] * jnp.sqrt(benefit[None] / per_cell)
        fields_of = jnp.where(
            passive[None] == 1, 1.0, jnp.minimum(ceiling[None], jnp.maximum(floor_value[None], trial))
        )
        partial_volumes = (
            jnp.sum(fields_of, axis=(1, 2)).reshape(len(midpoints), REGIONS, band_cells).sum(axis=2)
        )
        volumes = butterfly_sum(butterfly_sum(partial_volumes, "gy"), "gx")
        heavier_all = volumes > target[None, :]
        position = jnp.zeros((REGIONS,), jnp.int32)
        for depth in range(levels):
            middle = jnp.sqrt(low_end * high_end)
            nodes = lax.slice_in_dim(heavier_all, 2**depth - 1, 2 ** (depth + 1) - 1, axis=0)
            slots = lax.broadcasted_iota(jnp.int32, nodes.shape, 0)
            heavier = jnp.any(nodes & (slots == position[None, :]), axis=0)
            low_end = jnp.where(heavier, middle, low_end)
            high_end = jnp.where(heavier, high_end, middle)
            position = 2 * position + heavier.astype(jnp.int32)
        return (low_end, high_end)

    start = (jnp.full((REGIONS,), 0.0001, jnp.float32), jnp.full((REGIONS,), 10000.0, jnp.float32))
    low_end, high_end = bisect_round(0, start)
    design_next = candidate(jnp.sqrt(low_end * high_end))
    return (sensitivity, design_next)


def solution(mesh):
    placed = (
        P("gx", "gy", None),
        P("gx", "gy", None),
        P(None, None, None, "gx", "gy", None),
        P("gx", "gy", None),
        P(),
        P(),
        P(),
    )
    return jax.shard_map(
        shards,
        mesh=mesh,
        in_specs=placed,
        out_specs=(P("gx", "gy", None), P("gx", "gy", None)),
        check_vma=False,
    )
```

```python
import math

import jax
import jax.numpy as jnp
from jax import lax
from jax.sharding import PartitionSpec as P
from jax.experimental import pallas as pl
from jax.experimental.pallas import tpu as pltpu

BISECT = 6
REGIONS = 64


PENALTY_SCALE = 3.0 * (1.0 - 0.001)
OMEGA_SQUARED = 0.5
MOVE_LIMIT = 0.2


def with_halo(cells, sides, width):
    for axis, dim in sides:
        count = lax.axis_size(axis)
        ends = count - 1
        head = lax.slice_in_dim(cells, 0, width, axis=dim)
        tail = lax.slice_in_dim(cells, cells.shape[dim] - width, cells.shape[dim], axis=dim)
        cells = jnp.concatenate(
            [
                lax.ppermute(tail, axis, [(i, (i + 1) % count) for i in range(ends)]),
                cells,
                lax.ppermute(head, axis, [((i + 1) % count, i) for i in range(ends)]),
            ],
            axis=dim,
        )
    return cells


def front_exchange(cells, fields, width):
    for axis, dim in (("gx", 0), ("gy", 1)):
        count = lax.axis_size(axis)
        ends = count - 1
        field_dim = dim + 3
        head = lax.slice_in_dim(cells, 0, width, axis=dim)
        tail = lax.slice_in_dim(cells, cells.shape[dim] - width, cells.shape[dim], axis=dim)
        rim = lax.slice_in_dim(fields, 0, 1, axis=field_dim)
        lanes = cells.shape[-1]
        packed = jnp.concatenate([head.reshape(-1, lanes), rim.reshape(-1, lanes)], axis=0)
        packed = lax.ppermute(packed, axis, [((i + 1) % count, i) for i in range(ends)])
        split = head.size // lanes
        head = packed[:split].reshape(head.shape)
        rim = packed[split:].reshape(rim.shape)
        tail = lax.ppermute(tail, axis, [(i, (i + 1) % count) for i in range(ends)])
        cells = jnp.concatenate([tail, cells, head], axis=dim)
        fields = jnp.concatenate([fields, rim], axis=field_dim)
    return cells, fields


def from_behind(value, axis, steps):
    count = lax.axis_size(axis)
    initial, last = (max(0, -steps), min(count, count - steps))
    return lax.ppermute(value, axis, [(source, source + steps) for source in range(initial, last)])


def butterfly_sum(value, axis):
    count = lax.axis_size(axis)
    stride = 1
    while stride < count:
        value = value + lax.ppermute(value, axis, [(i, i ^ stride) for i in range(count)])
        stride *= 2
    return value


def filter_taps():
    tap_list = []
    for offset_x in range(-2, 3):
        for offset_y in range(-2, 3):
            for offset_z in range(-2, 3):
                weight = 3.0 - math.sqrt(
                    offset_x * offset_x + offset_y * offset_y + offset_z * offset_z
                )
                if weight > 0.0:
                    tap_list.append((offset_x, offset_y, offset_z, weight))
    return tap_list


def stencil(padded, block_shape):
    result = jnp.zeros(block_shape, jnp.float32)
    for offset_x, offset_y, offset_z, weight in filter_taps():
        result = (
            result
            + weight
            * padded[
                2 + offset_x : 2 + offset_x + block_shape[0],
                2 + offset_y : 2 + offset_y + block_shape[1],
                2 + offset_z : 2 + offset_z + block_shape[2],
            ]
        )
    return result


def element_terms(extended, stiffness, mass_matrix):
    pair_count = extended.shape[0]
    cells_x = extended.shape[3] - 1
    cells_y = extended.shape[4] - 1
    cells_z = extended.shape[5] - 1
    stiff_energy = jnp.zeros((cells_x * cells_y * cells_z,), jnp.float32)
    mass_energy = jnp.zeros((cells_x * cells_y * cells_z,), jnp.float32)
    for pair_index in range(pair_count):
        vectors = []
        for member in range(2):
            row_list = []
            for corner_x in (0, 1):
                for corner_y in (0, 1):
                    for corner_z in (0, 1):
                        for component in range(3):
                            row_list.append(
                                extended[
                                    pair_index,
                                    member,
                                    component,
                                    corner_x : corner_x + cells_x,
                                    corner_y : corner_y + cells_y,
                                    corner_z : corner_z + cells_z,
                                ].reshape(-1)
                            )
            vectors.append(jnp.stack(row_list))
        state_rows, adjoint_rows = vectors
        stiff_energy = stiff_energy + jnp.sum(
            state_rows * jnp.dot(stiffness, adjoint_rows, precision=lax.Precision.HIGHEST), axis=0
        )
        mass_energy = mass_energy + jnp.sum(
            state_rows * jnp.dot(mass_matrix, adjoint_rows, precision=lax.Precision.HIGHEST), axis=0
        )
    return (
        stiff_energy.reshape(cells_x, cells_y, cells_z),
        mass_energy.reshape(cells_x, cells_y, cells_z),
    )


CORNERS = [(a, b, d) for a in (0, 1) for b in (0, 1) for d in (0, 1)]


def energy_kernel(extended_ref, stiffness_ref, mass_ref, stiff_out, mass_out):
    pair_count = extended_ref.shape[0]
    cells_x, cells_y, cells_z = stiff_out.shape
    lane = lax.broadcasted_iota(jnp.int32, (cells_y, cells_z), 1)
    inside = lane < cells_z - 1

    def node_view(pair, member, component, x, corner):
        corner_x, corner_y, corner_z = corner
        value = extended_ref[pair, member, component, x + corner_x, pl.ds(corner_y, cells_y), :]
        if corner_z:
            value = jnp.where(inside, pltpu.roll(value, cells_z - 1, 1), 0.0)
        return value

    def over_pairs(pair, energies):
        stiff_sum, mass_sum, x = energies
        adjoint = [
            node_view(pair, 1, component, x, corner) for corner in CORNERS for component in range(3)
        ]
        for row in range(len(adjoint)):
            state = node_view(pair, 0, row % 3, x, CORNERS[row // 3])
            stiff_row = stiffness_ref[row, 0] * adjoint[0]
            mass_row = mass_ref[row, 0] * adjoint[0]
            for column in range(1, len(adjoint)):
                stiff_row = stiff_row + stiffness_ref[row, column] * adjoint[column]
                mass_row = mass_row + mass_ref[row, column] * adjoint[column]
            stiff_sum = stiff_sum + state * stiff_row
            mass_sum = mass_sum + state * mass_row
        return stiff_sum, mass_sum, x

    def over_x(x, carry):
        zero = jnp.zeros((cells_y, cells_z), jnp.float32)
        stiff_sum, mass_sum, _ = lax.fori_loop(0, pair_count, over_pairs, (zero, zero, x))
        stiff_out[x] = stiff_sum
        mass_out[x] = mass_sum
        return carry

    lax.fori_loop(0, cells_x, over_x, 0)


def mxu_energy_kernel(
    extended_ref, stiffness_ref, mass_ref, stiff_out, mass_out, coupling_ref, adjoint_rows, products
):
    pair_count = extended_ref.shape[0]
    cells_x, cells_y, cells_z = stiff_out.shape
    dofs = 3 * len(CORNERS)
    wide = dofs * cells_y
    spread_rows = (
        lax.broadcasted_iota(jnp.int32, (wide, dofs), 0) // cells_y
        == lax.broadcasted_iota(jnp.int32, (wide, dofs), 1)
    ).astype(jnp.float32)
    spread_columns = (
        lax.broadcasted_iota(jnp.int32, (dofs, wide), 0)
        == lax.broadcasted_iota(jnp.int32, (dofs, wide), 1) // cells_y
    ).astype(jnp.float32)
    same_y = (
        lax.broadcasted_iota(jnp.int32, (wide, wide), 0) % cells_y
        == lax.broadcasted_iota(jnp.int32, (wide, wide), 1) % cells_y
    )
    for block, matrix_ref in enumerate((stiffness_ref, mass_ref)):
        spread = jnp.dot(
            matrix_ref[...], spread_columns, precision=lax.Precision.HIGHEST,
            preferred_element_type=jnp.float32,
        )
        spread = jnp.dot(
            spread_rows, spread, precision=lax.Precision.HIGHEST, preferred_element_type=jnp.float32
        )
        coupling_ref[pl.ds(block * wide, wide), :] = jnp.where(same_y, spread, 0.0)
    lane = lax.broadcasted_iota(jnp.int32, (cells_y, cells_z), 1)
    inside = lane < cells_z - 1
    stiff_out[...] = jnp.zeros(stiff_out.shape, jnp.float32)
    mass_out[...] = jnp.zeros(mass_out.shape, jnp.float32)

    def node_view(pair, member, row, x):
        corner_x, corner_y, corner_z = CORNERS[row // 3]
        value = extended_ref[pair, member, row % 3, x + corner_x, pl.ds(corner_y, cells_y), :]
        if corner_z:
            value = jnp.where(inside, pltpu.roll(value, cells_z - 1, 1), 0.0)
        return value

    def over_pairs(pair, carry):
        def gather_x(x, inner):
            columns = pl.ds(pl.multiple_of(x * cells_z, cells_z), cells_z)
            for row in range(dofs):
                adjoint_rows[pl.ds(row * cells_y, cells_y), columns] = node_view(pair, 1, row, x)
            return inner

        lax.fori_loop(0, cells_x, gather_x, 0)
        products[...] = jnp.dot(
            coupling_ref[...],
            adjoint_rows[...],
            precision=lax.Precision.HIGHEST,
            preferred_element_type=jnp.float32,
        )

        def reduce_x(x, inner):
            columns = pl.ds(pl.multiple_of(x * cells_z, cells_z), cells_z)
            stiff_sum = stiff_out[x]
            mass_sum = mass_out[x]
            for row in range(dofs):
                state = node_view(pair, 0, row, x)
                stiff_sum = stiff_sum + state * products[pl.ds(row * cells_y, cells_y), columns]
                mass_sum = mass_sum + state * products[pl.ds((dofs + row) * cells_y, cells_y), columns]
            stiff_out[x] = stiff_sum
            mass_out[x] = mass_sum
            return inner

        lax.fori_loop(0, cells_x, reduce_x, 0)
        return carry

    lax.fori_loop(0, pair_count, over_pairs, 0)


def element_energies(extended, stiffness, mass_matrix):
    pair_count = extended.shape[0]
    cells = (extended.shape[3] - 1, extended.shape[4] - 1, extended.shape[5])
    voxels = cells[0] * cells[1] * cells[2]
    dofs = stiffness.shape[0]
    vmem = pl.BlockSpec(memory_space=pltpu.VMEM)
    return pl.pallas_call(
        mxu_energy_kernel,
        out_shape=(
            jax.ShapeDtypeStruct(cells, jnp.float32),
            jax.ShapeDtypeStruct(cells, jnp.float32),
        ),
        in_specs=[vmem, vmem, vmem],
        out_specs=(vmem, vmem),
        scratch_shapes=[
            pltpu.VMEM((2 * dofs * cells[1], dofs * cells[1]), jnp.float32),
            pltpu.VMEM((dofs * cells[1], cells[0] * cells[2]), jnp.float32),
            pltpu.VMEM((2 * dofs * cells[1], cells[0] * cells[2]), jnp.float32),
        ],
        cost_estimate=pl.CostEstimate(
            flops=pair_count * (4 * (dofs * cells[1]) ** 2 * cells[0] * cells[2] + 4 * dofs * voxels),
            bytes_accessed=extended.size * 4 + 2 * stiffness.size * 4 + 2 * voxels * 4,
            transcendentals=0,
        ),
    )(extended, stiffness, mass_matrix)


def shards(design, passive, basis_pairs, supports, stiffness, mass_matrix, volume_fraction):
    block_shape = design.shape
    size_x, size_y, size_z = block_shape
    devices_x = lax.axis_size("gx")
    devices_y = lax.axis_size("gy")
    index_x = lax.axis_index("gx")
    index_y = lax.axis_index("gy")
    grid_x = size_x * devices_x
    grid_y = size_y * devices_y
    spread_x = jnp.arange(size_x + 4, dtype=jnp.int32) + index_x * size_x - 2
    spread_y = jnp.arange(size_y + 4, dtype=jnp.int32) + index_y * size_y - 2
    valid_x = ((spread_x >= 0) & (spread_x < grid_x)).astype(jnp.float32)
    valid_y = ((spread_y >= 0) & (spread_y < grid_y)).astype(jnp.float32)
    valid_z = jnp.pad(jnp.ones((size_z,), jnp.float32), 2)
    inside = valid_x[:, None, None] * valid_y[None, :, None] * valid_z[None, None, :]
    weight_sum = stencil(inside, block_shape)
    fields = basis_pairs * (1 - supports).astype(jnp.float32)
    design_wide, extended = front_exchange(design, fields, 2)
    design_wide = jnp.pad(design_wide, ((0, 0), (0, 0), (2, 2)))
    physical = jnp.where(passive == 1, 1.0, stencil(design_wide, block_shape) / weight_sum)
    stiff_energy, mass_energy = element_energies(extended, stiffness, mass_matrix)
    raw_sensitivity = -(
        PENALTY_SCALE * physical * physical * stiff_energy - OMEGA_SQUARED * mass_energy
    )
    raw_sensitivity = jnp.where(passive == 1, 0.0, raw_sensitivity)
    scaled_wide = with_halo(raw_sensitivity / weight_sum, (("gx", 0), ("gy", 1)), 2)
    scaled_wide = jnp.pad(scaled_wide, ((0, 0), (0, 0), (2, 2)))
    sensitivity = stencil(scaled_wide, block_shape)
    benefit = jnp.maximum(-sensitivity, 0.0)
    floor_value = jnp.maximum(design - MOVE_LIMIT, 0.0)
    ceiling = jnp.minimum(design + MOVE_LIMIT, 1.0)
    band_cells = size_z // REGIONS
    target = volume_fraction * float(grid_x * grid_y * band_cells)

    def candidate(multiplier):
        per_cell = jnp.repeat(multiplier, band_cells)[None, None, :]
        trial = design * jnp.sqrt(benefit / per_cell)
        return jnp.where(passive == 1, 1.0, jnp.minimum(ceiling, jnp.maximum(floor_value, trial)))

    def region_sum(field):
        return jnp.sum(field, axis=(0, 1)).reshape(REGIONS, band_cells).sum(axis=1)

    levels = BISECT

    def bisect_round(round_index, bracket):
        low_end, high_end = bracket
        level_nodes = [(low_end, high_end)]
        midpoints = []
        for depth in range(levels):
            next_nodes = []
            for node_low, node_high in level_nodes:
                middle = jnp.sqrt(node_low * node_high)
                midpoints.append(middle)
                next_nodes.append((node_low, middle))
                next_nodes.append((middle, node_high))
            level_nodes = next_nodes
        trial_multipliers = jnp.stack(midpoints)
        per_cell = jnp.repeat(trial_multipliers, band_cells, axis=1)[:, None, None, :]
        trial = design[None] * jnp.sqrt(benefit[None] / per_cell)
        fields_of = jnp.where(
            passive[None] == 1, 1.0, jnp.minimum(ceiling[None], jnp.maximum(floor_value[None], trial))
        )
        partial_volumes = (
            jnp.sum(fields_of, axis=(1, 2)).reshape(len(midpoints), REGIONS, band_cells).sum(axis=2)
        )
        volumes = butterfly_sum(butterfly_sum(partial_volumes, "gy"), "gx")
        heavier_all = volumes > target[None, :]
        position = jnp.zeros((REGIONS,), jnp.int32)
        for depth in range(levels):
            middle = jnp.sqrt(low_end * high_end)
            nodes = lax.slice_in_dim(heavier_all, 2**depth - 1, 2 ** (depth + 1) - 1, axis=0)
            slots = lax.broadcasted_iota(jnp.int32, nodes.shape, 0)
            heavier = jnp.any(nodes & (slots == position[None, :]), axis=0)
            low_end = jnp.where(heavier, middle, low_end)
            high_end = jnp.where(heavier, high_end, middle)
            position = 2 * position + heavier.astype(jnp.int32)
        return (low_end, high_end)

    start = (jnp.full((REGIONS,), 0.0001, jnp.float32), jnp.full((REGIONS,), 10000.0, jnp.float32))
    low_end, high_end = bisect_round(0, start)
    design_next = candidate(jnp.sqrt(low_end * high_end))
    return (sensitivity, design_next)


def solution(mesh):
    placed = (
        P("gx", "gy", None),
        P("gx", "gy", None),
        P(None, None, None, "gx", "gy", None),
        P("gx", "gy", None),
        P(),
        P(),
        P(),
    )
    return jax.shard_map(
        shards,
        mesh=mesh,
        in_specs=placed,
        out_specs=(P("gx", "gy", None), P("gx", "gy", None)),
        check_vma=False,
    )
```

```python
import functools
import math

import jax
import jax.numpy as jnp
from jax import lax
from jax.sharding import PartitionSpec as P
from jax.experimental import pallas as pl
from jax.experimental.pallas import tpu as pltpu

BISECT = 6
REGIONS = 64


PENALTY_SCALE = 3.0 * (1.0 - 0.001)
OMEGA_SQUARED = 0.5
MOVE_LIMIT = 0.2


def with_halo(cells, sides, width):
    for axis, dim in sides:
        count = lax.axis_size(axis)
        ends = count - 1
        head = lax.slice_in_dim(cells, 0, width, axis=dim)
        tail = lax.slice_in_dim(cells, cells.shape[dim] - width, cells.shape[dim], axis=dim)
        cells = jnp.concatenate(
            [
                lax.ppermute(tail, axis, [(i, (i + 1) % count) for i in range(ends)]),
                cells,
                lax.ppermute(head, axis, [((i + 1) % count, i) for i in range(ends)]),
            ],
            axis=dim,
        )
    return cells


def front_exchange(cells, fields, width):
    stages = []
    for axis, dim in (("gy", 1), ("gx", 0)):
        count = lax.axis_size(axis)
        ends = count - 1
        field_dim = dim + 3
        head = lax.slice_in_dim(cells, 0, width, axis=dim)
        tail = lax.slice_in_dim(cells, cells.shape[dim] - width, cells.shape[dim], axis=dim)
        rim = lax.slice_in_dim(fields, 0, 1, axis=field_dim)
        lanes = cells.shape[-1]
        packed = jnp.concatenate([head.reshape(-1, lanes), rim.reshape(-1, lanes)], axis=0)
        packed = lax.ppermute(packed, axis, [((i + 1) % count, i) for i in range(ends)])
        split = head.size // lanes
        head = packed[:split].reshape(head.shape)
        rim = packed[split:].reshape(rim.shape)
        tail = lax.ppermute(tail, axis, [(i, (i + 1) % count) for i in range(ends)])
        cells = jnp.concatenate([tail, cells, head], axis=dim)
        fields = jnp.concatenate([fields, rim], axis=field_dim)
        stages.append(fields)
    return cells, stages[0], stages[1]


def from_behind(value, axis, steps):
    count = lax.axis_size(axis)
    initial, last = (max(0, -steps), min(count, count - steps))
    return lax.ppermute(value, axis, [(source, source + steps) for source in range(initial, last)])


def butterfly_sum(value, axis):
    count = lax.axis_size(axis)
    stride = 1
    while stride < count:
        value = value + lax.ppermute(value, axis, [(i, i ^ stride) for i in range(count)])
        stride *= 2
    return value


def filter_taps():
    tap_list = []
    for offset_x in range(-2, 3):
        for offset_y in range(-2, 3):
            for offset_z in range(-2, 3):
                weight = 3.0 - math.sqrt(
                    offset_x * offset_x + offset_y * offset_y + offset_z * offset_z
                )
                if weight > 0.0:
                    tap_list.append((offset_x, offset_y, offset_z, weight))
    return tap_list


def stencil(padded, block_shape):
    result = jnp.zeros(block_shape, jnp.float32)
    for offset_x, offset_y, offset_z, weight in filter_taps():
        result = (
            result
            + weight
            * padded[
                2 + offset_x : 2 + offset_x + block_shape[0],
                2 + offset_y : 2 + offset_y + block_shape[1],
                2 + offset_z : 2 + offset_z + block_shape[2],
            ]
        )
    return result


def element_terms(extended, stiffness, mass_matrix):
    pair_count = extended.shape[0]
    cells_x = extended.shape[3] - 1
    cells_y = extended.shape[4] - 1
    cells_z = extended.shape[5] - 1
    stiff_energy = jnp.zeros((cells_x * cells_y * cells_z,), jnp.float32)
    mass_energy = jnp.zeros((cells_x * cells_y * cells_z,), jnp.float32)
    for pair_index in range(pair_count):
        vectors = []
        for member in range(2):
            row_list = []
            for corner_x in (0, 1):
                for corner_y in (0, 1):
                    for corner_z in (0, 1):
                        for component in range(3):
                            row_list.append(
                                extended[
                                    pair_index,
                                    member,
                                    component,
                                    corner_x : corner_x + cells_x,
                                    corner_y : corner_y + cells_y,
                                    corner_z : corner_z + cells_z,
                                ].reshape(-1)
                            )
            vectors.append(jnp.stack(row_list))
        state_rows, adjoint_rows = vectors
        stiff_energy = stiff_energy + jnp.sum(
            state_rows * jnp.dot(stiffness, adjoint_rows, precision=lax.Precision.HIGHEST), axis=0
        )
        mass_energy = mass_energy + jnp.sum(
            state_rows * jnp.dot(mass_matrix, adjoint_rows, precision=lax.Precision.HIGHEST), axis=0
        )
    return (
        stiff_energy.reshape(cells_x, cells_y, cells_z),
        mass_energy.reshape(cells_x, cells_y, cells_z),
    )


CORNERS = [(a, b, d) for a in (0, 1) for b in (0, 1) for d in (0, 1)]


def energy_kernel(extended_ref, stiffness_ref, mass_ref, stiff_out, mass_out):
    pair_count = extended_ref.shape[0]
    cells_x, cells_y, cells_z = stiff_out.shape
    lane = lax.broadcasted_iota(jnp.int32, (cells_y, cells_z), 1)
    inside = lane < cells_z - 1

    def node_view(pair, member, component, x, corner):
        corner_x, corner_y, corner_z = corner
        value = extended_ref[pair, member, component, x + corner_x, pl.ds(corner_y, cells_y), :]
        if corner_z:
            value = jnp.where(inside, pltpu.roll(value, cells_z - 1, 1), 0.0)
        return value

    def over_pairs(pair, energies):
        stiff_sum, mass_sum, x = energies
        adjoint = [
            node_view(pair, 1, component, x, corner) for corner in CORNERS for component in range(3)
        ]
        for row in range(len(adjoint)):
            state = node_view(pair, 0, row % 3, x, CORNERS[row // 3])
            stiff_row = stiffness_ref[row, 0] * adjoint[0]
            mass_row = mass_ref[row, 0] * adjoint[0]
            for column in range(1, len(adjoint)):
                stiff_row = stiff_row + stiffness_ref[row, column] * adjoint[column]
                mass_row = mass_row + mass_ref[row, column] * adjoint[column]
            stiff_sum = stiff_sum + state * stiff_row
            mass_sum = mass_sum + state * mass_row
        return stiff_sum, mass_sum, x

    def over_x(x, carry):
        zero = jnp.zeros((cells_y, cells_z), jnp.float32)
        stiff_sum, mass_sum, _ = lax.fori_loop(0, pair_count, over_pairs, (zero, zero, x))
        stiff_out[x] = stiff_sum
        mass_out[x] = mass_sum
        return carry

    lax.fori_loop(0, cells_x, over_x, 0)


def mxu_energy_kernel(
    slices, extended_ref, stiffness_ref, mass_ref, stiff_out, mass_out, coupling_ref, adjoint_rows,
    products,
):
    pair_count = extended_ref.shape[0]
    _, cells_y, cells_z = stiff_out.shape
    dofs = 3 * len(CORNERS)
    wide = dofs * cells_y
    spread_rows = (
        lax.broadcasted_iota(jnp.int32, (wide, dofs), 0) // cells_y
        == lax.broadcasted_iota(jnp.int32, (wide, dofs), 1)
    ).astype(jnp.float32)
    spread_columns = (
        lax.broadcasted_iota(jnp.int32, (dofs, wide), 0)
        == lax.broadcasted_iota(jnp.int32, (dofs, wide), 1) // cells_y
    ).astype(jnp.float32)
    same_y = (
        lax.broadcasted_iota(jnp.int32, (wide, wide), 0) % cells_y
        == lax.broadcasted_iota(jnp.int32, (wide, wide), 1) % cells_y
    )
    for block, matrix_ref in enumerate((stiffness_ref, mass_ref)):
        spread = jnp.dot(
            matrix_ref[...], spread_columns, precision=lax.Precision.HIGHEST,
            preferred_element_type=jnp.float32,
        )
        spread = jnp.dot(
            spread_rows, spread, precision=lax.Precision.HIGHEST, preferred_element_type=jnp.float32
        )
        coupling_ref[pl.ds(block * wide, wide), :] = jnp.where(same_y, spread, 0.0)
    lane = lax.broadcasted_iota(jnp.int32, (cells_y, cells_z), 1)
    inside = lane < cells_z - 1
    stiff_out[...] = jnp.zeros(stiff_out.shape, jnp.float32)
    mass_out[...] = jnp.zeros(mass_out.shape, jnp.float32)

    def node_view(pair, member, row, x):
        corner_x, corner_y, corner_z = CORNERS[row // 3]
        value = extended_ref[pair, member, row % 3, x + corner_x, pl.ds(corner_y, cells_y), :]
        if corner_z:
            value = jnp.where(inside, pltpu.roll(value, cells_z - 1, 1), 0.0)
        return value

    def over_pairs(pair, carry):
        for place, x in enumerate(slices):
            columns = pl.ds(place * cells_z, cells_z)
            for row in range(dofs):
                adjoint_rows[pl.ds(row * cells_y, cells_y), columns] = node_view(pair, 1, row, x)
        products[...] = jnp.dot(
            coupling_ref[...],
            adjoint_rows[...],
            precision=lax.Precision.HIGHEST,
            preferred_element_type=jnp.float32,
        )
        for place, x in enumerate(slices):
            columns = pl.ds(place * cells_z, cells_z)
            stiff_sum = stiff_out[place]
            mass_sum = mass_out[place]
            for row in range(dofs):
                state = node_view(pair, 0, row, x)
                stiff_sum = stiff_sum + state * products[pl.ds(row * cells_y, cells_y), columns]
                mass_sum = mass_sum + state * products[pl.ds((dofs + row) * cells_y, cells_y), columns]
            stiff_out[place] = stiff_sum
            mass_out[place] = mass_sum
        return carry

    lax.fori_loop(0, pair_count, over_pairs, 0)


def element_energies(extended, stiffness, mass_matrix, slices):
    pair_count = extended.shape[0]
    cells = (len(slices), extended.shape[4] - 1, extended.shape[5])
    voxels = cells[0] * cells[1] * cells[2]
    dofs = stiffness.shape[0]
    vmem = pl.BlockSpec(memory_space=pltpu.VMEM)
    return pl.pallas_call(
        functools.partial(mxu_energy_kernel, slices),
        out_shape=(
            jax.ShapeDtypeStruct(cells, jnp.float32),
            jax.ShapeDtypeStruct(cells, jnp.float32),
        ),
        in_specs=[vmem, vmem, vmem],
        out_specs=(vmem, vmem),
        scratch_shapes=[
            pltpu.VMEM((2 * dofs * cells[1], dofs * cells[1]), jnp.float32),
            pltpu.VMEM((dofs * cells[1], cells[0] * cells[2]), jnp.float32),
            pltpu.VMEM((2 * dofs * cells[1], cells[0] * cells[2]), jnp.float32),
        ],
        cost_estimate=pl.CostEstimate(
            flops=pair_count * (4 * (dofs * cells[1]) ** 2 * cells[0] * cells[2] + 4 * dofs * voxels),
            bytes_accessed=extended.size * 4 + 2 * stiffness.size * 4 + 2 * voxels * 4,
            transcendentals=0,
        ),
    )(extended, stiffness, mass_matrix)


def shards(design, passive, basis_pairs, supports, stiffness, mass_matrix, volume_fraction):
    block_shape = design.shape
    size_x, size_y, size_z = block_shape
    devices_x = lax.axis_size("gx")
    devices_y = lax.axis_size("gy")
    index_x = lax.axis_index("gx")
    index_y = lax.axis_index("gy")
    grid_x = size_x * devices_x
    grid_y = size_y * devices_y
    spread_x = jnp.arange(size_x + 4, dtype=jnp.int32) + index_x * size_x - 2
    spread_y = jnp.arange(size_y + 4, dtype=jnp.int32) + index_y * size_y - 2
    valid_x = ((spread_x >= 0) & (spread_x < grid_x)).astype(jnp.float32)
    valid_y = ((spread_y >= 0) & (spread_y < grid_y)).astype(jnp.float32)
    valid_z = jnp.pad(jnp.ones((size_z,), jnp.float32), 2)
    inside = valid_x[:, None, None] * valid_y[None, :, None] * valid_z[None, None, :]
    weight_sum = stencil(inside, block_shape)
    fields = basis_pairs * (1 - supports).astype(jnp.float32)
    design_wide, widened, extended = front_exchange(design, fields, 2)
    design_wide = jnp.pad(design_wide, ((0, 0), (0, 0), (2, 2)))
    physical = jnp.where(passive == 1, 1.0, stencil(design_wide, block_shape) / weight_sum)
    last = size_x - 1
    early = (0, 1, last - 1)
    middle_slices = tuple(range(2, last - 1))
    parts = [
        element_energies(widened, stiffness, mass_matrix, early),
        element_energies(extended, stiffness, mass_matrix, (last,)),
        element_energies(widened, stiffness, mass_matrix, middle_slices),
    ]

    def scaled_raw(stiff_rows, mass_rows, first, end):
        physical_rows = physical[first:end]
        raw_rows = -(
            PENALTY_SCALE * physical_rows * physical_rows * stiff_rows - OMEGA_SQUARED * mass_rows
        )
        raw_rows = jnp.where(passive[first:end] == 1, 0.0, raw_rows)
        return raw_rows / weight_sum[first:end]

    (early_stiff, early_mass), (last_stiff, last_mass), (middle_stiff, middle_mass) = parts
    head_rows = scaled_raw(early_stiff[:2], early_mass[:2], 0, 2)
    tail_rows = scaled_raw(
        jnp.concatenate([early_stiff[2:], last_stiff], axis=0),
        jnp.concatenate([early_mass[2:], last_mass], axis=0),
        last - 1,
        last + 1,
    )
    middle_rows = scaled_raw(middle_stiff, middle_mass, 2, last - 1)
    count_x = lax.axis_size("gx")
    head_x = lax.ppermute(head_rows, "gx", [(i + 1, i) for i in range(count_x - 1)])
    tail_x = lax.ppermute(tail_rows, "gx", [(i, i + 1) for i in range(count_x - 1)])
    scaled = jnp.concatenate([head_rows, middle_rows, tail_rows], axis=0)
    scaled_wide = jnp.concatenate([tail_x, scaled, head_x], axis=0)
    scaled_wide = with_halo(scaled_wide, (("gy", 1),), 2)
    scaled_wide = jnp.pad(scaled_wide, ((0, 0), (0, 0), (2, 2)))
    sensitivity = stencil(scaled_wide, block_shape)
    benefit = jnp.maximum(-sensitivity, 0.0)
    floor_value = jnp.maximum(design - MOVE_LIMIT, 0.0)
    ceiling = jnp.minimum(design + MOVE_LIMIT, 1.0)
    band_cells = size_z // REGIONS
    target = volume_fraction * float(grid_x * grid_y * band_cells)

    def candidate(multiplier):
        per_cell = jnp.repeat(multiplier, band_cells)[None, None, :]
        trial = design * jnp.sqrt(benefit / per_cell)
        return jnp.where(passive == 1, 1.0, jnp.minimum(ceiling, jnp.maximum(floor_value, trial)))

    def region_sum(field):
        return jnp.sum(field, axis=(0, 1)).reshape(REGIONS, band_cells).sum(axis=1)

    levels = BISECT

    def bisect_round(round_index, bracket):
        low_end, high_end = bracket
        level_nodes = [(low_end, high_end)]
        midpoints = []
        for depth in range(levels):
            next_nodes = []
            for node_low, node_high in level_nodes:
                middle = jnp.sqrt(node_low * node_high)
                midpoints.append(middle)
                next_nodes.append((node_low, middle))
                next_nodes.append((middle, node_high))
            level_nodes = next_nodes
        trial_multipliers = jnp.stack(midpoints)
        per_cell = jnp.repeat(trial_multipliers, band_cells, axis=1)[:, None, None, :]
        trial = design[None] * jnp.sqrt(benefit[None] / per_cell)
        fields_of = jnp.where(
            passive[None] == 1, 1.0, jnp.minimum(ceiling[None], jnp.maximum(floor_value[None], trial))
        )
        partial_volumes = (
            jnp.sum(fields_of, axis=(1, 2)).reshape(len(midpoints), REGIONS, band_cells).sum(axis=2)
        )
        volumes = butterfly_sum(butterfly_sum(partial_volumes, "gy"), "gx")
        heavier_all = volumes > target[None, :]
        position = jnp.zeros((REGIONS,), jnp.int32)
        for depth in range(levels):
            middle = jnp.sqrt(low_end * high_end)
            nodes = lax.slice_in_dim(heavier_all, 2**depth - 1, 2 ** (depth + 1) - 1, axis=0)
            slots = lax.broadcasted_iota(jnp.int32, nodes.shape, 0)
            heavier = jnp.any(nodes & (slots == position[None, :]), axis=0)
            low_end = jnp.where(heavier, middle, low_end)
            high_end = jnp.where(heavier, high_end, middle)
            position = 2 * position + heavier.astype(jnp.int32)
        return (low_end, high_end)

    start = (jnp.full((REGIONS,), 0.0001, jnp.float32), jnp.full((REGIONS,), 10000.0, jnp.float32))
    low_end, high_end = bisect_round(0, start)
    design_next = candidate(jnp.sqrt(low_end * high_end))
    return (sensitivity, design_next)


def solution(mesh):
    placed = (
        P("gx", "gy", None),
        P("gx", "gy", None),
        P(None, None, None, "gx", "gy", None),
        P("gx", "gy", None),
        P(),
        P(),
        P(),
    )
    return jax.shard_map(
        shards,
        mesh=mesh,
        in_specs=placed,
        out_specs=(P("gx", "gy", None), P("gx", "gy", None)),
        check_vma=False,
    )
```

```python
import math

import jax
import jax.numpy as jnp
from jax import lax
from jax.sharding import PartitionSpec as P
from jax.experimental import pallas as pl
from jax.experimental.pallas import tpu as pltpu

BISECT = 6
REGIONS = 64


PENALTY_SCALE = 3.0 * (1.0 - 0.001)
OMEGA_SQUARED = 0.5
MOVE_LIMIT = 0.2


def with_halo(cells, sides, width):
    for axis, dim in sides:
        count = lax.axis_size(axis)
        ends = count - 1
        head = lax.slice_in_dim(cells, 0, width, axis=dim)
        tail = lax.slice_in_dim(cells, cells.shape[dim] - width, cells.shape[dim], axis=dim)
        cells = jnp.concatenate(
            [
                lax.ppermute(tail, axis, [(i, (i + 1) % count) for i in range(ends)]),
                cells,
                lax.ppermute(head, axis, [((i + 1) % count, i) for i in range(ends)]),
            ],
            axis=dim,
        )
    return cells


def front_exchange(cells, fields, width):
    for axis, dim in (("gx", 0), ("gy", 1)):
        count = lax.axis_size(axis)
        ends = count - 1
        field_dim = dim + 3
        head = lax.slice_in_dim(cells, 0, width, axis=dim)
        tail = lax.slice_in_dim(cells, cells.shape[dim] - width, cells.shape[dim], axis=dim)
        rim = lax.slice_in_dim(fields, 0, 1, axis=field_dim)
        lanes = cells.shape[-1]
        packed = jnp.concatenate([head.reshape(-1, lanes), rim.reshape(-1, lanes)], axis=0)
        packed = lax.ppermute(packed, axis, [((i + 1) % count, i) for i in range(ends)])
        split = head.size // lanes
        head = packed[:split].reshape(head.shape)
        rim = packed[split:].reshape(rim.shape)
        tail = lax.ppermute(tail, axis, [(i, (i + 1) % count) for i in range(ends)])
        cells = jnp.concatenate([tail, cells, head], axis=dim)
        fields = jnp.concatenate([fields, rim], axis=field_dim)
    return cells, fields


def from_behind(value, axis, steps):
    count = lax.axis_size(axis)
    initial, last = (max(0, -steps), min(count, count - steps))
    return lax.ppermute(value, axis, [(source, source + steps) for source in range(initial, last)])


def butterfly_sum(value, axis):
    count = lax.axis_size(axis)
    stride = 1
    while stride < count:
        value = value + lax.ppermute(value, axis, [(i, i ^ stride) for i in range(count)])
        stride *= 2
    return value


def filter_taps():
    tap_list = []
    for offset_x in range(-2, 3):
        for offset_y in range(-2, 3):
            for offset_z in range(-2, 3):
                weight = 3.0 - math.sqrt(
                    offset_x * offset_x + offset_y * offset_y + offset_z * offset_z
                )
                if weight > 0.0:
                    tap_list.append((offset_x, offset_y, offset_z, weight))
    return tap_list


def stencil(padded, block_shape):
    result = jnp.zeros(block_shape, jnp.float32)
    for offset_x, offset_y, offset_z, weight in filter_taps():
        result = (
            result
            + weight
            * padded[
                2 + offset_x : 2 + offset_x + block_shape[0],
                2 + offset_y : 2 + offset_y + block_shape[1],
                2 + offset_z : 2 + offset_z + block_shape[2],
            ]
        )
    return result


def element_terms(extended, stiffness, mass_matrix):
    pair_count = extended.shape[0]
    cells_x = extended.shape[3] - 1
    cells_y = extended.shape[4] - 1
    cells_z = extended.shape[5] - 1
    stiff_energy = jnp.zeros((cells_x * cells_y * cells_z,), jnp.float32)
    mass_energy = jnp.zeros((cells_x * cells_y * cells_z,), jnp.float32)
    for pair_index in range(pair_count):
        vectors = []
        for member in range(2):
            row_list = []
            for corner_x in (0, 1):
                for corner_y in (0, 1):
                    for corner_z in (0, 1):
                        for component in range(3):
                            row_list.append(
                                extended[
                                    pair_index,
                                    member,
                                    component,
                                    corner_x : corner_x + cells_x,
                                    corner_y : corner_y + cells_y,
                                    corner_z : corner_z + cells_z,
                                ].reshape(-1)
                            )
            vectors.append(jnp.stack(row_list))
        state_rows, adjoint_rows = vectors
        stiff_energy = stiff_energy + jnp.sum(
            state_rows * jnp.dot(stiffness, adjoint_rows, precision=lax.Precision.HIGHEST), axis=0
        )
        mass_energy = mass_energy + jnp.sum(
            state_rows * jnp.dot(mass_matrix, adjoint_rows, precision=lax.Precision.HIGHEST), axis=0
        )
    return (
        stiff_energy.reshape(cells_x, cells_y, cells_z),
        mass_energy.reshape(cells_x, cells_y, cells_z),
    )


CORNERS = [(a, b, d) for a in (0, 1) for b in (0, 1) for d in (0, 1)]


def energy_kernel(extended_ref, stiffness_ref, mass_ref, stiff_out, mass_out):
    pair_count = extended_ref.shape[0]
    cells_x, cells_y, cells_z = stiff_out.shape
    lane = lax.broadcasted_iota(jnp.int32, (cells_y, cells_z), 1)
    inside = lane < cells_z - 1

    def node_view(pair, member, component, x, corner):
        corner_x, corner_y, corner_z = corner
        value = extended_ref[pair, member, component, x + corner_x, pl.ds(corner_y, cells_y), :]
        if corner_z:
            value = jnp.where(inside, pltpu.roll(value, cells_z - 1, 1), 0.0)
        return value

    def over_pairs(pair, energies):
        stiff_sum, mass_sum, x = energies
        adjoint = [
            node_view(pair, 1, component, x, corner) for corner in CORNERS for component in range(3)
        ]
        for row in range(len(adjoint)):
            state = node_view(pair, 0, row % 3, x, CORNERS[row // 3])
            stiff_row = stiffness_ref[row, 0] * adjoint[0]
            mass_row = mass_ref[row, 0] * adjoint[0]
            for column in range(1, len(adjoint)):
                stiff_row = stiff_row + stiffness_ref[row, column] * adjoint[column]
                mass_row = mass_row + mass_ref[row, column] * adjoint[column]
            stiff_sum = stiff_sum + state * stiff_row
            mass_sum = mass_sum + state * mass_row
        return stiff_sum, mass_sum, x

    def over_x(x, carry):
        zero = jnp.zeros((cells_y, cells_z), jnp.float32)
        stiff_sum, mass_sum, _ = lax.fori_loop(0, pair_count, over_pairs, (zero, zero, x))
        stiff_out[x] = stiff_sum
        mass_out[x] = mass_sum
        return carry

    lax.fori_loop(0, cells_x, over_x, 0)


def mxu_energy_kernel(
    extended_ref, stiffness_ref, mass_ref, stiff_out, mass_out, coupling_ref, adjoint_rows, products
):
    pair_count = extended_ref.shape[0]
    cells_x, cells_y, cells_z = stiff_out.shape
    dofs = 3 * len(CORNERS)
    wide = dofs * cells_y
    spread_rows = (
        lax.broadcasted_iota(jnp.int32, (wide, dofs), 0) // cells_y
        == lax.broadcasted_iota(jnp.int32, (wide, dofs), 1)
    ).astype(jnp.float32)
    spread_columns = (
        lax.broadcasted_iota(jnp.int32, (dofs, wide), 0)
        == lax.broadcasted_iota(jnp.int32, (dofs, wide), 1) // cells_y
    ).astype(jnp.float32)
    same_y = (
        lax.broadcasted_iota(jnp.int32, (wide, wide), 0) % cells_y
        == lax.broadcasted_iota(jnp.int32, (wide, wide), 1) % cells_y
    )
    for block, matrix_ref in enumerate((stiffness_ref, mass_ref)):
        spread = jnp.dot(
            matrix_ref[...], spread_columns, precision=lax.Precision.HIGHEST,
            preferred_element_type=jnp.float32,
        )
        spread = jnp.dot(
            spread_rows, spread, precision=lax.Precision.HIGHEST, preferred_element_type=jnp.float32
        )
        coupling_ref[pl.ds(block * wide, wide), :] = jnp.where(same_y, spread, 0.0)
    lane = lax.broadcasted_iota(jnp.int32, (cells_y, cells_z), 1)
    inside = lane < cells_z - 1
    stiff_out[...] = jnp.zeros(stiff_out.shape, jnp.float32)
    mass_out[...] = jnp.zeros(mass_out.shape, jnp.float32)

    def node_view(pair, member, row, x):
        corner_x, corner_y, corner_z = CORNERS[row // 3]
        value = extended_ref[pair, member, row % 3, x + corner_x, pl.ds(corner_y, cells_y), :]
        if corner_z:
            value = jnp.where(inside, pltpu.roll(value, cells_z - 1, 1), 0.0)
        return value

    def over_pairs(pair, carry):
        def gather_x(x, inner):
            columns = pl.ds(pl.multiple_of(x * cells_z, cells_z), cells_z)
            for row in range(dofs):
                adjoint_rows[pl.ds(row * cells_y, cells_y), columns] = node_view(pair, 1, row, x)
            return inner

        lax.fori_loop(0, cells_x, gather_x, 0)
        products[...] = jnp.dot(
            coupling_ref[...],
            adjoint_rows[...],
            precision=lax.Precision.HIGHEST,
            preferred_element_type=jnp.float32,
        )

        def reduce_x(x, inner):
            columns = pl.ds(pl.multiple_of(x * cells_z, cells_z), cells_z)
            stiff_sum = stiff_out[x]
            mass_sum = mass_out[x]
            for row in range(dofs):
                state = node_view(pair, 0, row, x)
                stiff_sum = stiff_sum + state * products[pl.ds(row * cells_y, cells_y), columns]
                mass_sum = mass_sum + state * products[pl.ds((dofs + row) * cells_y, cells_y), columns]
            stiff_out[x] = stiff_sum
            mass_out[x] = mass_sum
            return inner

        lax.fori_loop(0, cells_x, reduce_x, 0)
        return carry

    lax.fori_loop(0, pair_count, over_pairs, 0)


def element_energies(extended, stiffness, mass_matrix):
    pair_count = extended.shape[0]
    cells = (extended.shape[3] - 1, extended.shape[4] - 1, extended.shape[5])
    voxels = cells[0] * cells[1] * cells[2]
    dofs = stiffness.shape[0]
    vmem = pl.BlockSpec(memory_space=pltpu.VMEM)
    return pl.pallas_call(
        mxu_energy_kernel,
        out_shape=(
            jax.ShapeDtypeStruct(cells, jnp.float32),
            jax.ShapeDtypeStruct(cells, jnp.float32),
        ),
        in_specs=[vmem, vmem, vmem],
        out_specs=(vmem, vmem),
        scratch_shapes=[
            pltpu.VMEM((2 * dofs * cells[1], dofs * cells[1]), jnp.float32),
            pltpu.VMEM((dofs * cells[1], cells[0] * cells[2]), jnp.float32),
            pltpu.VMEM((2 * dofs * cells[1], cells[0] * cells[2]), jnp.float32),
        ],
        cost_estimate=pl.CostEstimate(
            flops=pair_count * (4 * (dofs * cells[1]) ** 2 * cells[0] * cells[2] + 4 * dofs * voxels),
            bytes_accessed=extended.size * 4 + 2 * stiffness.size * 4 + 2 * voxels * 4,
            transcendentals=0,
        ),
    )(extended, stiffness, mass_matrix)


def shards(design, passive, basis_pairs, supports, stiffness, mass_matrix, volume_fraction):
    block_shape = design.shape
    size_x, size_y, size_z = block_shape
    devices_x = lax.axis_size("gx")
    devices_y = lax.axis_size("gy")
    index_x = lax.axis_index("gx")
    index_y = lax.axis_index("gy")
    grid_x = size_x * devices_x
    grid_y = size_y * devices_y
    spread_x = jnp.arange(size_x + 4, dtype=jnp.int32) + index_x * size_x - 2
    spread_y = jnp.arange(size_y + 4, dtype=jnp.int32) + index_y * size_y - 2
    valid_x = ((spread_x >= 0) & (spread_x < grid_x)).astype(jnp.float32)
    valid_y = ((spread_y >= 0) & (spread_y < grid_y)).astype(jnp.float32)
    valid_z = jnp.pad(jnp.ones((size_z,), jnp.float32), 2)
    inside = valid_x[:, None, None] * valid_y[None, :, None] * valid_z[None, None, :]
    weight_sum = stencil(inside, block_shape)
    fields = basis_pairs * (1 - supports).astype(jnp.float32)
    design_wide, extended = front_exchange(design, fields, 2)
    design_wide = jnp.pad(design_wide, ((0, 0), (0, 0), (2, 2)))
    physical = jnp.where(passive == 1, 1.0, stencil(design_wide, block_shape) / weight_sum)
    stiff_energy, mass_energy = element_energies(extended, stiffness, mass_matrix)
    raw_sensitivity = -(
        PENALTY_SCALE * physical * physical * stiff_energy - OMEGA_SQUARED * mass_energy
    )
    raw_sensitivity = jnp.where(passive == 1, 0.0, raw_sensitivity)
    scaled_wide = with_halo(raw_sensitivity / weight_sum, (("gx", 0), ("gy", 1)), 2)
    scaled_wide = jnp.pad(scaled_wide, ((0, 0), (0, 0), (2, 2)))
    sensitivity = stencil(scaled_wide, block_shape)
    benefit = jnp.maximum(-sensitivity, 0.0)
    floor_value = jnp.maximum(design - MOVE_LIMIT, 0.0)
    ceiling = jnp.minimum(design + MOVE_LIMIT, 1.0)
    band_cells = size_z // REGIONS
    target = volume_fraction * float(grid_x * grid_y * band_cells)

    def candidate(multiplier):
        per_cell = jnp.repeat(multiplier, band_cells)[None, None, :]
        trial = design * jnp.sqrt(benefit / per_cell)
        return jnp.where(passive == 1, 1.0, jnp.minimum(ceiling, jnp.maximum(floor_value, trial)))

    def region_sum(field):
        return jnp.sum(field, axis=(0, 1)).reshape(REGIONS, band_cells).sum(axis=1)

    levels = BISECT

    def bisect_round(round_index, bracket):
        low_end, high_end = bracket
        level_nodes = [(low_end, high_end)]
        midpoints = []
        for depth in range(levels):
            next_nodes = []
            for node_low, node_high in level_nodes:
                middle = jnp.sqrt(node_low * node_high)
                midpoints.append(middle)
                next_nodes.append((node_low, middle))
                next_nodes.append((middle, node_high))
            level_nodes = next_nodes
        trial_multipliers = jnp.stack(midpoints)
        per_cell = jnp.repeat(trial_multipliers, band_cells, axis=1)[:, None, None, :]
        trial = design[None] * jnp.sqrt(benefit[None] / per_cell)
        fields_of = jnp.where(
            passive[None] == 1, 1.0, jnp.minimum(ceiling[None], jnp.maximum(floor_value[None], trial))
        )
        partial_volumes = (
            jnp.sum(fields_of, axis=(1, 2)).reshape(len(midpoints), REGIONS, band_cells).sum(axis=2)
        )
        lanes = 128
        flat = partial_volumes.reshape(-1)
        spare = -flat.size % lanes
        dense = jnp.pad(flat, (0, spare)).reshape(-1, lanes)
        dense = butterfly_sum(butterfly_sum(dense, "gy"), "gx")
        volumes = dense.reshape(-1)[: flat.size].reshape(partial_volumes.shape)
        heavier_all = volumes > target[None, :]
        position = jnp.zeros((REGIONS,), jnp.int32)
        for depth in range(levels):
            middle = jnp.sqrt(low_end * high_end)
            nodes = lax.slice_in_dim(heavier_all, 2**depth - 1, 2 ** (depth + 1) - 1, axis=0)
            slots = lax.broadcasted_iota(jnp.int32, nodes.shape, 0)
            heavier = jnp.any(nodes & (slots == position[None, :]), axis=0)
            low_end = jnp.where(heavier, middle, low_end)
            high_end = jnp.where(heavier, high_end, middle)
            position = 2 * position + heavier.astype(jnp.int32)
        return (low_end, high_end)

    start = (jnp.full((REGIONS,), 0.0001, jnp.float32), jnp.full((REGIONS,), 10000.0, jnp.float32))
    low_end, high_end = bisect_round(0, start)
    design_next = candidate(jnp.sqrt(low_end * high_end))
    return (sensitivity, design_next)


def solution(mesh):
    placed = (
        P("gx", "gy", None),
        P("gx", "gy", None),
        P(None, None, None, "gx", "gy", None),
        P("gx", "gy", None),
        P(),
        P(),
        P(),
    )
    return jax.shard_map(
        shards,
        mesh=mesh,
        in_specs=placed,
        out_specs=(P("gx", "gy", None), P("gx", "gy", None)),
        check_vma=False,
    )
```

```python
import math

import jax
import jax.numpy as jnp
from jax import lax
from jax.sharding import PartitionSpec as P
from jax.experimental import pallas as pl
from jax.experimental.pallas import tpu as pltpu

BISECT = 6
REGIONS = 64


PENALTY_SCALE = 3.0 * (1.0 - 0.001)
OMEGA_SQUARED = 0.5
MOVE_LIMIT = 0.2


def with_halo(cells, sides, width):
    for axis, dim in sides:
        count = lax.axis_size(axis)
        ends = count - 1
        head = lax.slice_in_dim(cells, 0, width, axis=dim)
        tail = lax.slice_in_dim(cells, cells.shape[dim] - width, cells.shape[dim], axis=dim)
        cells = jnp.concatenate(
            [
                lax.ppermute(tail, axis, [(i, (i + 1) % count) for i in range(ends)]),
                cells,
                lax.ppermute(head, axis, [((i + 1) % count, i) for i in range(ends)]),
            ],
            axis=dim,
        )
    return cells


def front_exchange(cells, fields, width):
    for axis, dim in (("gx", 0), ("gy", 1)):
        count = lax.axis_size(axis)
        ends = count - 1
        field_dim = dim + 3
        head = lax.slice_in_dim(cells, 0, width, axis=dim)
        tail = lax.slice_in_dim(cells, cells.shape[dim] - width, cells.shape[dim], axis=dim)
        rim = lax.slice_in_dim(fields, 0, 1, axis=field_dim)
        lanes = cells.shape[-1]
        packed = jnp.concatenate([head.reshape(-1, lanes), rim.reshape(-1, lanes)], axis=0)
        packed = lax.ppermute(packed, axis, [((i + 1) % count, i) for i in range(ends)])
        split = head.size // lanes
        head = packed[:split].reshape(head.shape)
        rim = packed[split:].reshape(rim.shape)
        tail = lax.ppermute(tail, axis, [(i, (i + 1) % count) for i in range(ends)])
        cells = jnp.concatenate([tail, cells, head], axis=dim)
        fields = jnp.concatenate([fields, rim], axis=field_dim)
    return cells, fields


def from_behind(value, axis, steps):
    count = lax.axis_size(axis)
    initial, last = (max(0, -steps), min(count, count - steps))
    return lax.ppermute(value, axis, [(source, source + steps) for source in range(initial, last)])


def butterfly_sum(value, axis):
    count = lax.axis_size(axis)
    stride = 1
    while stride < count:
        value = value + lax.ppermute(value, axis, [(i, i ^ stride) for i in range(count)])
        stride *= 2
    return value


def filter_taps():
    tap_list = []
    for offset_x in range(-2, 3):
        for offset_y in range(-2, 3):
            for offset_z in range(-2, 3):
                weight = 3.0 - math.sqrt(
                    offset_x * offset_x + offset_y * offset_y + offset_z * offset_z
                )
                if weight > 0.0:
                    tap_list.append((offset_x, offset_y, offset_z, weight))
    return tap_list


def stencil(padded, block_shape):
    result = jnp.zeros(block_shape, jnp.float32)
    for offset_x, offset_y, offset_z, weight in filter_taps():
        result = (
            result
            + weight
            * padded[
                2 + offset_x : 2 + offset_x + block_shape[0],
                2 + offset_y : 2 + offset_y + block_shape[1],
                2 + offset_z : 2 + offset_z + block_shape[2],
            ]
        )
    return result


def element_terms(extended, stiffness, mass_matrix):
    pair_count = extended.shape[0]
    cells_x = extended.shape[3] - 1
    cells_y = extended.shape[4] - 1
    cells_z = extended.shape[5] - 1
    stiff_energy = jnp.zeros((cells_x * cells_y * cells_z,), jnp.float32)
    mass_energy = jnp.zeros((cells_x * cells_y * cells_z,), jnp.float32)
    for pair_index in range(pair_count):
        vectors = []
        for member in range(2):
            row_list = []
            for corner_x in (0, 1):
                for corner_y in (0, 1):
                    for corner_z in (0, 1):
                        for component in range(3):
                            row_list.append(
                                extended[
                                    pair_index,
                                    member,
                                    component,
                                    corner_x : corner_x + cells_x,
                                    corner_y : corner_y + cells_y,
                                    corner_z : corner_z + cells_z,
                                ].reshape(-1)
                            )
            vectors.append(jnp.stack(row_list))
        state_rows, adjoint_rows = vectors
        stiff_energy = stiff_energy + jnp.sum(
            state_rows * jnp.dot(stiffness, adjoint_rows, precision=lax.Precision.HIGHEST), axis=0
        )
        mass_energy = mass_energy + jnp.sum(
            state_rows * jnp.dot(mass_matrix, adjoint_rows, precision=lax.Precision.HIGHEST), axis=0
        )
    return (
        stiff_energy.reshape(cells_x, cells_y, cells_z),
        mass_energy.reshape(cells_x, cells_y, cells_z),
    )


CORNERS = [(a, b, d) for a in (0, 1) for b in (0, 1) for d in (0, 1)]


def energy_kernel(extended_ref, stiffness_ref, mass_ref, stiff_out, mass_out):
    pair_count = extended_ref.shape[0]
    cells_x, cells_y, cells_z = stiff_out.shape
    lane = lax.broadcasted_iota(jnp.int32, (cells_y, cells_z), 1)
    inside = lane < cells_z - 1

    def node_view(pair, member, component, x, corner):
        corner_x, corner_y, corner_z = corner
        value = extended_ref[pair, member, component, x + corner_x, pl.ds(corner_y, cells_y), :]
        if corner_z:
            value = jnp.where(inside, pltpu.roll(value, cells_z - 1, 1), 0.0)
        return value

    def over_pairs(pair, energies):
        stiff_sum, mass_sum, x = energies
        adjoint = [
            node_view(pair, 1, component, x, corner) for corner in CORNERS for component in range(3)
        ]
        for row in range(len(adjoint)):
            state = node_view(pair, 0, row % 3, x, CORNERS[row // 3])
            stiff_row = stiffness_ref[row, 0] * adjoint[0]
            mass_row = mass_ref[row, 0] * adjoint[0]
            for column in range(1, len(adjoint)):
                stiff_row = stiff_row + stiffness_ref[row, column] * adjoint[column]
                mass_row = mass_row + mass_ref[row, column] * adjoint[column]
            stiff_sum = stiff_sum + state * stiff_row
            mass_sum = mass_sum + state * mass_row
        return stiff_sum, mass_sum, x

    def over_x(x, carry):
        zero = jnp.zeros((cells_y, cells_z), jnp.float32)
        stiff_sum, mass_sum, _ = lax.fori_loop(0, pair_count, over_pairs, (zero, zero, x))
        stiff_out[x] = stiff_sum
        mass_out[x] = mass_sum
        return carry

    lax.fori_loop(0, cells_x, over_x, 0)


def mxu_energy_kernel(
    extended_ref, stiffness_ref, mass_ref, stiff_out, mass_out, coupling_ref, adjoint_rows, products
):
    pair_count = extended_ref.shape[0]
    cells_x, cells_y, cells_z = stiff_out.shape
    dofs = 3 * len(CORNERS)
    wide = dofs * cells_y
    spread_rows = (
        lax.broadcasted_iota(jnp.int32, (wide, dofs), 0) // cells_y
        == lax.broadcasted_iota(jnp.int32, (wide, dofs), 1)
    ).astype(jnp.float32)
    spread_columns = (
        lax.broadcasted_iota(jnp.int32, (dofs, wide), 0)
        == lax.broadcasted_iota(jnp.int32, (dofs, wide), 1) // cells_y
    ).astype(jnp.float32)
    same_y = (
        lax.broadcasted_iota(jnp.int32, (wide, wide), 0) % cells_y
        == lax.broadcasted_iota(jnp.int32, (wide, wide), 1) % cells_y
    )
    for block, matrix_ref in enumerate((stiffness_ref, mass_ref)):
        spread = jnp.dot(
            matrix_ref[...], spread_columns, precision=lax.Precision.HIGHEST,
            preferred_element_type=jnp.float32,
        )
        spread = jnp.dot(
            spread_rows, spread, precision=lax.Precision.HIGHEST, preferred_element_type=jnp.float32
        )
        coupling_ref[pl.ds(block * wide, wide), :] = jnp.where(same_y, spread, 0.0)
    lane = lax.broadcasted_iota(jnp.int32, (cells_y, cells_z), 1)
    inside = lane < cells_z - 1
    stiff_out[...] = jnp.zeros(stiff_out.shape, jnp.float32)
    mass_out[...] = jnp.zeros(mass_out.shape, jnp.float32)

    def node_view(pair, member, row, x):
        corner_x, corner_y, corner_z = CORNERS[row // 3]
        value = extended_ref[pair, member, row % 3, x + corner_x, pl.ds(corner_y, cells_y), :]
        if corner_z:
            value = jnp.where(inside, pltpu.roll(value, cells_z - 1, 1), 0.0)
        return value

    def over_pairs(pair, carry):
        def gather_x(x, inner):
            columns = pl.ds(pl.multiple_of(x * cells_z, cells_z), cells_z)
            for row in range(dofs):
                adjoint_rows[pl.ds(row * cells_y, cells_y), columns] = node_view(pair, 1, row, x)
            return inner

        lax.fori_loop(0, cells_x, gather_x, 0)
        products[...] = jnp.dot(
            coupling_ref[...],
            adjoint_rows[...],
            precision=lax.Precision.HIGH,
            preferred_element_type=jnp.float32,
        )

        def reduce_x(x, inner):
            columns = pl.ds(pl.multiple_of(x * cells_z, cells_z), cells_z)
            stiff_sum = stiff_out[x]
            mass_sum = mass_out[x]
            for row in range(dofs):
                state = node_view(pair, 0, row, x)
                stiff_sum = stiff_sum + state * products[pl.ds(row * cells_y, cells_y), columns]
                mass_sum = mass_sum + state * products[pl.ds((dofs + row) * cells_y, cells_y), columns]
            stiff_out[x] = stiff_sum
            mass_out[x] = mass_sum
            return inner

        lax.fori_loop(0, cells_x, reduce_x, 0)
        return carry

    lax.fori_loop(0, pair_count, over_pairs, 0)


def element_energies(extended, stiffness, mass_matrix):
    pair_count = extended.shape[0]
    cells = (extended.shape[3] - 1, extended.shape[4] - 1, extended.shape[5])
    voxels = cells[0] * cells[1] * cells[2]
    dofs = stiffness.shape[0]
    vmem = pl.BlockSpec(memory_space=pltpu.VMEM)
    return pl.pallas_call(
        mxu_energy_kernel,
        out_shape=(
            jax.ShapeDtypeStruct(cells, jnp.float32),
            jax.ShapeDtypeStruct(cells, jnp.float32),
        ),
        in_specs=[vmem, vmem, vmem],
        out_specs=(vmem, vmem),
        scratch_shapes=[
            pltpu.VMEM((2 * dofs * cells[1], dofs * cells[1]), jnp.float32),
            pltpu.VMEM((dofs * cells[1], cells[0] * cells[2]), jnp.float32),
            pltpu.VMEM((2 * dofs * cells[1], cells[0] * cells[2]), jnp.float32),
        ],
        cost_estimate=pl.CostEstimate(
            flops=pair_count * (4 * (dofs * cells[1]) ** 2 * cells[0] * cells[2] + 4 * dofs * voxels),
            bytes_accessed=extended.size * 4 + 2 * stiffness.size * 4 + 2 * voxels * 4,
            transcendentals=0,
        ),
    )(extended, stiffness, mass_matrix)


def shards(design, passive, basis_pairs, supports, stiffness, mass_matrix, volume_fraction):
    block_shape = design.shape
    size_x, size_y, size_z = block_shape
    devices_x = lax.axis_size("gx")
    devices_y = lax.axis_size("gy")
    index_x = lax.axis_index("gx")
    index_y = lax.axis_index("gy")
    grid_x = size_x * devices_x
    grid_y = size_y * devices_y
    spread_x = jnp.arange(size_x + 4, dtype=jnp.int32) + index_x * size_x - 2
    spread_y = jnp.arange(size_y + 4, dtype=jnp.int32) + index_y * size_y - 2
    valid_x = ((spread_x >= 0) & (spread_x < grid_x)).astype(jnp.float32)
    valid_y = ((spread_y >= 0) & (spread_y < grid_y)).astype(jnp.float32)
    valid_z = jnp.pad(jnp.ones((size_z,), jnp.float32), 2)
    inside = valid_x[:, None, None] * valid_y[None, :, None] * valid_z[None, None, :]
    weight_sum = stencil(inside, block_shape)
    fields = basis_pairs * (1 - supports).astype(jnp.float32)
    design_wide, extended = front_exchange(design, fields, 2)
    design_wide = jnp.pad(design_wide, ((0, 0), (0, 0), (2, 2)))
    physical = jnp.where(passive == 1, 1.0, stencil(design_wide, block_shape) / weight_sum)
    stiff_energy, mass_energy = element_energies(extended, stiffness, mass_matrix)
    raw_sensitivity = -(
        PENALTY_SCALE * physical * physical * stiff_energy - OMEGA_SQUARED * mass_energy
    )
    raw_sensitivity = jnp.where(passive == 1, 0.0, raw_sensitivity)
    scaled_wide = with_halo(raw_sensitivity / weight_sum, (("gx", 0), ("gy", 1)), 2)
    scaled_wide = jnp.pad(scaled_wide, ((0, 0), (0, 0), (2, 2)))
    sensitivity = stencil(scaled_wide, block_shape)
    benefit = jnp.maximum(-sensitivity, 0.0)
    floor_value = jnp.maximum(design - MOVE_LIMIT, 0.0)
    ceiling = jnp.minimum(design + MOVE_LIMIT, 1.0)
    band_cells = size_z // REGIONS
    target = volume_fraction * float(grid_x * grid_y * band_cells)

    def candidate(multiplier):
        per_cell = jnp.repeat(multiplier, band_cells)[None, None, :]
        trial = design * jnp.sqrt(benefit / per_cell)
        return jnp.where(passive == 1, 1.0, jnp.minimum(ceiling, jnp.maximum(floor_value, trial)))

    def region_sum(field):
        return jnp.sum(field, axis=(0, 1)).reshape(REGIONS, band_cells).sum(axis=1)

    levels = BISECT

    def bisect_round(round_index, bracket):
        low_end, high_end = bracket
        level_nodes = [(low_end, high_end)]
        midpoints = []
        for depth in range(levels):
            next_nodes = []
            for node_low, node_high in level_nodes:
                middle = jnp.sqrt(node_low * node_high)
                midpoints.append(middle)
                next_nodes.append((node_low, middle))
                next_nodes.append((middle, node_high))
            level_nodes = next_nodes
        trial_multipliers = jnp.stack(midpoints)
        per_cell = jnp.repeat(trial_multipliers, band_cells, axis=1)[:, None, None, :]
        trial = design[None] * jnp.sqrt(benefit[None] / per_cell)
        fields_of = jnp.where(
            passive[None] == 1, 1.0, jnp.minimum(ceiling[None], jnp.maximum(floor_value[None], trial))
        )
        partial_volumes = (
            jnp.sum(fields_of, axis=(1, 2)).reshape(len(midpoints), REGIONS, band_cells).sum(axis=2)
        )
        lanes = 128
        flat = partial_volumes.reshape(-1)
        spare = -flat.size % lanes
        dense = jnp.pad(flat, (0, spare)).reshape(-1, lanes)
        dense = butterfly_sum(butterfly_sum(dense, "gy"), "gx")
        volumes = dense.reshape(-1)[: flat.size].reshape(partial_volumes.shape)
        heavier_all = volumes > target[None, :]
        position = jnp.zeros((REGIONS,), jnp.int32)
        for depth in range(levels):
            middle = jnp.sqrt(low_end * high_end)
            nodes = lax.slice_in_dim(heavier_all, 2**depth - 1, 2 ** (depth + 1) - 1, axis=0)
            slots = lax.broadcasted_iota(jnp.int32, nodes.shape, 0)
            heavier = jnp.any(nodes & (slots == position[None, :]), axis=0)
            low_end = jnp.where(heavier, middle, low_end)
            high_end = jnp.where(heavier, high_end, middle)
            position = 2 * position + heavier.astype(jnp.int32)
        return (low_end, high_end)

    start = (jnp.full((REGIONS,), 0.0001, jnp.float32), jnp.full((REGIONS,), 10000.0, jnp.float32))
    low_end, high_end = bisect_round(0, start)
    design_next = candidate(jnp.sqrt(low_end * high_end))
    return (sensitivity, design_next)


def solution(mesh):
    placed = (
        P("gx", "gy", None),
        P("gx", "gy", None),
        P(None, None, None, "gx", "gy", None),
        P("gx", "gy", None),
        P(),
        P(),
        P(),
    )
    return jax.shard_map(
        shards,
        mesh=mesh,
        in_specs=placed,
        out_specs=(P("gx", "gy", None), P("gx", "gy", None)),
        check_vma=False,
    )
```

```python
import math

import jax
import jax.numpy as jnp
from jax import lax
from jax.sharding import PartitionSpec as P
from jax.experimental import pallas as pl
from jax.experimental.pallas import tpu as pltpu

BISECT = 6
REGIONS = 64


PENALTY_SCALE = 3.0 * (1.0 - 0.001)
OMEGA_SQUARED = 0.5
MOVE_LIMIT = 0.2


def with_halo(cells, sides, width):
    for axis, dim in sides:
        count = lax.axis_size(axis)
        ends = count - 1
        head = lax.slice_in_dim(cells, 0, width, axis=dim)
        tail = lax.slice_in_dim(cells, cells.shape[dim] - width, cells.shape[dim], axis=dim)
        cells = jnp.concatenate(
            [
                lax.ppermute(tail, axis, [(i, (i + 1) % count) for i in range(ends)]),
                cells,
                lax.ppermute(head, axis, [((i + 1) % count, i) for i in range(ends)]),
            ],
            axis=dim,
        )
    return cells


def front_exchange(cells, fields, width):
    for axis, dim in (("gx", 0), ("gy", 1)):
        count = lax.axis_size(axis)
        ends = count - 1
        field_dim = dim + 3
        head = lax.slice_in_dim(cells, 0, width, axis=dim)
        tail = lax.slice_in_dim(cells, cells.shape[dim] - width, cells.shape[dim], axis=dim)
        rim = lax.slice_in_dim(fields, 0, 1, axis=field_dim)
        lanes = cells.shape[-1]
        packed = jnp.concatenate([head.reshape(-1, lanes), rim.reshape(-1, lanes)], axis=0)
        packed = lax.ppermute(packed, axis, [((i + 1) % count, i) for i in range(ends)])
        split = head.size // lanes
        head = packed[:split].reshape(head.shape)
        rim = packed[split:].reshape(rim.shape)
        tail = lax.ppermute(tail, axis, [(i, (i + 1) % count) for i in range(ends)])
        cells = jnp.concatenate([tail, cells, head], axis=dim)
        fields = jnp.concatenate([fields, rim], axis=field_dim)
    return cells, fields


def from_behind(value, axis, steps):
    count = lax.axis_size(axis)
    initial, last = (max(0, -steps), min(count, count - steps))
    return lax.ppermute(value, axis, [(source, source + steps) for source in range(initial, last)])


def butterfly_sum(value, axis):
    count = lax.axis_size(axis)
    stride = 1
    while stride < count:
        value = value + lax.ppermute(value, axis, [(i, i ^ stride) for i in range(count)])
        stride *= 2
    return value


def filter_taps():
    tap_list = []
    for offset_x in range(-2, 3):
        for offset_y in range(-2, 3):
            for offset_z in range(-2, 3):
                weight = 3.0 - math.sqrt(
                    offset_x * offset_x + offset_y * offset_y + offset_z * offset_z
                )
                if weight > 0.0:
                    tap_list.append((offset_x, offset_y, offset_z, weight))
    return tap_list


def stencil(padded, block_shape):
    result = jnp.zeros(block_shape, jnp.float32)
    for offset_x, offset_y, offset_z, weight in filter_taps():
        result = (
            result
            + weight
            * padded[
                2 + offset_x : 2 + offset_x + block_shape[0],
                2 + offset_y : 2 + offset_y + block_shape[1],
                2 + offset_z : 2 + offset_z + block_shape[2],
            ]
        )
    return result


def element_terms(extended, stiffness, mass_matrix):
    pair_count = extended.shape[0]
    cells_x = extended.shape[3] - 1
    cells_y = extended.shape[4] - 1
    cells_z = extended.shape[5] - 1
    stiff_energy = jnp.zeros((cells_x * cells_y * cells_z,), jnp.float32)
    mass_energy = jnp.zeros((cells_x * cells_y * cells_z,), jnp.float32)
    for pair_index in range(pair_count):
        vectors = []
        for member in range(2):
            row_list = []
            for corner_x in (0, 1):
                for corner_y in (0, 1):
                    for corner_z in (0, 1):
                        for component in range(3):
                            row_list.append(
                                extended[
                                    pair_index,
                                    member,
                                    component,
                                    corner_x : corner_x + cells_x,
                                    corner_y : corner_y + cells_y,
                                    corner_z : corner_z + cells_z,
                                ].reshape(-1)
                            )
            vectors.append(jnp.stack(row_list))
        state_rows, adjoint_rows = vectors
        stiff_energy = stiff_energy + jnp.sum(
            state_rows * jnp.dot(stiffness, adjoint_rows, precision=lax.Precision.HIGHEST), axis=0
        )
        mass_energy = mass_energy + jnp.sum(
            state_rows * jnp.dot(mass_matrix, adjoint_rows, precision=lax.Precision.HIGHEST), axis=0
        )
    return (
        stiff_energy.reshape(cells_x, cells_y, cells_z),
        mass_energy.reshape(cells_x, cells_y, cells_z),
    )


CORNERS = [(a, b, d) for a in (0, 1) for b in (0, 1) for d in (0, 1)]


def energy_kernel(extended_ref, stiffness_ref, mass_ref, stiff_out, mass_out):
    pair_count = extended_ref.shape[0]
    cells_x, cells_y, cells_z = stiff_out.shape
    lane = lax.broadcasted_iota(jnp.int32, (cells_y, cells_z), 1)
    inside = lane < cells_z - 1

    def node_view(pair, member, component, x, corner):
        corner_x, corner_y, corner_z = corner
        value = extended_ref[pair, member, component, x + corner_x, pl.ds(corner_y, cells_y), :]
        if corner_z:
            value = jnp.where(inside, pltpu.roll(value, cells_z - 1, 1), 0.0)
        return value

    def over_pairs(pair, energies):
        stiff_sum, mass_sum, x = energies
        adjoint = [
            node_view(pair, 1, component, x, corner) for corner in CORNERS for component in range(3)
        ]
        for row in range(len(adjoint)):
            state = node_view(pair, 0, row % 3, x, CORNERS[row // 3])
            stiff_row = stiffness_ref[row, 0] * adjoint[0]
            mass_row = mass_ref[row, 0] * adjoint[0]
            for column in range(1, len(adjoint)):
                stiff_row = stiff_row + stiffness_ref[row, column] * adjoint[column]
                mass_row = mass_row + mass_ref[row, column] * adjoint[column]
            stiff_sum = stiff_sum + state * stiff_row
            mass_sum = mass_sum + state * mass_row
        return stiff_sum, mass_sum, x

    def over_x(x, carry):
        zero = jnp.zeros((cells_y, cells_z), jnp.float32)
        stiff_sum, mass_sum, _ = lax.fori_loop(0, pair_count, over_pairs, (zero, zero, x))
        stiff_out[x] = stiff_sum
        mass_out[x] = mass_sum
        return carry

    lax.fori_loop(0, cells_x, over_x, 0)


def mxu_energy_kernel(
    extended_ref, stiffness_ref, mass_ref, stiff_out, mass_out, coupling_ref, state_rows,
    adjoint_rows, products,
):
    pair_count = extended_ref.shape[0]
    cells_x, cells_y, cells_z = stiff_out.shape
    dofs = 3 * len(CORNERS)
    wide = dofs * cells_y
    spread_rows = (
        lax.broadcasted_iota(jnp.int32, (wide, dofs), 0) // cells_y
        == lax.broadcasted_iota(jnp.int32, (wide, dofs), 1)
    ).astype(jnp.float32)
    spread_columns = (
        lax.broadcasted_iota(jnp.int32, (dofs, wide), 0)
        == lax.broadcasted_iota(jnp.int32, (dofs, wide), 1) // cells_y
    ).astype(jnp.float32)
    same_y = (
        lax.broadcasted_iota(jnp.int32, (wide, wide), 0) % cells_y
        == lax.broadcasted_iota(jnp.int32, (wide, wide), 1) % cells_y
    )
    for block, matrix_ref in enumerate((stiffness_ref, mass_ref)):
        spread = jnp.dot(
            matrix_ref[...], spread_columns, precision=lax.Precision.HIGHEST,
            preferred_element_type=jnp.float32,
        )
        spread = jnp.dot(
            spread_rows, spread, precision=lax.Precision.HIGHEST, preferred_element_type=jnp.float32
        )
        coupling_ref[pl.ds(block * wide, wide), :] = jnp.where(same_y, spread, 0.0)
    lane = lax.broadcasted_iota(jnp.int32, (cells_y, cells_z), 1)
    inside = lane < cells_z - 1
    stiff_out[...] = jnp.zeros(stiff_out.shape, jnp.float32)
    mass_out[...] = jnp.zeros(mass_out.shape, jnp.float32)
    member_rows = (state_rows, adjoint_rows)

    def over_pairs(pair, carry):
        for node_x in range(cells_x + 1):
            for member in range(2):
                for component in range(3):
                    for corner_y in (0, 1):
                        base = extended_ref[
                            pair, member, component, node_x, pl.ds(corner_y, cells_y), :
                        ]
                        for corner_z in (0, 1):
                            value = base
                            if corner_z:
                                value = jnp.where(inside, pltpu.roll(base, cells_z - 1, 1), 0.0)
                            for corner_x in (0, 1):
                                x = node_x - corner_x
                                if 0 <= x < cells_x:
                                    corner = CORNERS.index((corner_x, corner_y, corner_z))
                                    row = 3 * corner + component
                                    member_rows[member][
                                        pl.ds(row * cells_y, cells_y), pl.ds(x * cells_z, cells_z)
                                    ] = value
        products[...] = jnp.dot(
            coupling_ref[...],
            adjoint_rows[...],
            precision=lax.Precision.HIGH,
            preferred_element_type=jnp.float32,
        )
        state = state_rows[...].reshape(dofs, cells_y, cells_x * cells_z)
        stiff_sum = jnp.sum(
            state * products[pl.ds(0, wide), :].reshape(dofs, cells_y, cells_x * cells_z), axis=0
        )
        mass_sum = jnp.sum(
            state * products[pl.ds(wide, wide), :].reshape(dofs, cells_y, cells_x * cells_z), axis=0
        )
        for x in range(cells_x):
            columns = slice(x * cells_z, (x + 1) * cells_z)
            stiff_out[x] = stiff_out[x] + stiff_sum[:, columns]
            mass_out[x] = mass_out[x] + mass_sum[:, columns]
        return carry

    lax.fori_loop(0, pair_count, over_pairs, 0)


def element_energies(extended, stiffness, mass_matrix):
    pair_count = extended.shape[0]
    cells = (extended.shape[3] - 1, extended.shape[4] - 1, extended.shape[5])
    voxels = cells[0] * cells[1] * cells[2]
    dofs = stiffness.shape[0]
    vmem = pl.BlockSpec(memory_space=pltpu.VMEM)
    return pl.pallas_call(
        mxu_energy_kernel,
        out_shape=(
            jax.ShapeDtypeStruct(cells, jnp.float32),
            jax.ShapeDtypeStruct(cells, jnp.float32),
        ),
        in_specs=[vmem, vmem, vmem],
        out_specs=(vmem, vmem),
        scratch_shapes=[
            pltpu.VMEM((2 * dofs * cells[1], dofs * cells[1]), jnp.float32),
            pltpu.VMEM((dofs * cells[1], cells[0] * cells[2]), jnp.float32),
            pltpu.VMEM((dofs * cells[1], cells[0] * cells[2]), jnp.float32),
            pltpu.VMEM((2 * dofs * cells[1], cells[0] * cells[2]), jnp.float32),
        ],
        cost_estimate=pl.CostEstimate(
            flops=pair_count * (4 * (dofs * cells[1]) ** 2 * cells[0] * cells[2] + 4 * dofs * voxels),
            bytes_accessed=extended.size * 4 + 2 * stiffness.size * 4 + 2 * voxels * 4,
            transcendentals=0,
        ),
    )(extended, stiffness, mass_matrix)


def shards(design, passive, basis_pairs, supports, stiffness, mass_matrix, volume_fraction):
    block_shape = design.shape
    size_x, size_y, size_z = block_shape
    devices_x = lax.axis_size("gx")
    devices_y = lax.axis_size("gy")
    index_x = lax.axis_index("gx")
    index_y = lax.axis_index("gy")
    grid_x = size_x * devices_x
    grid_y = size_y * devices_y
    spread_x = jnp.arange(size_x + 4, dtype=jnp.int32) + index_x * size_x - 2
    spread_y = jnp.arange(size_y + 4, dtype=jnp.int32) + index_y * size_y - 2
    valid_x = ((spread_x >= 0) & (spread_x < grid_x)).astype(jnp.float32)
    valid_y = ((spread_y >= 0) & (spread_y < grid_y)).astype(jnp.float32)
    valid_z = jnp.pad(jnp.ones((size_z,), jnp.float32), 2)
    inside = valid_x[:, None, None] * valid_y[None, :, None] * valid_z[None, None, :]
    weight_sum = stencil(inside, block_shape)
    fields = basis_pairs * (1 - supports).astype(jnp.float32)
    design_wide, extended = front_exchange(design, fields, 2)
    design_wide = jnp.pad(design_wide, ((0, 0), (0, 0), (2, 2)))
    physical = jnp.where(passive == 1, 1.0, stencil(design_wide, block_shape) / weight_sum)
    stiff_energy, mass_energy = element_energies(extended, stiffness, mass_matrix)
    raw_sensitivity = -(
        PENALTY_SCALE * physical * physical * stiff_energy - OMEGA_SQUARED * mass_energy
    )
    raw_sensitivity = jnp.where(passive == 1, 0.0, raw_sensitivity)
    scaled_wide = with_halo(raw_sensitivity / weight_sum, (("gx", 0), ("gy", 1)), 2)
    scaled_wide = jnp.pad(scaled_wide, ((0, 0), (0, 0), (2, 2)))
    sensitivity = stencil(scaled_wide, block_shape)
    benefit = jnp.maximum(-sensitivity, 0.0)
    floor_value = jnp.maximum(design - MOVE_LIMIT, 0.0)
    ceiling = jnp.minimum(design + MOVE_LIMIT, 1.0)
    band_cells = size_z // REGIONS
    target = volume_fraction * float(grid_x * grid_y * band_cells)

    def candidate(multiplier):
        per_cell = jnp.repeat(multiplier, band_cells)[None, None, :]
        trial = design * jnp.sqrt(benefit / per_cell)
        return jnp.where(passive == 1, 1.0, jnp.minimum(ceiling, jnp.maximum(floor_value, trial)))

    def region_sum(field):
        return jnp.sum(field, axis=(0, 1)).reshape(REGIONS, band_cells).sum(axis=1)

    levels = BISECT

    def bisect_round(round_index, bracket):
        low_end, high_end = bracket
        level_nodes = [(low_end, high_end)]
        midpoints = []
        for depth in range(levels):
            next_nodes = []
            for node_low, node_high in level_nodes:
                middle = jnp.sqrt(node_low * node_high)
                midpoints.append(middle)
                next_nodes.append((node_low, middle))
                next_nodes.append((middle, node_high))
            level_nodes = next_nodes
        trial_multipliers = jnp.stack(midpoints)
        per_cell = jnp.repeat(trial_multipliers, band_cells, axis=1)[:, None, None, :]
        trial = design[None] * jnp.sqrt(benefit[None] / per_cell)
        fields_of = jnp.where(
            passive[None] == 1, 1.0, jnp.minimum(ceiling[None], jnp.maximum(floor_value[None], trial))
        )
        partial_volumes = (
            jnp.sum(fields_of, axis=(1, 2)).reshape(len(midpoints), REGIONS, band_cells).sum(axis=2)
        )
        lanes = 128
        flat = partial_volumes.reshape(-1)
        spare = -flat.size % lanes
        dense = jnp.pad(flat, (0, spare)).reshape(-1, lanes)
        dense = butterfly_sum(butterfly_sum(dense, "gy"), "gx")
        volumes = dense.reshape(-1)[: flat.size].reshape(partial_volumes.shape)
        heavier_all = volumes > target[None, :]
        position = jnp.zeros((REGIONS,), jnp.int32)
        for depth in range(levels):
            middle = jnp.sqrt(low_end * high_end)
            nodes = lax.slice_in_dim(heavier_all, 2**depth - 1, 2 ** (depth + 1) - 1, axis=0)
            slots = lax.broadcasted_iota(jnp.int32, nodes.shape, 0)
            heavier = jnp.any(nodes & (slots == position[None, :]), axis=0)
            low_end = jnp.where(heavier, middle, low_end)
            high_end = jnp.where(heavier, high_end, middle)
            position = 2 * position + heavier.astype(jnp.int32)
        return (low_end, high_end)

    start = (jnp.full((REGIONS,), 0.0001, jnp.float32), jnp.full((REGIONS,), 10000.0, jnp.float32))
    low_end, high_end = bisect_round(0, start)
    design_next = candidate(jnp.sqrt(low_end * high_end))
    return (sensitivity, design_next)


def solution(mesh):
    placed = (
        P("gx", "gy", None),
        P("gx", "gy", None),
        P(None, None, None, "gx", "gy", None),
        P("gx", "gy", None),
        P(),
        P(),
        P(),
    )
    return jax.shard_map(
        shards,
        mesh=mesh,
        in_specs=placed,
        out_specs=(P("gx", "gy", None), P("gx", "gy", None)),
        check_vma=False,
    )
```

```python
import math

import jax
import jax.numpy as jnp
from jax import lax
from jax.sharding import PartitionSpec as P
from jax.experimental import pallas as pl
from jax.experimental.pallas import tpu as pltpu

BISECT = 6
REGIONS = 64


PENALTY_SCALE = 3.0 * (1.0 - 0.001)
OMEGA_SQUARED = 0.5
MOVE_LIMIT = 0.2


def with_halo(cells, sides, width):
    for axis, dim in sides:
        count = lax.axis_size(axis)
        ends = count - 1
        head = lax.slice_in_dim(cells, 0, width, axis=dim)
        tail = lax.slice_in_dim(cells, cells.shape[dim] - width, cells.shape[dim], axis=dim)
        cells = jnp.concatenate(
            [
                lax.ppermute(tail, axis, [(i, (i + 1) % count) for i in range(ends)]),
                cells,
                lax.ppermute(head, axis, [((i + 1) % count, i) for i in range(ends)]),
            ],
            axis=dim,
        )
    return cells


def front_exchange(cells, basis_pairs, supports, width):
    open_nodes = (1 - supports).astype(jnp.float32)
    rim = basis_pairs[:, :, :, :1] * open_nodes[:1]
    rims = []
    for axis, dim in (("gx", 0), ("gy", 1)):
        count = lax.axis_size(axis)
        ends = count - 1
        head = lax.slice_in_dim(cells, 0, width, axis=dim)
        tail = lax.slice_in_dim(cells, cells.shape[dim] - width, cells.shape[dim], axis=dim)
        lanes = cells.shape[-1]
        packed = jnp.concatenate([head.reshape(-1, lanes), rim.reshape(-1, lanes)], axis=0)
        packed = lax.ppermute(packed, axis, [((i + 1) % count, i) for i in range(ends)])
        split = head.size // lanes
        head = packed[:split].reshape(head.shape)
        received = packed[split:].reshape(rim.shape)
        tail = lax.ppermute(tail, axis, [(i, (i + 1) % count) for i in range(ends)])
        cells = jnp.concatenate([tail, cells, head], axis=dim)
        rims.append(received)
        if axis == "gx":
            rim = jnp.concatenate(
                [basis_pairs[:, :, :, :, :1] * open_nodes[:, :1], received[:, :, :, :, :1]], axis=3
            )
    return cells, rims


def from_behind(value, axis, steps):
    count = lax.axis_size(axis)
    initial, last = (max(0, -steps), min(count, count - steps))
    return lax.ppermute(value, axis, [(source, source + steps) for source in range(initial, last)])


def butterfly_sum(value, axis):
    count = lax.axis_size(axis)
    stride = 1
    while stride < count:
        value = value + lax.ppermute(value, axis, [(i, i ^ stride) for i in range(count)])
        stride *= 2
    return value


def filter_taps():
    tap_list = []
    for offset_x in range(-2, 3):
        for offset_y in range(-2, 3):
            for offset_z in range(-2, 3):
                weight = 3.0 - math.sqrt(
                    offset_x * offset_x + offset_y * offset_y + offset_z * offset_z
                )
                if weight > 0.0:
                    tap_list.append((offset_x, offset_y, offset_z, weight))
    return tap_list


def stencil(padded, block_shape):
    result = jnp.zeros(block_shape, jnp.float32)
    for offset_x, offset_y, offset_z, weight in filter_taps():
        result = (
            result
            + weight
            * padded[
                2 + offset_x : 2 + offset_x + block_shape[0],
                2 + offset_y : 2 + offset_y + block_shape[1],
                2 + offset_z : 2 + offset_z + block_shape[2],
            ]
        )
    return result


def element_terms(extended, stiffness, mass_matrix):
    pair_count = extended.shape[0]
    cells_x = extended.shape[3] - 1
    cells_y = extended.shape[4] - 1
    cells_z = extended.shape[5] - 1
    stiff_energy = jnp.zeros((cells_x * cells_y * cells_z,), jnp.float32)
    mass_energy = jnp.zeros((cells_x * cells_y * cells_z,), jnp.float32)
    for pair_index in range(pair_count):
        vectors = []
        for member in range(2):
            row_list = []
            for corner_x in (0, 1):
                for corner_y in (0, 1):
                    for corner_z in (0, 1):
                        for component in range(3):
                            row_list.append(
                                extended[
                                    pair_index,
                                    member,
                                    component,
                                    corner_x : corner_x + cells_x,
                                    corner_y : corner_y + cells_y,
                                    corner_z : corner_z + cells_z,
                                ].reshape(-1)
                            )
            vectors.append(jnp.stack(row_list))
        state_rows, adjoint_rows = vectors
        stiff_energy = stiff_energy + jnp.sum(
            state_rows * jnp.dot(stiffness, adjoint_rows, precision=lax.Precision.HIGHEST), axis=0
        )
        mass_energy = mass_energy + jnp.sum(
            state_rows * jnp.dot(mass_matrix, adjoint_rows, precision=lax.Precision.HIGHEST), axis=0
        )
    return (
        stiff_energy.reshape(cells_x, cells_y, cells_z),
        mass_energy.reshape(cells_x, cells_y, cells_z),
    )


CORNERS = [(a, b, d) for a in (0, 1) for b in (0, 1) for d in (0, 1)]


def energy_kernel(extended_ref, stiffness_ref, mass_ref, stiff_out, mass_out):
    pair_count = extended_ref.shape[0]
    cells_x, cells_y, cells_z = stiff_out.shape
    lane = lax.broadcasted_iota(jnp.int32, (cells_y, cells_z), 1)
    inside = lane < cells_z - 1
    last_row = lax.broadcasted_iota(jnp.int32, (cells_y, cells_z), 0) == cells_y - 1

    def node_view(pair, member, component, x, corner):
        corner_x, corner_y, corner_z = corner
        value = extended_ref[pair, member, component, x + corner_x, pl.ds(corner_y, cells_y), :]
        if corner_z:
            value = jnp.where(inside, pltpu.roll(value, cells_z - 1, 1), 0.0)
        return value

    def over_pairs(pair, energies):
        stiff_sum, mass_sum, x = energies
        adjoint = [
            node_view(pair, 1, component, x, corner) for corner in CORNERS for component in range(3)
        ]
        for row in range(len(adjoint)):
            state = node_view(pair, 0, row % 3, x, CORNERS[row // 3])
            stiff_row = stiffness_ref[row, 0] * adjoint[0]
            mass_row = mass_ref[row, 0] * adjoint[0]
            for column in range(1, len(adjoint)):
                stiff_row = stiff_row + stiffness_ref[row, column] * adjoint[column]
                mass_row = mass_row + mass_ref[row, column] * adjoint[column]
            stiff_sum = stiff_sum + state * stiff_row
            mass_sum = mass_sum + state * mass_row
        return stiff_sum, mass_sum, x

    def over_x(x, carry):
        zero = jnp.zeros((cells_y, cells_z), jnp.float32)
        stiff_sum, mass_sum, _ = lax.fori_loop(0, pair_count, over_pairs, (zero, zero, x))
        stiff_out[x] = stiff_sum
        mass_out[x] = mass_sum
        return carry

    lax.fori_loop(0, cells_x, over_x, 0)


def mxu_energy_kernel(
    fields_ref, rim_x_ref, rim_y_ref, stiffness_ref, mass_ref, stiff_out, mass_out, coupling_ref,
    state_rows, adjoint_rows, products,
):
    pair_count = fields_ref.shape[0]
    cells_x, cells_y, cells_z = stiff_out.shape
    dofs = 3 * len(CORNERS)
    wide = dofs * cells_y
    spread_rows = (
        lax.broadcasted_iota(jnp.int32, (wide, dofs), 0) // cells_y
        == lax.broadcasted_iota(jnp.int32, (wide, dofs), 1)
    ).astype(jnp.float32)
    spread_columns = (
        lax.broadcasted_iota(jnp.int32, (dofs, wide), 0)
        == lax.broadcasted_iota(jnp.int32, (dofs, wide), 1) // cells_y
    ).astype(jnp.float32)
    same_y = (
        lax.broadcasted_iota(jnp.int32, (wide, wide), 0) % cells_y
        == lax.broadcasted_iota(jnp.int32, (wide, wide), 1) % cells_y
    )
    for block, matrix_ref in enumerate((stiffness_ref, mass_ref)):
        spread = jnp.dot(
            matrix_ref[...], spread_columns, precision=lax.Precision.HIGHEST,
            preferred_element_type=jnp.float32,
        )
        spread = jnp.dot(
            spread_rows, spread, precision=lax.Precision.HIGHEST, preferred_element_type=jnp.float32
        )
        coupling_ref[pl.ds(block * wide, wide), :] = jnp.where(same_y, spread, 0.0)
    lane = lax.broadcasted_iota(jnp.int32, (cells_y, cells_z), 1)
    inside = lane < cells_z - 1
    last_row = lax.broadcasted_iota(jnp.int32, (cells_y, cells_z), 0) == cells_y - 1
    stiff_out[...] = jnp.zeros(stiff_out.shape, jnp.float32)
    mass_out[...] = jnp.zeros(mass_out.shape, jnp.float32)
    member_rows = (state_rows, adjoint_rows)

    def over_pairs(pair, carry):
        for node_x in range(cells_x + 1):
            for member in range(2):
                for component in range(3):
                    if node_x < cells_x:
                        tile = fields_ref[pair, member, component, node_x]
                    else:
                        tile = rim_x_ref[pair, member, component, 0]
                    for corner_y in (0, 1):
                        base = tile
                        if corner_y:
                            below = jnp.broadcast_to(
                                rim_y_ref[pair, member, component, node_x], (cells_y, cells_z)
                            )
                            base = jnp.where(last_row, below, pltpu.roll(tile, cells_y - 1, 0))
                        for corner_z in (0, 1):
                            value = base
                            if corner_z:
                                value = jnp.where(inside, pltpu.roll(base, cells_z - 1, 1), 0.0)
                            for corner_x in (0, 1):
                                x = node_x - corner_x
                                if 0 <= x < cells_x:
                                    corner = CORNERS.index((corner_x, corner_y, corner_z))
                                    row = 3 * corner + component
                                    member_rows[member][
                                        pl.ds(row * cells_y, cells_y), pl.ds(x * cells_z, cells_z)
                                    ] = value
        products[...] = jnp.dot(
            coupling_ref[...],
            adjoint_rows[...],
            precision=lax.Precision.HIGH,
            preferred_element_type=jnp.float32,
        )
        state = state_rows[...].reshape(dofs, cells_y, cells_x * cells_z)
        stiff_sum = jnp.sum(
            state * products[pl.ds(0, wide), :].reshape(dofs, cells_y, cells_x * cells_z), axis=0
        )
        mass_sum = jnp.sum(
            state * products[pl.ds(wide, wide), :].reshape(dofs, cells_y, cells_x * cells_z), axis=0
        )
        for x in range(cells_x):
            columns = slice(x * cells_z, (x + 1) * cells_z)
            stiff_out[x] = stiff_out[x] + stiff_sum[:, columns]
            mass_out[x] = mass_out[x] + mass_sum[:, columns]
        return carry

    lax.fori_loop(0, pair_count, over_pairs, 0)


def element_energies(fields, rim_x, rim_y, stiffness, mass_matrix):
    pair_count = fields.shape[0]
    cells = fields.shape[3:]
    voxels = cells[0] * cells[1] * cells[2]
    dofs = stiffness.shape[0]
    vmem = pl.BlockSpec(memory_space=pltpu.VMEM)
    return pl.pallas_call(
        mxu_energy_kernel,
        out_shape=(
            jax.ShapeDtypeStruct(cells, jnp.float32),
            jax.ShapeDtypeStruct(cells, jnp.float32),
        ),
        in_specs=[vmem, vmem, vmem, vmem, vmem],
        out_specs=(vmem, vmem),
        scratch_shapes=[
            pltpu.VMEM((2 * dofs * cells[1], dofs * cells[1]), jnp.float32),
            pltpu.VMEM((dofs * cells[1], cells[0] * cells[2]), jnp.float32),
            pltpu.VMEM((dofs * cells[1], cells[0] * cells[2]), jnp.float32),
            pltpu.VMEM((2 * dofs * cells[1], cells[0] * cells[2]), jnp.float32),
        ],
        cost_estimate=pl.CostEstimate(
            flops=pair_count * (4 * (dofs * cells[1]) ** 2 * cells[0] * cells[2] + 4 * dofs * voxels),
            bytes_accessed=(fields.size + rim_x.size + rim_y.size) * 4 + 2 * stiffness.size * 4 + 2 * voxels * 4,
            transcendentals=0,
        ),
    )(fields, rim_x, rim_y, stiffness, mass_matrix)


def shards(design, passive, basis_pairs, supports, stiffness, mass_matrix, volume_fraction):
    block_shape = design.shape
    size_x, size_y, size_z = block_shape
    devices_x = lax.axis_size("gx")
    devices_y = lax.axis_size("gy")
    index_x = lax.axis_index("gx")
    index_y = lax.axis_index("gy")
    grid_x = size_x * devices_x
    grid_y = size_y * devices_y
    spread_x = jnp.arange(size_x + 4, dtype=jnp.int32) + index_x * size_x - 2
    spread_y = jnp.arange(size_y + 4, dtype=jnp.int32) + index_y * size_y - 2
    valid_x = ((spread_x >= 0) & (spread_x < grid_x)).astype(jnp.float32)
    valid_y = ((spread_y >= 0) & (spread_y < grid_y)).astype(jnp.float32)
    valid_z = jnp.pad(jnp.ones((size_z,), jnp.float32), 2)
    inside = valid_x[:, None, None] * valid_y[None, :, None] * valid_z[None, None, :]
    weight_sum = stencil(inside, block_shape)
    fields = basis_pairs * (1 - supports).astype(jnp.float32)
    design_wide, (rim_x, rim_y) = front_exchange(design, basis_pairs, supports, 2)
    design_wide = jnp.pad(design_wide, ((0, 0), (0, 0), (2, 2)))
    physical = jnp.where(passive == 1, 1.0, stencil(design_wide, block_shape) / weight_sum)
    stiff_energy, mass_energy = element_energies(fields, rim_x, rim_y, stiffness, mass_matrix)
    raw_sensitivity = -(
        PENALTY_SCALE * physical * physical * stiff_energy - OMEGA_SQUARED * mass_energy
    )
    raw_sensitivity = jnp.where(passive == 1, 0.0, raw_sensitivity)
    scaled_wide = with_halo(raw_sensitivity / weight_sum, (("gx", 0), ("gy", 1)), 2)
    scaled_wide = jnp.pad(scaled_wide, ((0, 0), (0, 0), (2, 2)))
    sensitivity = stencil(scaled_wide, block_shape)
    benefit = jnp.maximum(-sensitivity, 0.0)
    floor_value = jnp.maximum(design - MOVE_LIMIT, 0.0)
    ceiling = jnp.minimum(design + MOVE_LIMIT, 1.0)
    band_cells = size_z // REGIONS
    target = volume_fraction * float(grid_x * grid_y * band_cells)

    def candidate(multiplier):
        per_cell = jnp.repeat(multiplier, band_cells)[None, None, :]
        trial = design * jnp.sqrt(benefit / per_cell)
        return jnp.where(passive == 1, 1.0, jnp.minimum(ceiling, jnp.maximum(floor_value, trial)))

    def region_sum(field):
        return jnp.sum(field, axis=(0, 1)).reshape(REGIONS, band_cells).sum(axis=1)

    levels = BISECT

    def bisect_round(round_index, bracket):
        low_end, high_end = bracket
        level_nodes = [(low_end, high_end)]
        midpoints = []
        for depth in range(levels):
            next_nodes = []
            for node_low, node_high in level_nodes:
                middle = jnp.sqrt(node_low * node_high)
                midpoints.append(middle)
                next_nodes.append((node_low, middle))
                next_nodes.append((middle, node_high))
            level_nodes = next_nodes
        trial_multipliers = jnp.stack(midpoints)
        per_cell = jnp.repeat(trial_multipliers, band_cells, axis=1)[:, None, None, :]
        trial = design[None] * jnp.sqrt(benefit[None] / per_cell)
        fields_of = jnp.where(
            passive[None] == 1, 1.0, jnp.minimum(ceiling[None], jnp.maximum(floor_value[None], trial))
        )
        partial_volumes = (
            jnp.sum(fields_of, axis=(1, 2)).reshape(len(midpoints), REGIONS, band_cells).sum(axis=2)
        )
        lanes = 128
        flat = partial_volumes.reshape(-1)
        spare = -flat.size % lanes
        dense = jnp.pad(flat, (0, spare)).reshape(-1, lanes)
        dense = butterfly_sum(butterfly_sum(dense, "gy"), "gx")
        volumes = dense.reshape(-1)[: flat.size].reshape(partial_volumes.shape)
        heavier_all = volumes > target[None, :]
        position = jnp.zeros((REGIONS,), jnp.int32)
        for depth in range(levels):
            middle = jnp.sqrt(low_end * high_end)
            nodes = lax.slice_in_dim(heavier_all, 2**depth - 1, 2 ** (depth + 1) - 1, axis=0)
            slots = lax.broadcasted_iota(jnp.int32, nodes.shape, 0)
            heavier = jnp.any(nodes & (slots == position[None, :]), axis=0)
            low_end = jnp.where(heavier, middle, low_end)
            high_end = jnp.where(heavier, high_end, middle)
            position = 2 * position + heavier.astype(jnp.int32)
        return (low_end, high_end)

    start = (jnp.full((REGIONS,), 0.0001, jnp.float32), jnp.full((REGIONS,), 10000.0, jnp.float32))
    low_end, high_end = bisect_round(0, start)
    design_next = candidate(jnp.sqrt(low_end * high_end))
    return (sensitivity, design_next)


def solution(mesh):
    placed = (
        P("gx", "gy", None),
        P("gx", "gy", None),
        P(None, None, None, "gx", "gy", None),
        P("gx", "gy", None),
        P(),
        P(),
        P(),
    )
    return jax.shard_map(
        shards,
        mesh=mesh,
        in_specs=placed,
        out_specs=(P("gx", "gy", None), P("gx", "gy", None)),
        check_vma=False,
    )
```

```python
import functools
import math

import jax
import jax.numpy as jnp
from jax import lax
from jax.sharding import PartitionSpec as P
from jax.experimental import pallas as pl
from jax.experimental.pallas import tpu as pltpu

BISECT = 6
REGIONS = 64


PENALTY_SCALE = 3.0 * (1.0 - 0.001)
OMEGA_SQUARED = 0.5
MOVE_LIMIT = 0.2


def with_halo(cells, sides, width):
    for axis, dim in sides:
        count = lax.axis_size(axis)
        ends = count - 1
        head = lax.slice_in_dim(cells, 0, width, axis=dim)
        tail = lax.slice_in_dim(cells, cells.shape[dim] - width, cells.shape[dim], axis=dim)
        cells = jnp.concatenate(
            [
                lax.ppermute(tail, axis, [(i, (i + 1) % count) for i in range(ends)]),
                cells,
                lax.ppermute(head, axis, [((i + 1) % count, i) for i in range(ends)]),
            ],
            axis=dim,
        )
    return cells


def front_exchange(cells, basis_pairs, supports, width):
    open_nodes = (1 - supports).astype(jnp.float32)
    rim = basis_pairs[:, :, :, :1] * open_nodes[:1]
    rims = []
    for axis, dim in (("gx", 0), ("gy", 1)):
        count = lax.axis_size(axis)
        ends = count - 1
        head = lax.slice_in_dim(cells, 0, width, axis=dim)
        tail = lax.slice_in_dim(cells, cells.shape[dim] - width, cells.shape[dim], axis=dim)
        lanes = cells.shape[-1]
        packed = jnp.concatenate([head.reshape(-1, lanes), rim.reshape(-1, lanes)], axis=0)
        packed = lax.ppermute(packed, axis, [((i + 1) % count, i) for i in range(ends)])
        split = head.size // lanes
        head = packed[:split].reshape(head.shape)
        received = packed[split:].reshape(rim.shape)
        tail = lax.ppermute(tail, axis, [(i, (i + 1) % count) for i in range(ends)])
        cells = jnp.concatenate([tail, cells, head], axis=dim)
        rims.append(received)
        if axis == "gx":
            rim = jnp.concatenate(
                [basis_pairs[:, :, :, :, :1] * open_nodes[:, :1], received[:, :, :, :, :1]], axis=3
            )
    return cells, rims


def from_behind(value, axis, steps):
    count = lax.axis_size(axis)
    initial, last = (max(0, -steps), min(count, count - steps))
    return lax.ppermute(value, axis, [(source, source + steps) for source in range(initial, last)])


def butterfly_sum(value, axis):
    count = lax.axis_size(axis)
    stride = 1
    while stride < count:
        value = value + lax.ppermute(value, axis, [(i, i ^ stride) for i in range(count)])
        stride *= 2
    return value


def filter_taps():
    tap_list = []
    for offset_x in range(-2, 3):
        for offset_y in range(-2, 3):
            for offset_z in range(-2, 3):
                weight = 3.0 - math.sqrt(
                    offset_x * offset_x + offset_y * offset_y + offset_z * offset_z
                )
                if weight > 0.0:
                    tap_list.append((offset_x, offset_y, offset_z, weight))
    return tap_list


def stencil(padded, block_shape):
    result = jnp.zeros(block_shape, jnp.float32)
    for offset_x, offset_y, offset_z, weight in filter_taps():
        result = (
            result
            + weight
            * padded[
                2 + offset_x : 2 + offset_x + block_shape[0],
                2 + offset_y : 2 + offset_y + block_shape[1],
                2 + offset_z : 2 + offset_z + block_shape[2],
            ]
        )
    return result


def element_terms(extended, stiffness, mass_matrix):
    pair_count = extended.shape[0]
    cells_x = extended.shape[3] - 1
    cells_y = extended.shape[4] - 1
    cells_z = extended.shape[5] - 1
    stiff_energy = jnp.zeros((cells_x * cells_y * cells_z,), jnp.float32)
    mass_energy = jnp.zeros((cells_x * cells_y * cells_z,), jnp.float32)
    for pair_index in range(pair_count):
        vectors = []
        for member in range(2):
            row_list = []
            for corner_x in (0, 1):
                for corner_y in (0, 1):
                    for corner_z in (0, 1):
                        for component in range(3):
                            row_list.append(
                                extended[
                                    pair_index,
                                    member,
                                    component,
                                    corner_x : corner_x + cells_x,
                                    corner_y : corner_y + cells_y,
                                    corner_z : corner_z + cells_z,
                                ].reshape(-1)
                            )
            vectors.append(jnp.stack(row_list))
        state_rows, adjoint_rows = vectors
        stiff_energy = stiff_energy + jnp.sum(
            state_rows * jnp.dot(stiffness, adjoint_rows, precision=lax.Precision.HIGHEST), axis=0
        )
        mass_energy = mass_energy + jnp.sum(
            state_rows * jnp.dot(mass_matrix, adjoint_rows, precision=lax.Precision.HIGHEST), axis=0
        )
    return (
        stiff_energy.reshape(cells_x, cells_y, cells_z),
        mass_energy.reshape(cells_x, cells_y, cells_z),
    )


CORNERS = [(a, b, d) for a in (0, 1) for b in (0, 1) for d in (0, 1)]


def energy_kernel(extended_ref, stiffness_ref, mass_ref, stiff_out, mass_out):
    pair_count = extended_ref.shape[0]
    cells_x, cells_y, cells_z = stiff_out.shape
    lane = lax.broadcasted_iota(jnp.int32, (cells_y, cells_z), 1)
    inside = lane < cells_z - 1
    last_row = lax.broadcasted_iota(jnp.int32, (cells_y, cells_z), 0) == cells_y - 1

    def node_view(pair, member, component, x, corner):
        corner_x, corner_y, corner_z = corner
        value = extended_ref[pair, member, component, x + corner_x, pl.ds(corner_y, cells_y), :]
        if corner_z:
            value = jnp.where(inside, pltpu.roll(value, cells_z - 1, 1), 0.0)
        return value

    def over_pairs(pair, energies):
        stiff_sum, mass_sum, x = energies
        adjoint = [
            node_view(pair, 1, component, x, corner) for corner in CORNERS for component in range(3)
        ]
        for row in range(len(adjoint)):
            state = node_view(pair, 0, row % 3, x, CORNERS[row // 3])
            stiff_row = stiffness_ref[row, 0] * adjoint[0]
            mass_row = mass_ref[row, 0] * adjoint[0]
            for column in range(1, len(adjoint)):
                stiff_row = stiff_row + stiffness_ref[row, column] * adjoint[column]
                mass_row = mass_row + mass_ref[row, column] * adjoint[column]
            stiff_sum = stiff_sum + state * stiff_row
            mass_sum = mass_sum + state * mass_row
        return stiff_sum, mass_sum, x

    def over_x(x, carry):
        zero = jnp.zeros((cells_y, cells_z), jnp.float32)
        stiff_sum, mass_sum, _ = lax.fori_loop(0, pair_count, over_pairs, (zero, zero, x))
        stiff_out[x] = stiff_sum
        mass_out[x] = mass_sum
        return carry

    lax.fori_loop(0, cells_x, over_x, 0)


def mxu_energy_kernel(slices, scaled, *refs):
    if scaled:
        (fields_ref, rim_x_ref, rim_y_ref, stiffness_ref, mass_ref, physical_ref, passive_ref,
         weight_ref, stiff_out, mass_out, scaled_out, coupling_ref, state_rows, adjoint_rows,
         products) = refs
    else:
        (fields_ref, rim_x_ref, rim_y_ref, stiffness_ref, mass_ref, stiff_out, mass_out,
         coupling_ref, state_rows, adjoint_rows, products) = refs
    pair_count = fields_ref.shape[0]
    cells_x = fields_ref.shape[3]
    _, cells_y, cells_z = stiff_out.shape
    columns_of = len(slices) * cells_z
    dofs = 3 * len(CORNERS)
    wide = dofs * cells_y
    spread_rows = (
        lax.broadcasted_iota(jnp.int32, (wide, dofs), 0) // cells_y
        == lax.broadcasted_iota(jnp.int32, (wide, dofs), 1)
    ).astype(jnp.float32)
    spread_columns = (
        lax.broadcasted_iota(jnp.int32, (dofs, wide), 0)
        == lax.broadcasted_iota(jnp.int32, (dofs, wide), 1) // cells_y
    ).astype(jnp.float32)
    same_y = (
        lax.broadcasted_iota(jnp.int32, (wide, wide), 0) % cells_y
        == lax.broadcasted_iota(jnp.int32, (wide, wide), 1) % cells_y
    )
    for block, matrix_ref in enumerate((stiffness_ref, mass_ref)):
        spread = jnp.dot(
            matrix_ref[...], spread_columns, precision=lax.Precision.HIGHEST,
            preferred_element_type=jnp.float32,
        )
        spread = jnp.dot(
            spread_rows, spread, precision=lax.Precision.HIGHEST, preferred_element_type=jnp.float32
        )
        coupling_ref[pl.ds(block * wide, wide), :] = jnp.where(same_y, spread, 0.0)
    lane = lax.broadcasted_iota(jnp.int32, (cells_y, cells_z), 1)
    inside = lane < cells_z - 1
    last_row = lax.broadcasted_iota(jnp.int32, (cells_y, cells_z), 0) == cells_y - 1
    stiff_out[...] = jnp.zeros(stiff_out.shape, jnp.float32)
    mass_out[...] = jnp.zeros(mass_out.shape, jnp.float32)
    member_rows = (state_rows, adjoint_rows)

    def over_pairs(pair, carry):
        for node_x in sorted(set(slices) | {x + 1 for x in slices}):
            for member in range(2):
                for component in range(3):
                    if node_x < cells_x:
                        tile = fields_ref[pair, member, component, node_x]
                    else:
                        tile = rim_x_ref[pair, member, component, 0]
                    for corner_y in (0, 1):
                        base = tile
                        if corner_y:
                            below = jnp.broadcast_to(
                                rim_y_ref[pair, member, component, node_x], (cells_y, cells_z)
                            )
                            base = jnp.where(last_row, below, pltpu.roll(tile, cells_y - 1, 0))
                        for corner_z in (0, 1):
                            value = base
                            if corner_z:
                                value = jnp.where(inside, pltpu.roll(base, cells_z - 1, 1), 0.0)
                            for corner_x in (0, 1):
                                x = node_x - corner_x
                                if x in slices:
                                    place = slices.index(x)
                                    corner = CORNERS.index((corner_x, corner_y, corner_z))
                                    row = 3 * corner + component
                                    member_rows[member][
                                        pl.ds(row * cells_y, cells_y), pl.ds(place * cells_z, cells_z)
                                    ] = value
        products[...] = jnp.dot(
            coupling_ref[...],
            adjoint_rows[...],
            precision=lax.Precision.HIGH,
            preferred_element_type=jnp.float32,
        )
        state = state_rows[...].reshape(dofs, cells_y, columns_of)
        stiff_sum = jnp.sum(
            state * products[pl.ds(0, wide), :].reshape(dofs, cells_y, columns_of), axis=0
        )
        mass_sum = jnp.sum(
            state * products[pl.ds(wide, wide), :].reshape(dofs, cells_y, columns_of), axis=0
        )
        for place in range(len(slices)):
            columns = slice(place * cells_z, (place + 1) * cells_z)
            stiff_out[place] = stiff_out[place] + stiff_sum[:, columns]
            mass_out[place] = mass_out[place] + mass_sum[:, columns]
        return carry

    lax.fori_loop(0, pair_count, over_pairs, 0)
    if scaled:
        physical_rows = physical_ref[...]
        raw_rows = -(
            PENALTY_SCALE * physical_rows * physical_rows * stiff_out[...]
            - OMEGA_SQUARED * mass_out[...]
        )
        raw_rows = jnp.where(passive_ref[...] == 1, 0.0, raw_rows)
        scaled_out[...] = raw_rows / weight_ref[...]


def element_energies(fields, rim_x, rim_y, stiffness, mass_matrix, slices, scaling=()):
    pair_count = fields.shape[0]
    cells = (len(slices),) + fields.shape[4:]
    voxels = cells[0] * cells[1] * cells[2]
    dofs = stiffness.shape[0]
    vmem = pl.BlockSpec(memory_space=pltpu.VMEM)
    return pl.pallas_call(
        functools.partial(mxu_energy_kernel, slices, bool(scaling)),
        out_shape=(jax.ShapeDtypeStruct(cells, jnp.float32),) * (3 if scaling else 2),
        in_specs=[vmem] * (5 + len(scaling)),
        out_specs=(vmem,) * (3 if scaling else 2),
        scratch_shapes=[
            pltpu.VMEM((2 * dofs * cells[1], dofs * cells[1]), jnp.float32),
            pltpu.VMEM((dofs * cells[1], cells[0] * cells[2]), jnp.float32),
            pltpu.VMEM((dofs * cells[1], cells[0] * cells[2]), jnp.float32),
            pltpu.VMEM((2 * dofs * cells[1], cells[0] * cells[2]), jnp.float32),
        ],
        cost_estimate=pl.CostEstimate(
            flops=pair_count * (4 * (dofs * cells[1]) ** 2 * cells[0] * cells[2] + 4 * dofs * voxels),
            bytes_accessed=(fields.size + rim_x.size + rim_y.size) * 4 * cells[0] // fields.shape[3]
            + 2 * stiffness.size * 4 + 2 * voxels * 4,
            transcendentals=0,
        ),
    )(fields, rim_x, rim_y, stiffness, mass_matrix, *scaling)


def shards(design, passive, basis_pairs, supports, stiffness, mass_matrix, volume_fraction):
    block_shape = design.shape
    size_x, size_y, size_z = block_shape
    devices_x = lax.axis_size("gx")
    devices_y = lax.axis_size("gy")
    index_x = lax.axis_index("gx")
    index_y = lax.axis_index("gy")
    grid_x = size_x * devices_x
    grid_y = size_y * devices_y
    spread_x = jnp.arange(size_x + 4, dtype=jnp.int32) + index_x * size_x - 2
    spread_y = jnp.arange(size_y + 4, dtype=jnp.int32) + index_y * size_y - 2
    valid_x = ((spread_x >= 0) & (spread_x < grid_x)).astype(jnp.float32)
    valid_y = ((spread_y >= 0) & (spread_y < grid_y)).astype(jnp.float32)
    valid_z = jnp.pad(jnp.ones((size_z,), jnp.float32), 2)
    inside = valid_x[:, None, None] * valid_y[None, :, None] * valid_z[None, None, :]
    weight_sum = stencil(inside, block_shape)
    fields = basis_pairs * (1 - supports).astype(jnp.float32)
    design_wide, (rim_x, rim_y) = front_exchange(design, basis_pairs, supports, 2)
    design_wide = jnp.pad(design_wide, ((0, 0), (0, 0), (2, 2)))
    physical = jnp.where(passive == 1, 1.0, stencil(design_wide, block_shape) / weight_sum)
    last = size_x - 1
    rim_slices = (0, 1, last - 1, last)
    inner_slices = tuple(range(2, last - 1))
    rim_scaling = tuple(
        jnp.concatenate([array[:2], array[last - 1 :]], axis=0) for array in (physical, passive, weight_sum)
    )
    _, _, rim_rows = element_energies(
        fields, rim_x, rim_y, stiffness, mass_matrix, rim_slices, rim_scaling
    )
    inner_stiff, inner_mass = element_energies(
        fields, rim_x, rim_y, stiffness, mass_matrix, inner_slices
    )

    def scaled_raw(stiff_rows, mass_rows, first, end):
        physical_rows = physical[first:end]
        raw_rows = -(
            PENALTY_SCALE * physical_rows * physical_rows * stiff_rows - OMEGA_SQUARED * mass_rows
        )
        raw_rows = jnp.where(passive[first:end] == 1, 0.0, raw_rows)
        return raw_rows / weight_sum[first:end]

    head_rows = rim_rows[:2]
    tail_rows = rim_rows[2:]
    inner_rows = scaled_raw(inner_stiff, inner_mass, 2, last - 1)
    count_x = lax.axis_size("gx")
    head_x = lax.ppermute(head_rows, "gx", [(i + 1, i) for i in range(count_x - 1)])
    tail_x = lax.ppermute(tail_rows, "gx", [(i, i + 1) for i in range(count_x - 1)])
    scaled_wide = jnp.concatenate([tail_x, head_rows, inner_rows, tail_rows, head_x], axis=0)
    scaled_wide = with_halo(scaled_wide, (("gy", 1),), 2)
    scaled_wide = jnp.pad(scaled_wide, ((0, 0), (0, 0), (2, 2)))
    sensitivity = stencil(scaled_wide, block_shape)
    benefit = jnp.maximum(-sensitivity, 0.0)
    floor_value = jnp.maximum(design - MOVE_LIMIT, 0.0)
    ceiling = jnp.minimum(design + MOVE_LIMIT, 1.0)
    band_cells = size_z // REGIONS
    target = volume_fraction * float(grid_x * grid_y * band_cells)

    def candidate(multiplier):
        per_cell = jnp.repeat(multiplier, band_cells)[None, None, :]
        trial = design * jnp.sqrt(benefit / per_cell)
        return jnp.where(passive == 1, 1.0, jnp.minimum(ceiling, jnp.maximum(floor_value, trial)))

    def region_sum(field):
        return jnp.sum(field, axis=(0, 1)).reshape(REGIONS, band_cells).sum(axis=1)

    levels = BISECT

    def bisect_round(round_index, bracket):
        low_end, high_end = bracket
        level_nodes = [(low_end, high_end)]
        midpoints = []
        for depth in range(levels):
            next_nodes = []
            for node_low, node_high in level_nodes:
                middle = jnp.sqrt(node_low * node_high)
                midpoints.append(middle)
                next_nodes.append((node_low, middle))
                next_nodes.append((middle, node_high))
            level_nodes = next_nodes
        trial_multipliers = jnp.stack(midpoints)
        per_cell = jnp.repeat(trial_multipliers, band_cells, axis=1)[:, None, None, :]
        trial = design[None] * jnp.sqrt(benefit[None] / per_cell)
        fields_of = jnp.where(
            passive[None] == 1, 1.0, jnp.minimum(ceiling[None], jnp.maximum(floor_value[None], trial))
        )
        partial_volumes = (
            jnp.sum(fields_of, axis=(1, 2)).reshape(len(midpoints), REGIONS, band_cells).sum(axis=2)
        )
        lanes = 128
        flat = partial_volumes.reshape(-1)
        spare = -flat.size % lanes
        dense = jnp.pad(flat, (0, spare)).reshape(-1, lanes)
        dense = butterfly_sum(butterfly_sum(dense, "gy"), "gx")
        volumes = dense.reshape(-1)[: flat.size].reshape(partial_volumes.shape)
        heavier_all = volumes > target[None, :]
        position = jnp.zeros((REGIONS,), jnp.int32)
        for depth in range(levels):
            middle = jnp.sqrt(low_end * high_end)
            nodes = lax.slice_in_dim(heavier_all, 2**depth - 1, 2 ** (depth + 1) - 1, axis=0)
            slots = lax.broadcasted_iota(jnp.int32, nodes.shape, 0)
            heavier = jnp.any(nodes & (slots == position[None, :]), axis=0)
            low_end = jnp.where(heavier, middle, low_end)
            high_end = jnp.where(heavier, high_end, middle)
            position = 2 * position + heavier.astype(jnp.int32)
        return (low_end, high_end)

    start = (jnp.full((REGIONS,), 0.0001, jnp.float32), jnp.full((REGIONS,), 10000.0, jnp.float32))
    low_end, high_end = bisect_round(0, start)
    design_next = candidate(jnp.sqrt(low_end * high_end))
    return (sensitivity, design_next)


def solution(mesh):
    placed = (
        P("gx", "gy", None),
        P("gx", "gy", None),
        P(None, None, None, "gx", "gy", None),
        P("gx", "gy", None),
        P(),
        P(),
        P(),
    )
    return jax.shard_map(
        shards,
        mesh=mesh,
        in_specs=placed,
        out_specs=(P("gx", "gy", None), P("gx", "gy", None)),
        check_vma=False,
    )
```

```python
import math

import jax
import jax.numpy as jnp
from jax import lax
from jax.sharding import PartitionSpec as P
from jax.experimental import pallas as pl
from jax.experimental.pallas import tpu as pltpu

BISECT = 6
REGIONS = 64


PENALTY_SCALE = 3.0 * (1.0 - 0.001)
OMEGA_SQUARED = 0.5
MOVE_LIMIT = 0.2


def with_halo(cells, sides, width):
    for axis, dim in sides:
        count = lax.axis_size(axis)
        ends = count - 1
        head = lax.slice_in_dim(cells, 0, width, axis=dim)
        tail = lax.slice_in_dim(cells, cells.shape[dim] - width, cells.shape[dim], axis=dim)
        cells = jnp.concatenate(
            [
                lax.ppermute(tail, axis, [(i, (i + 1) % count) for i in range(ends)]),
                cells,
                lax.ppermute(head, axis, [((i + 1) % count, i) for i in range(ends)]),
            ],
            axis=dim,
        )
    return cells


def front_exchange(cells, basis_pairs, supports, width):
    open_nodes = (1 - supports).astype(jnp.float32)
    rim = basis_pairs[:, :, :, :1] * open_nodes[:1]
    rims = []
    for axis, dim in (("gx", 0), ("gy", 1)):
        count = lax.axis_size(axis)
        ends = count - 1
        head = lax.slice_in_dim(cells, 0, width, axis=dim)
        tail = lax.slice_in_dim(cells, cells.shape[dim] - width, cells.shape[dim], axis=dim)
        lanes = cells.shape[-1]
        packed = jnp.concatenate([head.reshape(-1, lanes), rim.reshape(-1, lanes)], axis=0)
        packed = lax.ppermute(packed, axis, [((i + 1) % count, i) for i in range(ends)])
        split = head.size // lanes
        head = packed[:split].reshape(head.shape)
        received = packed[split:].reshape(rim.shape)
        tail = lax.ppermute(tail, axis, [(i, (i + 1) % count) for i in range(ends)])
        cells = jnp.concatenate([tail, cells, head], axis=dim)
        rims.append(received)
        if axis == "gx":
            rim = jnp.concatenate(
                [basis_pairs[:, :, :, :, :1] * open_nodes[:, :1], received[:, :, :, :, :1]], axis=3
            )
    return cells, rims


def from_behind(value, axis, steps):
    count = lax.axis_size(axis)
    initial, last = (max(0, -steps), min(count, count - steps))
    return lax.ppermute(value, axis, [(source, source + steps) for source in range(initial, last)])


def butterfly_sum(value, axis):
    count = lax.axis_size(axis)
    stride = 1
    while stride < count:
        value = value + lax.ppermute(value, axis, [(i, i ^ stride) for i in range(count)])
        stride *= 2
    return value


def filter_taps():
    tap_list = []
    for offset_x in range(-2, 3):
        for offset_y in range(-2, 3):
            for offset_z in range(-2, 3):
                weight = 3.0 - math.sqrt(
                    offset_x * offset_x + offset_y * offset_y + offset_z * offset_z
                )
                if weight > 0.0:
                    tap_list.append((offset_x, offset_y, offset_z, weight))
    return tap_list


def stencil(padded, block_shape):
    result = jnp.zeros(block_shape, jnp.float32)
    for offset_x, offset_y, offset_z, weight in filter_taps():
        result = (
            result
            + weight
            * padded[
                2 + offset_x : 2 + offset_x + block_shape[0],
                2 + offset_y : 2 + offset_y + block_shape[1],
                2 + offset_z : 2 + offset_z + block_shape[2],
            ]
        )
    return result


def element_terms(extended, stiffness, mass_matrix):
    pair_count = extended.shape[0]
    cells_x = extended.shape[3] - 1
    cells_y = extended.shape[4] - 1
    cells_z = extended.shape[5] - 1
    stiff_energy = jnp.zeros((cells_x * cells_y * cells_z,), jnp.float32)
    mass_energy = jnp.zeros((cells_x * cells_y * cells_z,), jnp.float32)
    for pair_index in range(pair_count):
        vectors = []
        for member in range(2):
            row_list = []
            for corner_x in (0, 1):
                for corner_y in (0, 1):
                    for corner_z in (0, 1):
                        for component in range(3):
                            row_list.append(
                                extended[
                                    pair_index,
                                    member,
                                    component,
                                    corner_x : corner_x + cells_x,
                                    corner_y : corner_y + cells_y,
                                    corner_z : corner_z + cells_z,
                                ].reshape(-1)
                            )
            vectors.append(jnp.stack(row_list))
        state_rows, adjoint_rows = vectors
        stiff_energy = stiff_energy + jnp.sum(
            state_rows * jnp.dot(stiffness, adjoint_rows, precision=lax.Precision.HIGHEST), axis=0
        )
        mass_energy = mass_energy + jnp.sum(
            state_rows * jnp.dot(mass_matrix, adjoint_rows, precision=lax.Precision.HIGHEST), axis=0
        )
    return (
        stiff_energy.reshape(cells_x, cells_y, cells_z),
        mass_energy.reshape(cells_x, cells_y, cells_z),
    )


CORNERS = [(a, b, d) for a in (0, 1) for b in (0, 1) for d in (0, 1)]


def energy_kernel(extended_ref, stiffness_ref, mass_ref, stiff_out, mass_out):
    pair_count = extended_ref.shape[0]
    cells_x, cells_y, cells_z = stiff_out.shape
    lane = lax.broadcasted_iota(jnp.int32, (cells_y, cells_z), 1)
    inside = lane < cells_z - 1
    last_row = lax.broadcasted_iota(jnp.int32, (cells_y, cells_z), 0) == cells_y - 1

    def node_view(pair, member, component, x, corner):
        corner_x, corner_y, corner_z = corner
        value = extended_ref[pair, member, component, x + corner_x, pl.ds(corner_y, cells_y), :]
        if corner_z:
            value = jnp.where(inside, pltpu.roll(value, cells_z - 1, 1), 0.0)
        return value

    def over_pairs(pair, energies):
        stiff_sum, mass_sum, x = energies
        adjoint = [
            node_view(pair, 1, component, x, corner) for corner in CORNERS for component in range(3)
        ]
        for row in range(len(adjoint)):
            state = node_view(pair, 0, row % 3, x, CORNERS[row // 3])
            stiff_row = stiffness_ref[row, 0] * adjoint[0]
            mass_row = mass_ref[row, 0] * adjoint[0]
            for column in range(1, len(adjoint)):
                stiff_row = stiff_row + stiffness_ref[row, column] * adjoint[column]
                mass_row = mass_row + mass_ref[row, column] * adjoint[column]
            stiff_sum = stiff_sum + state * stiff_row
            mass_sum = mass_sum + state * mass_row
        return stiff_sum, mass_sum, x

    def over_x(x, carry):
        zero = jnp.zeros((cells_y, cells_z), jnp.float32)
        stiff_sum, mass_sum, _ = lax.fori_loop(0, pair_count, over_pairs, (zero, zero, x))
        stiff_out[x] = stiff_sum
        mass_out[x] = mass_sum
        return carry

    lax.fori_loop(0, cells_x, over_x, 0)


def mxu_energy_kernel(
    fields_ref, rim_x_ref, rim_y_ref, stiffness_ref, mass_ref, stiff_out, mass_out, coupling_ref,
    state_rows, adjoint_rows, products,
):
    pair_count = fields_ref.shape[0]
    cells_x, cells_y, cells_z = stiff_out.shape
    dofs = 3 * len(CORNERS)
    wide = dofs * cells_y
    spread_rows = (
        lax.broadcasted_iota(jnp.int32, (wide, dofs), 0) // cells_y
        == lax.broadcasted_iota(jnp.int32, (wide, dofs), 1)
    ).astype(jnp.float32)
    spread_columns = (
        lax.broadcasted_iota(jnp.int32, (dofs, wide), 0)
        == lax.broadcasted_iota(jnp.int32, (dofs, wide), 1) // cells_y
    ).astype(jnp.float32)
    same_y = (
        lax.broadcasted_iota(jnp.int32, (wide, wide), 0) % cells_y
        == lax.broadcasted_iota(jnp.int32, (wide, wide), 1) % cells_y
    )
    for block, matrix_ref in enumerate((stiffness_ref, mass_ref)):
        spread = jnp.dot(
            matrix_ref[...], spread_columns, precision=lax.Precision.HIGHEST,
            preferred_element_type=jnp.float32,
        )
        spread = jnp.dot(
            spread_rows, spread, precision=lax.Precision.HIGHEST, preferred_element_type=jnp.float32
        )
        coupling_ref[pl.ds(block * wide, wide), :] = jnp.where(same_y, spread, 0.0)
    lane = lax.broadcasted_iota(jnp.int32, (cells_y, cells_z), 1)
    inside = lane < cells_z - 1
    last_row = lax.broadcasted_iota(jnp.int32, (cells_y, cells_z), 0) == cells_y - 1
    stiff_out[...] = jnp.zeros(stiff_out.shape, jnp.float32)
    mass_out[...] = jnp.zeros(mass_out.shape, jnp.float32)
    member_rows = (state_rows, adjoint_rows)

    def over_pairs(pair, carry):
        for node_x in range(cells_x + 1):
            for member in range(2):
                for component in range(3):
                    if node_x < cells_x:
                        tile = fields_ref[pair, member, component, node_x]
                    else:
                        tile = rim_x_ref[pair, member, component, 0]
                    for corner_y in (0, 1):
                        base = tile
                        if corner_y:
                            below = jnp.broadcast_to(
                                rim_y_ref[pair, member, component, node_x], (cells_y, cells_z)
                            )
                            base = jnp.where(last_row, below, pltpu.roll(tile, cells_y - 1, 0))
                        for corner_z in (0, 1):
                            value = base
                            if corner_z:
                                value = jnp.where(inside, pltpu.roll(base, cells_z - 1, 1), 0.0)
                            for corner_x in (0, 1):
                                x = node_x - corner_x
                                if 0 <= x < cells_x:
                                    corner = CORNERS.index((corner_x, corner_y, corner_z))
                                    row = 3 * corner + component
                                    member_rows[member][
                                        pl.ds(row * cells_y, cells_y), pl.ds(x * cells_z, cells_z)
                                    ] = value
        products[...] = jnp.dot(
            coupling_ref[...],
            adjoint_rows[...],
            precision=lax.Precision.HIGH,
            preferred_element_type=jnp.float32,
        )
        state = state_rows[...].reshape(dofs, cells_y, cells_x * cells_z)
        stiff_sum = jnp.sum(
            state * products[pl.ds(0, wide), :].reshape(dofs, cells_y, cells_x * cells_z), axis=0
        )
        mass_sum = jnp.sum(
            state * products[pl.ds(wide, wide), :].reshape(dofs, cells_y, cells_x * cells_z), axis=0
        )
        for x in range(cells_x):
            columns = slice(x * cells_z, (x + 1) * cells_z)
            stiff_out[x] = stiff_out[x] + stiff_sum[:, columns]
            mass_out[x] = mass_out[x] + mass_sum[:, columns]
        return carry

    lax.fori_loop(0, pair_count, over_pairs, 0)


def element_energies(fields, rim_x, rim_y, stiffness, mass_matrix):
    pair_count = fields.shape[0]
    cells = fields.shape[3:]
    voxels = cells[0] * cells[1] * cells[2]
    dofs = stiffness.shape[0]
    vmem = pl.BlockSpec(memory_space=pltpu.VMEM)
    return pl.pallas_call(
        mxu_energy_kernel,
        out_shape=(
            jax.ShapeDtypeStruct(cells, jnp.float32),
            jax.ShapeDtypeStruct(cells, jnp.float32),
        ),
        in_specs=[vmem, vmem, vmem, vmem, vmem],
        out_specs=(vmem, vmem),
        scratch_shapes=[
            pltpu.VMEM((2 * dofs * cells[1], dofs * cells[1]), jnp.float32),
            pltpu.VMEM((dofs * cells[1], cells[0] * cells[2]), jnp.float32),
            pltpu.VMEM((dofs * cells[1], cells[0] * cells[2]), jnp.float32),
            pltpu.VMEM((2 * dofs * cells[1], cells[0] * cells[2]), jnp.float32),
        ],
        cost_estimate=pl.CostEstimate(
            flops=pair_count * (4 * (dofs * cells[1]) ** 2 * cells[0] * cells[2] + 4 * dofs * voxels),
            bytes_accessed=(fields.size + rim_x.size + rim_y.size) * 4 + 2 * stiffness.size * 4 + 2 * voxels * 4,
            transcendentals=0,
        ),
    )(fields, rim_x, rim_y, stiffness, mass_matrix)


def shards(design, passive, basis_pairs, supports, stiffness, mass_matrix, volume_fraction):
    block_shape = design.shape
    size_x, size_y, size_z = block_shape
    devices_x = lax.axis_size("gx")
    devices_y = lax.axis_size("gy")
    index_x = lax.axis_index("gx")
    index_y = lax.axis_index("gy")
    grid_x = size_x * devices_x
    grid_y = size_y * devices_y
    spread_x = jnp.arange(size_x + 4, dtype=jnp.int32) + index_x * size_x - 2
    spread_y = jnp.arange(size_y + 4, dtype=jnp.int32) + index_y * size_y - 2
    valid_x = ((spread_x >= 0) & (spread_x < grid_x)).astype(jnp.float32)
    valid_y = ((spread_y >= 0) & (spread_y < grid_y)).astype(jnp.float32)
    valid_z = jnp.pad(jnp.ones((size_z,), jnp.float32), 2)
    inside = valid_x[:, None, None] * valid_y[None, :, None] * valid_z[None, None, :]
    weight_sum = stencil(inside, block_shape)
    fields = basis_pairs * (1 - supports).astype(jnp.float32)
    design_wide, (rim_x, rim_y) = front_exchange(design, basis_pairs, supports, 2)
    design_wide = jnp.pad(design_wide, ((0, 0), (0, 0), (2, 2)))
    physical = jnp.where(passive == 1, 1.0, stencil(design_wide, block_shape) / weight_sum)
    stiff_energy, mass_energy = element_energies(fields, rim_x, rim_y, stiffness, mass_matrix)
    raw_sensitivity = -(
        PENALTY_SCALE * physical * physical * stiff_energy - OMEGA_SQUARED * mass_energy
    )
    raw_sensitivity = jnp.where(passive == 1, 0.0, raw_sensitivity)
    scaled_wide = with_halo(raw_sensitivity / weight_sum, (("gx", 0), ("gy", 1)), 2)
    scaled_wide = jnp.pad(scaled_wide, ((0, 0), (0, 0), (2, 2)))
    sensitivity = stencil(scaled_wide, block_shape)
    benefit = jnp.maximum(-sensitivity, 0.0)
    floor_value = jnp.maximum(design - MOVE_LIMIT, 0.0)
    ceiling = jnp.minimum(design + MOVE_LIMIT, 1.0)
    band_cells = size_z // REGIONS
    target = volume_fraction * float(grid_x * grid_y * band_cells)

    def candidate(multiplier):
        per_cell = jnp.repeat(multiplier, band_cells)[None, None, :]
        trial = design * jnp.sqrt(benefit / per_cell)
        return jnp.where(passive == 1, 1.0, jnp.minimum(ceiling, jnp.maximum(floor_value, trial)))

    def region_sum(field):
        return jnp.sum(field, axis=(0, 1)).reshape(REGIONS, band_cells).sum(axis=1)

    levels = BISECT

    def bisect_round(round_index, bracket):
        low_end, high_end = bracket
        level_nodes = [(low_end, high_end)]
        midpoints = []
        for depth in range(levels):
            next_nodes = []
            for node_low, node_high in level_nodes:
                middle = jnp.sqrt(node_low * node_high)
                midpoints.append(middle)
                next_nodes.append((node_low, middle))
                next_nodes.append((middle, node_high))
            level_nodes = next_nodes
        trial_multipliers = jnp.stack(midpoints)
        per_cell = jnp.repeat(trial_multipliers, band_cells, axis=1)[:, None, None, :]
        trial = design[None] * jnp.sqrt(benefit[None] / per_cell)
        fields_of = jnp.where(
            passive[None] == 1, 1.0, jnp.minimum(ceiling[None], jnp.maximum(floor_value[None], trial))
        )
        partial_volumes = (
            jnp.sum(fields_of, axis=(1, 2)).reshape(len(midpoints), REGIONS, band_cells).sum(axis=2)
        )
        lanes = 128
        flat = partial_volumes.reshape(-1)
        spare = -flat.size % lanes
        dense = jnp.pad(flat, (0, spare)).reshape(-1, lanes)
        dense = butterfly_sum(butterfly_sum(dense, "gx"), "gy")
        volumes = dense.reshape(-1)[: flat.size].reshape(partial_volumes.shape)
        heavier_all = volumes > target[None, :]
        position = jnp.zeros((REGIONS,), jnp.int32)
        for depth in range(levels):
            middle = jnp.sqrt(low_end * high_end)
            nodes = lax.slice_in_dim(heavier_all, 2**depth - 1, 2 ** (depth + 1) - 1, axis=0)
            slots = lax.broadcasted_iota(jnp.int32, nodes.shape, 0)
            heavier = jnp.any(nodes & (slots == position[None, :]), axis=0)
            low_end = jnp.where(heavier, middle, low_end)
            high_end = jnp.where(heavier, high_end, middle)
            position = 2 * position + heavier.astype(jnp.int32)
        return (low_end, high_end)

    start = (jnp.full((REGIONS,), 0.0001, jnp.float32), jnp.full((REGIONS,), 10000.0, jnp.float32))
    low_end, high_end = bisect_round(0, start)
    design_next = candidate(jnp.sqrt(low_end * high_end))
    return (sensitivity, design_next)


def solution(mesh):
    placed = (
        P("gx", "gy", None),
        P("gx", "gy", None),
        P(None, None, None, "gx", "gy", None),
        P("gx", "gy", None),
        P(),
        P(),
        P(),
    )
    return jax.shard_map(
        shards,
        mesh=mesh,
        in_specs=placed,
        out_specs=(P("gx", "gy", None), P("gx", "gy", None)),
        check_vma=False,
    )
```

```python
import math

import jax
import jax.numpy as jnp
from jax import lax
from jax.sharding import PartitionSpec as P
from jax.experimental import pallas as pl
from jax.experimental.pallas import tpu as pltpu

BISECT = 6
REGIONS = 64


PENALTY_SCALE = 3.0 * (1.0 - 0.001)
OMEGA_SQUARED = 0.5
MOVE_LIMIT = 0.2


def with_halo(cells, sides, width):
    for axis, dim in sides:
        count = lax.axis_size(axis)
        ends = count - 1
        head = lax.slice_in_dim(cells, 0, width, axis=dim)
        tail = lax.slice_in_dim(cells, cells.shape[dim] - width, cells.shape[dim], axis=dim)
        cells = jnp.concatenate(
            [
                lax.ppermute(tail, axis, [(i, (i + 1) % count) for i in range(ends)]),
                cells,
                lax.ppermute(head, axis, [((i + 1) % count, i) for i in range(ends)]),
            ],
            axis=dim,
        )
    return cells


def front_exchange(cells, basis_pairs, supports, width):
    rim = basis_pairs[:, :, :, :1] * (1 - supports[:1]).astype(jnp.float32)
    rims = []
    for axis, dim in (("gx", 0), ("gy", 1)):
        count = lax.axis_size(axis)
        ends = count - 1
        head = lax.slice_in_dim(cells, 0, width, axis=dim)
        tail = lax.slice_in_dim(cells, cells.shape[dim] - width, cells.shape[dim], axis=dim)
        lanes = cells.shape[-1]
        packed = jnp.concatenate([head.reshape(-1, lanes), rim.reshape(-1, lanes)], axis=0)
        packed = lax.ppermute(packed, axis, [((i + 1) % count, i) for i in range(ends)])
        split = head.size // lanes
        head = packed[:split].reshape(head.shape)
        received = packed[split:].reshape(rim.shape)
        tail = lax.ppermute(tail, axis, [(i, (i + 1) % count) for i in range(ends)])
        cells = jnp.concatenate([tail, cells, head], axis=dim)
        rims.append(received)
        if axis == "gx":
            rim = jnp.concatenate(
                [
                    basis_pairs[:, :, :, :, :1] * (1 - supports[:, :1]).astype(jnp.float32),
                    received[:, :, :, :, :1],
                ],
                axis=3,
            )
    return cells, rims


def from_behind(value, axis, steps):
    count = lax.axis_size(axis)
    initial, last = (max(0, -steps), min(count, count - steps))
    return lax.ppermute(value, axis, [(source, source + steps) for source in range(initial, last)])


def butterfly_sum(value, axis):
    count = lax.axis_size(axis)
    stride = 1
    while stride < count:
        value = value + lax.ppermute(value, axis, [(i, i ^ stride) for i in range(count)])
        stride *= 2
    return value


def filter_taps():
    tap_list = []
    for offset_x in range(-2, 3):
        for offset_y in range(-2, 3):
            for offset_z in range(-2, 3):
                weight = 3.0 - math.sqrt(
                    offset_x * offset_x + offset_y * offset_y + offset_z * offset_z
                )
                if weight > 0.0:
                    tap_list.append((offset_x, offset_y, offset_z, weight))
    return tap_list


def stencil(padded, block_shape):
    result = jnp.zeros(block_shape, jnp.float32)
    for offset_x, offset_y, offset_z, weight in filter_taps():
        result = (
            result
            + weight
            * padded[
                2 + offset_x : 2 + offset_x + block_shape[0],
                2 + offset_y : 2 + offset_y + block_shape[1],
                2 + offset_z : 2 + offset_z + block_shape[2],
            ]
        )
    return result


def element_terms(extended, stiffness, mass_matrix):
    pair_count = extended.shape[0]
    cells_x = extended.shape[3] - 1
    cells_y = extended.shape[4] - 1
    cells_z = extended.shape[5] - 1
    stiff_energy = jnp.zeros((cells_x * cells_y * cells_z,), jnp.float32)
    mass_energy = jnp.zeros((cells_x * cells_y * cells_z,), jnp.float32)
    for pair_index in range(pair_count):
        vectors = []
        for member in range(2):
            row_list = []
            for corner_x in (0, 1):
                for corner_y in (0, 1):
                    for corner_z in (0, 1):
                        for component in range(3):
                            row_list.append(
                                extended[
                                    pair_index,
                                    member,
                                    component,
                                    corner_x : corner_x + cells_x,
                                    corner_y : corner_y + cells_y,
                                    corner_z : corner_z + cells_z,
                                ].reshape(-1)
                            )
            vectors.append(jnp.stack(row_list))
        state_rows, adjoint_rows = vectors
        stiff_energy = stiff_energy + jnp.sum(
            state_rows * jnp.dot(stiffness, adjoint_rows, precision=lax.Precision.HIGHEST), axis=0
        )
        mass_energy = mass_energy + jnp.sum(
            state_rows * jnp.dot(mass_matrix, adjoint_rows, precision=lax.Precision.HIGHEST), axis=0
        )
    return (
        stiff_energy.reshape(cells_x, cells_y, cells_z),
        mass_energy.reshape(cells_x, cells_y, cells_z),
    )


CORNERS = [(a, b, d) for a in (0, 1) for b in (0, 1) for d in (0, 1)]


def energy_kernel(extended_ref, stiffness_ref, mass_ref, stiff_out, mass_out):
    pair_count = extended_ref.shape[0]
    cells_x, cells_y, cells_z = stiff_out.shape
    lane = lax.broadcasted_iota(jnp.int32, (cells_y, cells_z), 1)
    inside = lane < cells_z - 1
    last_row = lax.broadcasted_iota(jnp.int32, (cells_y, cells_z), 0) == cells_y - 1

    def node_view(pair, member, component, x, corner):
        corner_x, corner_y, corner_z = corner
        value = extended_ref[pair, member, component, x + corner_x, pl.ds(corner_y, cells_y), :]
        if corner_z:
            value = jnp.where(inside, pltpu.roll(value, cells_z - 1, 1), 0.0)
        return value

    def over_pairs(pair, energies):
        stiff_sum, mass_sum, x = energies
        adjoint = [
            node_view(pair, 1, component, x, corner) for corner in CORNERS for component in range(3)
        ]
        for row in range(len(adjoint)):
            state = node_view(pair, 0, row % 3, x, CORNERS[row // 3])
            stiff_row = stiffness_ref[row, 0] * adjoint[0]
            mass_row = mass_ref[row, 0] * adjoint[0]
            for column in range(1, len(adjoint)):
                stiff_row = stiff_row + stiffness_ref[row, column] * adjoint[column]
                mass_row = mass_row + mass_ref[row, column] * adjoint[column]
            stiff_sum = stiff_sum + state * stiff_row
            mass_sum = mass_sum + state * mass_row
        return stiff_sum, mass_sum, x

    def over_x(x, carry):
        zero = jnp.zeros((cells_y, cells_z), jnp.float32)
        stiff_sum, mass_sum, _ = lax.fori_loop(0, pair_count, over_pairs, (zero, zero, x))
        stiff_out[x] = stiff_sum
        mass_out[x] = mass_sum
        return carry

    lax.fori_loop(0, cells_x, over_x, 0)


def mxu_energy_kernel(
    fields_ref, rim_x_ref, rim_y_ref, stiffness_ref, mass_ref, stiff_out, mass_out, coupling_ref,
    state_rows, adjoint_rows, products,
):
    pair_count = fields_ref.shape[0]
    cells_x, cells_y, cells_z = stiff_out.shape
    dofs = 3 * len(CORNERS)
    wide = dofs * cells_y
    spread_rows = (
        lax.broadcasted_iota(jnp.int32, (wide, dofs), 0) // cells_y
        == lax.broadcasted_iota(jnp.int32, (wide, dofs), 1)
    ).astype(jnp.float32)
    spread_columns = (
        lax.broadcasted_iota(jnp.int32, (dofs, wide), 0)
        == lax.broadcasted_iota(jnp.int32, (dofs, wide), 1) // cells_y
    ).astype(jnp.float32)
    same_y = (
        lax.broadcasted_iota(jnp.int32, (wide, wide), 0) % cells_y
        == lax.broadcasted_iota(jnp.int32, (wide, wide), 1) % cells_y
    )
    for block, matrix_ref in enumerate((stiffness_ref, mass_ref)):
        spread = jnp.dot(
            matrix_ref[...], spread_columns, precision=lax.Precision.HIGHEST,
            preferred_element_type=jnp.float32,
        )
        spread = jnp.dot(
            spread_rows, spread, precision=lax.Precision.HIGHEST, preferred_element_type=jnp.float32
        )
        coupling_ref[pl.ds(block * wide, wide), :] = jnp.where(same_y, spread, 0.0)
    lane = lax.broadcasted_iota(jnp.int32, (cells_y, cells_z), 1)
    inside = lane < cells_z - 1
    last_row = lax.broadcasted_iota(jnp.int32, (cells_y, cells_z), 0) == cells_y - 1
    stiff_out[...] = jnp.zeros(stiff_out.shape, jnp.float32)
    mass_out[...] = jnp.zeros(mass_out.shape, jnp.float32)
    member_rows = (state_rows, adjoint_rows)

    def over_pairs(pair, carry):
        for node_x in range(cells_x + 1):
            for member in range(2):
                for component in range(3):
                    if node_x < cells_x:
                        tile = fields_ref[pair, member, component, node_x]
                    else:
                        tile = rim_x_ref[pair, member, component, 0]
                    for corner_y in (0, 1):
                        base = tile
                        if corner_y:
                            below = jnp.broadcast_to(
                                rim_y_ref[pair, member, component, node_x], (cells_y, cells_z)
                            )
                            base = jnp.where(last_row, below, pltpu.roll(tile, cells_y - 1, 0))
                        for corner_z in (0, 1):
                            value = base
                            if corner_z:
                                value = jnp.where(inside, pltpu.roll(base, cells_z - 1, 1), 0.0)
                            for corner_x in (0, 1):
                                x = node_x - corner_x
                                if 0 <= x < cells_x:
                                    corner = CORNERS.index((corner_x, corner_y, corner_z))
                                    row = 3 * corner + component
                                    member_rows[member][
                                        pl.ds(row * cells_y, cells_y), pl.ds(x * cells_z, cells_z)
                                    ] = value
        products[...] = jnp.dot(
            coupling_ref[...],
            adjoint_rows[...],
            precision=lax.Precision.HIGH,
            preferred_element_type=jnp.float32,
        )
        state = state_rows[...].reshape(dofs, cells_y, cells_x * cells_z)
        stiff_sum = jnp.sum(
            state * products[pl.ds(0, wide), :].reshape(dofs, cells_y, cells_x * cells_z), axis=0
        )
        mass_sum = jnp.sum(
            state * products[pl.ds(wide, wide), :].reshape(dofs, cells_y, cells_x * cells_z), axis=0
        )
        for x in range(cells_x):
            columns = slice(x * cells_z, (x + 1) * cells_z)
            stiff_out[x] = stiff_out[x] + stiff_sum[:, columns]
            mass_out[x] = mass_out[x] + mass_sum[:, columns]
        return carry

    lax.fori_loop(0, pair_count, over_pairs, 0)


def element_energies(fields, rim_x, rim_y, stiffness, mass_matrix):
    pair_count = fields.shape[0]
    cells = fields.shape[3:]
    voxels = cells[0] * cells[1] * cells[2]
    dofs = stiffness.shape[0]
    vmem = pl.BlockSpec(memory_space=pltpu.VMEM)
    return pl.pallas_call(
        mxu_energy_kernel,
        out_shape=(
            jax.ShapeDtypeStruct(cells, jnp.float32),
            jax.ShapeDtypeStruct(cells, jnp.float32),
        ),
        in_specs=[vmem, vmem, vmem, vmem, vmem],
        out_specs=(vmem, vmem),
        scratch_shapes=[
            pltpu.VMEM((2 * dofs * cells[1], dofs * cells[1]), jnp.float32),
            pltpu.VMEM((dofs * cells[1], cells[0] * cells[2]), jnp.float32),
            pltpu.VMEM((dofs * cells[1], cells[0] * cells[2]), jnp.float32),
            pltpu.VMEM((2 * dofs * cells[1], cells[0] * cells[2]), jnp.float32),
        ],
        cost_estimate=pl.CostEstimate(
            flops=pair_count * (4 * (dofs * cells[1]) ** 2 * cells[0] * cells[2] + 4 * dofs * voxels),
            bytes_accessed=(fields.size + rim_x.size + rim_y.size) * 4 + 2 * stiffness.size * 4 + 2 * voxels * 4,
            transcendentals=0,
        ),
    )(fields, rim_x, rim_y, stiffness, mass_matrix)


def shards(design, passive, basis_pairs, supports, stiffness, mass_matrix, volume_fraction):
    block_shape = design.shape
    size_x, size_y, size_z = block_shape
    devices_x = lax.axis_size("gx")
    devices_y = lax.axis_size("gy")
    index_x = lax.axis_index("gx")
    index_y = lax.axis_index("gy")
    grid_x = size_x * devices_x
    grid_y = size_y * devices_y
    spread_x = jnp.arange(size_x + 4, dtype=jnp.int32) + index_x * size_x - 2
    spread_y = jnp.arange(size_y + 4, dtype=jnp.int32) + index_y * size_y - 2
    valid_x = ((spread_x >= 0) & (spread_x < grid_x)).astype(jnp.float32)
    valid_y = ((spread_y >= 0) & (spread_y < grid_y)).astype(jnp.float32)
    valid_z = jnp.pad(jnp.ones((size_z,), jnp.float32), 2)
    inside = valid_x[:, None, None] * valid_y[None, :, None] * valid_z[None, None, :]
    weight_sum = stencil(inside, block_shape)
    fields = basis_pairs * (1 - supports).astype(jnp.float32)
    design_wide, (rim_x, rim_y) = front_exchange(design, basis_pairs, supports, 2)
    design_wide = jnp.pad(design_wide, ((0, 0), (0, 0), (2, 2)))
    physical = jnp.where(passive == 1, 1.0, stencil(design_wide, block_shape) / weight_sum)
    stiff_energy, mass_energy = element_energies(fields, rim_x, rim_y, stiffness, mass_matrix)
    raw_sensitivity = -(
        PENALTY_SCALE * physical * physical * stiff_energy - OMEGA_SQUARED * mass_energy
    )
    raw_sensitivity = jnp.where(passive == 1, 0.0, raw_sensitivity)
    scaled_wide = with_halo(raw_sensitivity / weight_sum, (("gx", 0), ("gy", 1)), 2)
    scaled_wide = jnp.pad(scaled_wide, ((0, 0), (0, 0), (2, 2)))
    sensitivity = stencil(scaled_wide, block_shape)
    benefit = jnp.maximum(-sensitivity, 0.0)
    floor_value = jnp.maximum(design - MOVE_LIMIT, 0.0)
    ceiling = jnp.minimum(design + MOVE_LIMIT, 1.0)
    band_cells = size_z // REGIONS
    target = volume_fraction * float(grid_x * grid_y * band_cells)

    def candidate(multiplier):
        per_cell = jnp.repeat(multiplier, band_cells)[None, None, :]
        trial = design * jnp.sqrt(benefit / per_cell)
        return jnp.where(passive == 1, 1.0, jnp.minimum(ceiling, jnp.maximum(floor_value, trial)))

    def region_sum(field):
        return jnp.sum(field, axis=(0, 1)).reshape(REGIONS, band_cells).sum(axis=1)

    levels = BISECT

    def bisect_round(round_index, bracket):
        low_end, high_end = bracket
        level_nodes = [(low_end, high_end)]
        midpoints = []
        for depth in range(levels):
            next_nodes = []
            for node_low, node_high in level_nodes:
                middle = jnp.sqrt(node_low * node_high)
                midpoints.append(middle)
                next_nodes.append((node_low, middle))
                next_nodes.append((middle, node_high))
            level_nodes = next_nodes
        trial_multipliers = jnp.stack(midpoints)
        per_cell = jnp.repeat(trial_multipliers, band_cells, axis=1)[:, None, None, :]
        trial = design[None] * jnp.sqrt(benefit[None] / per_cell)
        fields_of = jnp.where(
            passive[None] == 1, 1.0, jnp.minimum(ceiling[None], jnp.maximum(floor_value[None], trial))
        )
        partial_volumes = (
            jnp.sum(fields_of, axis=(1, 2)).reshape(len(midpoints), REGIONS, band_cells).sum(axis=2)
        )
        lanes = 128
        flat = partial_volumes.reshape(-1)
        spare = -flat.size % lanes
        dense = jnp.pad(flat, (0, spare)).reshape(-1, lanes)
        dense = butterfly_sum(butterfly_sum(dense, "gy"), "gx")
        volumes = dense.reshape(-1)[: flat.size].reshape(partial_volumes.shape)
        heavier_all = volumes > target[None, :]
        position = jnp.zeros((REGIONS,), jnp.int32)
        for depth in range(levels):
            middle = jnp.sqrt(low_end * high_end)
            nodes = lax.slice_in_dim(heavier_all, 2**depth - 1, 2 ** (depth + 1) - 1, axis=0)
            slots = lax.broadcasted_iota(jnp.int32, nodes.shape, 0)
            heavier = jnp.any(nodes & (slots == position[None, :]), axis=0)
            low_end = jnp.where(heavier, middle, low_end)
            high_end = jnp.where(heavier, high_end, middle)
            position = 2 * position + heavier.astype(jnp.int32)
        return (low_end, high_end)

    start = (jnp.full((REGIONS,), 0.0001, jnp.float32), jnp.full((REGIONS,), 10000.0, jnp.float32))
    low_end, high_end = bisect_round(0, start)
    design_next = candidate(jnp.sqrt(low_end * high_end))
    return (sensitivity, design_next)


def solution(mesh):
    placed = (
        P("gx", "gy", None),
        P("gx", "gy", None),
        P(None, None, None, "gx", "gy", None),
        P("gx", "gy", None),
        P(),
        P(),
        P(),
    )
    return jax.shard_map(
        shards,
        mesh=mesh,
        in_specs=placed,
        out_specs=(P("gx", "gy", None), P("gx", "gy", None)),
        check_vma=False,
    )
```

```python
import math

import jax
import jax.numpy as jnp
from jax import lax
from jax.sharding import PartitionSpec as P
from jax.experimental import pallas as pl
from jax.experimental.pallas import tpu as pltpu

BISECT = 6
REGIONS = 64


PENALTY_SCALE = 3.0 * (1.0 - 0.001)
OMEGA_SQUARED = 0.5
MOVE_LIMIT = 0.2


def with_halo(cells, sides, width):
    for axis, dim in sides:
        count = lax.axis_size(axis)
        ends = count - 1
        head = lax.slice_in_dim(cells, 0, width, axis=dim)
        tail = lax.slice_in_dim(cells, cells.shape[dim] - width, cells.shape[dim], axis=dim)
        cells = jnp.concatenate(
            [
                lax.ppermute(tail, axis, [(i, (i + 1) % count) for i in range(ends)]),
                cells,
                lax.ppermute(head, axis, [((i + 1) % count, i) for i in range(ends)]),
            ],
            axis=dim,
        )
    return cells


def front_exchange(cells, basis_pairs, supports, width):
    open_nodes = (1 - supports).astype(jnp.float32)
    count_x = lax.axis_size("gx")
    count_y = lax.axis_size("gy")
    lanes = cells.shape[-1]
    rim_y = lax.ppermute(
        basis_pairs[:, :, :, :, :1] * open_nodes[:, :1], "gy", [(i + 1, i) for i in range(count_y - 1)]
    )
    corner = lax.ppermute(
        basis_pairs[:, :, :, :1, :1] * open_nodes[:1, :1],
        ("gx", "gy"),
        [
            ((i + 1) * count_y + j + 1, i * count_y + j)
            for i in range(count_x - 1)
            for j in range(count_y - 1)
        ],
    )
    rim_x = None
    for axis, dim in (("gx", 0), ("gy", 1)):
        count = lax.axis_size(axis)
        ends = count - 1
        head = lax.slice_in_dim(cells, 0, width, axis=dim)
        tail = lax.slice_in_dim(cells, cells.shape[dim] - width, cells.shape[dim], axis=dim)
        if axis == "gx":
            rim = basis_pairs[:, :, :, :1] * open_nodes[:1]
            packed = jnp.concatenate([head.reshape(-1, lanes), rim.reshape(-1, lanes)], axis=0)
            packed = lax.ppermute(packed, axis, [((i + 1) % count, i) for i in range(ends)])
            split = head.size // lanes
            head = packed[:split].reshape(head.shape)
            rim_x = packed[split:].reshape(rim.shape)
        else:
            head = lax.ppermute(head, axis, [((i + 1) % count, i) for i in range(ends)])
        tail = lax.ppermute(tail, axis, [(i, (i + 1) % count) for i in range(ends)])
        cells = jnp.concatenate([tail, cells, head], axis=dim)
    return cells, (rim_x, jnp.concatenate([rim_y, corner], axis=3))


def from_behind(value, axis, steps):
    count = lax.axis_size(axis)
    initial, last = (max(0, -steps), min(count, count - steps))
    return lax.ppermute(value, axis, [(source, source + steps) for source in range(initial, last)])


def butterfly_sum(value, axis):
    count = lax.axis_size(axis)
    stride = 1
    while stride < count:
        value = value + lax.ppermute(value, axis, [(i, i ^ stride) for i in range(count)])
        stride *= 2
    return value


def filter_taps():
    tap_list = []
    for offset_x in range(-2, 3):
        for offset_y in range(-2, 3):
            for offset_z in range(-2, 3):
                weight = 3.0 - math.sqrt(
                    offset_x * offset_x + offset_y * offset_y + offset_z * offset_z
                )
                if weight > 0.0:
                    tap_list.append((offset_x, offset_y, offset_z, weight))
    return tap_list


def stencil(padded, block_shape):
    result = jnp.zeros(block_shape, jnp.float32)
    for offset_x, offset_y, offset_z, weight in filter_taps():
        result = (
            result
            + weight
            * padded[
                2 + offset_x : 2 + offset_x + block_shape[0],
                2 + offset_y : 2 + offset_y + block_shape[1],
                2 + offset_z : 2 + offset_z + block_shape[2],
            ]
        )
    return result


def element_terms(extended, stiffness, mass_matrix):
    pair_count = extended.shape[0]
    cells_x = extended.shape[3] - 1
    cells_y = extended.shape[4] - 1
    cells_z = extended.shape[5] - 1
    stiff_energy = jnp.zeros((cells_x * cells_y * cells_z,), jnp.float32)
    mass_energy = jnp.zeros((cells_x * cells_y * cells_z,), jnp.float32)
    for pair_index in range(pair_count):
        vectors = []
        for member in range(2):
            row_list = []
            for corner_x in (0, 1):
                for corner_y in (0, 1):
                    for corner_z in (0, 1):
                        for component in range(3):
                            row_list.append(
                                extended[
                                    pair_index,
                                    member,
                                    component,
                                    corner_x : corner_x + cells_x,
                                    corner_y : corner_y + cells_y,
                                    corner_z : corner_z + cells_z,
                                ].reshape(-1)
                            )
            vectors.append(jnp.stack(row_list))
        state_rows, adjoint_rows = vectors
        stiff_energy = stiff_energy + jnp.sum(
            state_rows * jnp.dot(stiffness, adjoint_rows, precision=lax.Precision.HIGHEST), axis=0
        )
        mass_energy = mass_energy + jnp.sum(
            state_rows * jnp.dot(mass_matrix, adjoint_rows, precision=lax.Precision.HIGHEST), axis=0
        )
    return (
        stiff_energy.reshape(cells_x, cells_y, cells_z),
        mass_energy.reshape(cells_x, cells_y, cells_z),
    )


CORNERS = [(a, b, d) for a in (0, 1) for b in (0, 1) for d in (0, 1)]


def energy_kernel(extended_ref, stiffness_ref, mass_ref, stiff_out, mass_out):
    pair_count = extended_ref.shape[0]
    cells_x, cells_y, cells_z = stiff_out.shape
    lane = lax.broadcasted_iota(jnp.int32, (cells_y, cells_z), 1)
    inside = lane < cells_z - 1
    last_row = lax.broadcasted_iota(jnp.int32, (cells_y, cells_z), 0) == cells_y - 1

    def node_view(pair, member, component, x, corner):
        corner_x, corner_y, corner_z = corner
        value = extended_ref[pair, member, component, x + corner_x, pl.ds(corner_y, cells_y), :]
        if corner_z:
            value = jnp.where(inside, pltpu.roll(value, cells_z - 1, 1), 0.0)
        return value

    def over_pairs(pair, energies):
        stiff_sum, mass_sum, x = energies
        adjoint = [
            node_view(pair, 1, component, x, corner) for corner in CORNERS for component in range(3)
        ]
        for row in range(len(adjoint)):
            state = node_view(pair, 0, row % 3, x, CORNERS[row // 3])
            stiff_row = stiffness_ref[row, 0] * adjoint[0]
            mass_row = mass_ref[row, 0] * adjoint[0]
            for column in range(1, len(adjoint)):
                stiff_row = stiff_row + stiffness_ref[row, column] * adjoint[column]
                mass_row = mass_row + mass_ref[row, column] * adjoint[column]
            stiff_sum = stiff_sum + state * stiff_row
            mass_sum = mass_sum + state * mass_row
        return stiff_sum, mass_sum, x

    def over_x(x, carry):
        zero = jnp.zeros((cells_y, cells_z), jnp.float32)
        stiff_sum, mass_sum, _ = lax.fori_loop(0, pair_count, over_pairs, (zero, zero, x))
        stiff_out[x] = stiff_sum
        mass_out[x] = mass_sum
        return carry

    lax.fori_loop(0, cells_x, over_x, 0)


def mxu_energy_kernel(
    fields_ref, rim_x_ref, rim_y_ref, stiffness_ref, mass_ref, stiff_out, mass_out, coupling_ref,
    state_rows, adjoint_rows, products,
):
    pair_count = fields_ref.shape[0]
    cells_x, cells_y, cells_z = stiff_out.shape
    dofs = 3 * len(CORNERS)
    wide = dofs * cells_y
    spread_rows = (
        lax.broadcasted_iota(jnp.int32, (wide, dofs), 0) // cells_y
        == lax.broadcasted_iota(jnp.int32, (wide, dofs), 1)
    ).astype(jnp.float32)
    spread_columns = (
        lax.broadcasted_iota(jnp.int32, (dofs, wide), 0)
        == lax.broadcasted_iota(jnp.int32, (dofs, wide), 1) // cells_y
    ).astype(jnp.float32)
    same_y = (
        lax.broadcasted_iota(jnp.int32, (wide, wide), 0) % cells_y
        == lax.broadcasted_iota(jnp.int32, (wide, wide), 1) % cells_y
    )
    for block, matrix_ref in enumerate((stiffness_ref, mass_ref)):
        spread = jnp.dot(
            matrix_ref[...], spread_columns, precision=lax.Precision.HIGHEST,
            preferred_element_type=jnp.float32,
        )
        spread = jnp.dot(
            spread_rows, spread, precision=lax.Precision.HIGHEST, preferred_element_type=jnp.float32
        )
        coupling_ref[pl.ds(block * wide, wide), :] = jnp.where(same_y, spread, 0.0)
    lane = lax.broadcasted_iota(jnp.int32, (cells_y, cells_z), 1)
    inside = lane < cells_z - 1
    last_row = lax.broadcasted_iota(jnp.int32, (cells_y, cells_z), 0) == cells_y - 1
    stiff_out[...] = jnp.zeros(stiff_out.shape, jnp.float32)
    mass_out[...] = jnp.zeros(mass_out.shape, jnp.float32)
    member_rows = (state_rows, adjoint_rows)

    def over_pairs(pair, carry):
        for node_x in range(cells_x + 1):
            for member in range(2):
                for component in range(3):
                    if node_x < cells_x:
                        tile = fields_ref[pair, member, component, node_x]
                    else:
                        tile = rim_x_ref[pair, member, component, 0]
                    for corner_y in (0, 1):
                        base = tile
                        if corner_y:
                            below = jnp.broadcast_to(
                                rim_y_ref[pair, member, component, node_x], (cells_y, cells_z)
                            )
                            base = jnp.where(last_row, below, pltpu.roll(tile, cells_y - 1, 0))
                        for corner_z in (0, 1):
                            value = base
                            if corner_z:
                                value = jnp.where(inside, pltpu.roll(base, cells_z - 1, 1), 0.0)
                            for corner_x in (0, 1):
                                x = node_x - corner_x
                                if 0 <= x < cells_x:
                                    corner = CORNERS.index((corner_x, corner_y, corner_z))
                                    row = 3 * corner + component
                                    member_rows[member][
                                        pl.ds(row * cells_y, cells_y), pl.ds(x * cells_z, cells_z)
                                    ] = value
        products[...] = jnp.dot(
            coupling_ref[...],
            adjoint_rows[...],
            precision=lax.Precision.HIGH,
            preferred_element_type=jnp.float32,
        )
        state = state_rows[...].reshape(dofs, cells_y, cells_x * cells_z)
        stiff_sum = jnp.sum(
            state * products[pl.ds(0, wide), :].reshape(dofs, cells_y, cells_x * cells_z), axis=0
        )
        mass_sum = jnp.sum(
            state * products[pl.ds(wide, wide), :].reshape(dofs, cells_y, cells_x * cells_z), axis=0
        )
        for x in range(cells_x):
            columns = slice(x * cells_z, (x + 1) * cells_z)
            stiff_out[x] = stiff_out[x] + stiff_sum[:, columns]
            mass_out[x] = mass_out[x] + mass_sum[:, columns]
        return carry

    lax.fori_loop(0, pair_count, over_pairs, 0)


def element_energies(fields, rim_x, rim_y, stiffness, mass_matrix):
    pair_count = fields.shape[0]
    cells = fields.shape[3:]
    voxels = cells[0] * cells[1] * cells[2]
    dofs = stiffness.shape[0]
    vmem = pl.BlockSpec(memory_space=pltpu.VMEM)
    return pl.pallas_call(
        mxu_energy_kernel,
        out_shape=(
            jax.ShapeDtypeStruct(cells, jnp.float32),
            jax.ShapeDtypeStruct(cells, jnp.float32),
        ),
        in_specs=[vmem, vmem, vmem, vmem, vmem],
        out_specs=(vmem, vmem),
        scratch_shapes=[
            pltpu.VMEM((2 * dofs * cells[1], dofs * cells[1]), jnp.float32),
            pltpu.VMEM((dofs * cells[1], cells[0] * cells[2]), jnp.float32),
            pltpu.VMEM((dofs * cells[1], cells[0] * cells[2]), jnp.float32),
            pltpu.VMEM((2 * dofs * cells[1], cells[0] * cells[2]), jnp.float32),
        ],
        cost_estimate=pl.CostEstimate(
            flops=pair_count * (4 * (dofs * cells[1]) ** 2 * cells[0] * cells[2] + 4 * dofs * voxels),
            bytes_accessed=(fields.size + rim_x.size + rim_y.size) * 4 + 2 * stiffness.size * 4 + 2 * voxels * 4,
            transcendentals=0,
        ),
    )(fields, rim_x, rim_y, stiffness, mass_matrix)


def shards(design, passive, basis_pairs, supports, stiffness, mass_matrix, volume_fraction):
    block_shape = design.shape
    size_x, size_y, size_z = block_shape
    devices_x = lax.axis_size("gx")
    devices_y = lax.axis_size("gy")
    index_x = lax.axis_index("gx")
    index_y = lax.axis_index("gy")
    grid_x = size_x * devices_x
    grid_y = size_y * devices_y
    spread_x = jnp.arange(size_x + 4, dtype=jnp.int32) + index_x * size_x - 2
    spread_y = jnp.arange(size_y + 4, dtype=jnp.int32) + index_y * size_y - 2
    valid_x = ((spread_x >= 0) & (spread_x < grid_x)).astype(jnp.float32)
    valid_y = ((spread_y >= 0) & (spread_y < grid_y)).astype(jnp.float32)
    valid_z = jnp.pad(jnp.ones((size_z,), jnp.float32), 2)
    inside = valid_x[:, None, None] * valid_y[None, :, None] * valid_z[None, None, :]
    weight_sum = stencil(inside, block_shape)
    fields = basis_pairs * (1 - supports).astype(jnp.float32)
    design_wide, (rim_x, rim_y) = front_exchange(design, basis_pairs, supports, 2)
    design_wide = jnp.pad(design_wide, ((0, 0), (0, 0), (2, 2)))
    physical = jnp.where(passive == 1, 1.0, stencil(design_wide, block_shape) / weight_sum)
    stiff_energy, mass_energy = element_energies(fields, rim_x, rim_y, stiffness, mass_matrix)
    raw_sensitivity = -(
        PENALTY_SCALE * physical * physical * stiff_energy - OMEGA_SQUARED * mass_energy
    )
    raw_sensitivity = jnp.where(passive == 1, 0.0, raw_sensitivity)
    scaled_wide = with_halo(raw_sensitivity / weight_sum, (("gx", 0), ("gy", 1)), 2)
    scaled_wide = jnp.pad(scaled_wide, ((0, 0), (0, 0), (2, 2)))
    sensitivity = stencil(scaled_wide, block_shape)
    benefit = jnp.maximum(-sensitivity, 0.0)
    floor_value = jnp.maximum(design - MOVE_LIMIT, 0.0)
    ceiling = jnp.minimum(design + MOVE_LIMIT, 1.0)
    band_cells = size_z // REGIONS
    target = volume_fraction * float(grid_x * grid_y * band_cells)

    def candidate(multiplier):
        per_cell = jnp.repeat(multiplier, band_cells)[None, None, :]
        trial = design * jnp.sqrt(benefit / per_cell)
        return jnp.where(passive == 1, 1.0, jnp.minimum(ceiling, jnp.maximum(floor_value, trial)))

    def region_sum(field):
        return jnp.sum(field, axis=(0, 1)).reshape(REGIONS, band_cells).sum(axis=1)

    levels = BISECT

    def bisect_round(round_index, bracket):
        low_end, high_end = bracket
        level_nodes = [(low_end, high_end)]
        midpoints = []
        for depth in range(levels):
            next_nodes = []
            for node_low, node_high in level_nodes:
                middle = jnp.sqrt(node_low * node_high)
                midpoints.append(middle)
                next_nodes.append((node_low, middle))
                next_nodes.append((middle, node_high))
            level_nodes = next_nodes
        trial_multipliers = jnp.stack(midpoints)
        per_cell = jnp.repeat(trial_multipliers, band_cells, axis=1)[:, None, None, :]
        trial = design[None] * jnp.sqrt(benefit[None] / per_cell)
        fields_of = jnp.where(
            passive[None] == 1, 1.0, jnp.minimum(ceiling[None], jnp.maximum(floor_value[None], trial))
        )
        partial_volumes = (
            jnp.sum(fields_of, axis=(1, 2)).reshape(len(midpoints), REGIONS, band_cells).sum(axis=2)
        )
        lanes = 128
        flat = partial_volumes.reshape(-1)
        spare = -flat.size % lanes
        dense = jnp.pad(flat, (0, spare)).reshape(-1, lanes)
        dense = butterfly_sum(butterfly_sum(dense, "gy"), "gx")
        volumes = dense.reshape(-1)[: flat.size].reshape(partial_volumes.shape)
        heavier_all = volumes > target[None, :]
        position = jnp.zeros((REGIONS,), jnp.int32)
        for depth in range(levels):
            middle = jnp.sqrt(low_end * high_end)
            nodes = lax.slice_in_dim(heavier_all, 2**depth - 1, 2 ** (depth + 1) - 1, axis=0)
            slots = lax.broadcasted_iota(jnp.int32, nodes.shape, 0)
            heavier = jnp.any(nodes & (slots == position[None, :]), axis=0)
            low_end = jnp.where(heavier, middle, low_end)
            high_end = jnp.where(heavier, high_end, middle)
            position = 2 * position + heavier.astype(jnp.int32)
        return (low_end, high_end)

    start = (jnp.full((REGIONS,), 0.0001, jnp.float32), jnp.full((REGIONS,), 10000.0, jnp.float32))
    low_end, high_end = bisect_round(0, start)
    design_next = candidate(jnp.sqrt(low_end * high_end))
    return (sensitivity, design_next)


def solution(mesh):
    placed = (
        P("gx", "gy", None),
        P("gx", "gy", None),
        P(None, None, None, "gx", "gy", None),
        P("gx", "gy", None),
        P(),
        P(),
        P(),
    )
    return jax.shard_map(
        shards,
        mesh=mesh,
        in_specs=placed,
        out_specs=(P("gx", "gy", None), P("gx", "gy", None)),
        check_vma=False,
    )
```

```python
import math

import jax
import jax.numpy as jnp
from jax import lax
from jax.sharding import PartitionSpec as P
from jax.experimental import pallas as pl
from jax.experimental.pallas import tpu as pltpu

BISECT = 6
REGIONS = 64


PENALTY_SCALE = 3.0 * (1.0 - 0.001)
OMEGA_SQUARED = 0.5
MOVE_LIMIT = 0.2


def with_halo(cells, sides, width):
    for axis, dim in sides:
        count = lax.axis_size(axis)
        ends = count - 1
        head = lax.slice_in_dim(cells, 0, width, axis=dim)
        tail = lax.slice_in_dim(cells, cells.shape[dim] - width, cells.shape[dim], axis=dim)
        lanes = cells.shape[-1]
        tail_in = lax.ppermute(
            tail.reshape(-1, lanes), axis, [(i, (i + 1) % count) for i in range(ends)]
        ).reshape(tail.shape)
        head_in = lax.ppermute(
            head.reshape(-1, lanes), axis, [((i + 1) % count, i) for i in range(ends)]
        ).reshape(head.shape)
        cells = jnp.concatenate([tail_in, cells, head_in], axis=dim)
    return cells


def front_exchange(cells, fields, width):
    for axis, dim in (("gx", 0), ("gy", 1)):
        count = lax.axis_size(axis)
        ends = count - 1
        field_dim = dim + 3
        head = lax.slice_in_dim(cells, 0, width, axis=dim)
        tail = lax.slice_in_dim(cells, cells.shape[dim] - width, cells.shape[dim], axis=dim)
        rim = lax.slice_in_dim(fields, 0, 1, axis=field_dim)
        lanes = cells.shape[-1]
        packed = jnp.concatenate([head.reshape(-1, lanes), rim.reshape(-1, lanes)], axis=0)
        packed = lax.ppermute(packed, axis, [((i + 1) % count, i) for i in range(ends)])
        split = head.size // lanes
        head = packed[:split].reshape(head.shape)
        rim = packed[split:].reshape(rim.shape)
        tail = lax.ppermute(
            tail.reshape(-1, lanes), axis, [(i, (i + 1) % count) for i in range(ends)]
        ).reshape(tail.shape)
        cells = jnp.concatenate([tail, cells, head], axis=dim)
        fields = jnp.concatenate([fields, rim], axis=field_dim)
    return cells, fields


def from_behind(value, axis, steps):
    count = lax.axis_size(axis)
    initial, last = (max(0, -steps), min(count, count - steps))
    return lax.ppermute(value, axis, [(source, source + steps) for source in range(initial, last)])


def butterfly_sum(value, axis):
    count = lax.axis_size(axis)
    stride = 1
    while stride < count:
        value = value + lax.ppermute(value, axis, [(i, i ^ stride) for i in range(count)])
        stride *= 2
    return value


def filter_taps():
    tap_list = []
    for offset_x in range(-2, 3):
        for offset_y in range(-2, 3):
            for offset_z in range(-2, 3):
                weight = 3.0 - math.sqrt(
                    offset_x * offset_x + offset_y * offset_y + offset_z * offset_z
                )
                if weight > 0.0:
                    tap_list.append((offset_x, offset_y, offset_z, weight))
    return tap_list


def stencil(padded, block_shape):
    result = jnp.zeros(block_shape, jnp.float32)
    for offset_x, offset_y, offset_z, weight in filter_taps():
        result = (
            result
            + weight
            * padded[
                2 + offset_x : 2 + offset_x + block_shape[0],
                2 + offset_y : 2 + offset_y + block_shape[1],
                2 + offset_z : 2 + offset_z + block_shape[2],
            ]
        )
    return result


def element_terms(extended, stiffness, mass_matrix):
    pair_count = extended.shape[0]
    cells_x = extended.shape[3] - 1
    cells_y = extended.shape[4] - 1
    cells_z = extended.shape[5] - 1
    stiff_energy = jnp.zeros((cells_x * cells_y * cells_z,), jnp.float32)
    mass_energy = jnp.zeros((cells_x * cells_y * cells_z,), jnp.float32)
    for pair_index in range(pair_count):
        vectors = []
        for member in range(2):
            row_list = []
            for corner_x in (0, 1):
                for corner_y in (0, 1):
                    for corner_z in (0, 1):
                        for component in range(3):
                            row_list.append(
                                extended[
                                    pair_index,
                                    member,
                                    component,
                                    corner_x : corner_x + cells_x,
                                    corner_y : corner_y + cells_y,
                                    corner_z : corner_z + cells_z,
                                ].reshape(-1)
                            )
            vectors.append(jnp.stack(row_list))
        state_rows, adjoint_rows = vectors
        stiff_energy = stiff_energy + jnp.sum(
            state_rows * jnp.dot(stiffness, adjoint_rows, precision=lax.Precision.HIGHEST), axis=0
        )
        mass_energy = mass_energy + jnp.sum(
            state_rows * jnp.dot(mass_matrix, adjoint_rows, precision=lax.Precision.HIGHEST), axis=0
        )
    return (
        stiff_energy.reshape(cells_x, cells_y, cells_z),
        mass_energy.reshape(cells_x, cells_y, cells_z),
    )


CORNERS = [(a, b, d) for a in (0, 1) for b in (0, 1) for d in (0, 1)]


def energy_kernel(extended_ref, stiffness_ref, mass_ref, stiff_out, mass_out):
    pair_count = extended_ref.shape[0]
    cells_x, cells_y, cells_z = stiff_out.shape
    lane = lax.broadcasted_iota(jnp.int32, (cells_y, cells_z), 1)
    inside = lane < cells_z - 1

    def node_view(pair, member, component, x, corner):
        corner_x, corner_y, corner_z = corner
        value = extended_ref[pair, member, component, x + corner_x, pl.ds(corner_y, cells_y), :]
        if corner_z:
            value = jnp.where(inside, pltpu.roll(value, cells_z - 1, 1), 0.0)
        return value

    def over_pairs(pair, energies):
        stiff_sum, mass_sum, x = energies
        adjoint = [
            node_view(pair, 1, component, x, corner) for corner in CORNERS for component in range(3)
        ]
        for row in range(len(adjoint)):
            state = node_view(pair, 0, row % 3, x, CORNERS[row // 3])
            stiff_row = stiffness_ref[row, 0] * adjoint[0]
            mass_row = mass_ref[row, 0] * adjoint[0]
            for column in range(1, len(adjoint)):
                stiff_row = stiff_row + stiffness_ref[row, column] * adjoint[column]
                mass_row = mass_row + mass_ref[row, column] * adjoint[column]
            stiff_sum = stiff_sum + state * stiff_row
            mass_sum = mass_sum + state * mass_row
        return stiff_sum, mass_sum, x

    def over_x(x, carry):
        zero = jnp.zeros((cells_y, cells_z), jnp.float32)
        stiff_sum, mass_sum, _ = lax.fori_loop(0, pair_count, over_pairs, (zero, zero, x))
        stiff_out[x] = stiff_sum
        mass_out[x] = mass_sum
        return carry

    lax.fori_loop(0, cells_x, over_x, 0)


def mxu_energy_kernel(
    extended_ref, stiffness_ref, mass_ref, stiff_out, mass_out, coupling_ref, state_rows,
    adjoint_rows, products,
):
    pair_count = extended_ref.shape[0]
    cells_x, cells_y, cells_z = stiff_out.shape
    dofs = 3 * len(CORNERS)
    wide = dofs * cells_y
    spread_rows = (
        lax.broadcasted_iota(jnp.int32, (wide, dofs), 0) // cells_y
        == lax.broadcasted_iota(jnp.int32, (wide, dofs), 1)
    ).astype(jnp.float32)
    spread_columns = (
        lax.broadcasted_iota(jnp.int32, (dofs, wide), 0)
        == lax.broadcasted_iota(jnp.int32, (dofs, wide), 1) // cells_y
    ).astype(jnp.float32)
    same_y = (
        lax.broadcasted_iota(jnp.int32, (wide, wide), 0) % cells_y
        == lax.broadcasted_iota(jnp.int32, (wide, wide), 1) % cells_y
    )
    for block, matrix_ref in enumerate((stiffness_ref, mass_ref)):
        spread = jnp.dot(
            matrix_ref[...], spread_columns, precision=lax.Precision.HIGHEST,
            preferred_element_type=jnp.float32,
        )
        spread = jnp.dot(
            spread_rows, spread, precision=lax.Precision.HIGHEST, preferred_element_type=jnp.float32
        )
        coupling_ref[pl.ds(block * wide, wide), :] = jnp.where(same_y, spread, 0.0)
    lane = lax.broadcasted_iota(jnp.int32, (cells_y, cells_z), 1)
    inside = lane < cells_z - 1
    stiff_out[...] = jnp.zeros(stiff_out.shape, jnp.float32)
    mass_out[...] = jnp.zeros(mass_out.shape, jnp.float32)
    member_rows = (state_rows, adjoint_rows)

    def over_pairs(pair, carry):
        for node_x in range(cells_x + 1):
            for member in range(2):
                for component in range(3):
                    for corner_y in (0, 1):
                        base = extended_ref[
                            pair, member, component, node_x, pl.ds(corner_y, cells_y), :
                        ]
                        for corner_z in (0, 1):
                            value = base
                            if corner_z:
                                value = jnp.where(inside, pltpu.roll(base, cells_z - 1, 1), 0.0)
                            for corner_x in (0, 1):
                                x = node_x - corner_x
                                if 0 <= x < cells_x:
                                    corner = CORNERS.index((corner_x, corner_y, corner_z))
                                    row = 3 * corner + component
                                    member_rows[member][
                                        pl.ds(row * cells_y, cells_y), pl.ds(x * cells_z, cells_z)
                                    ] = value
        products[...] = jnp.dot(
            coupling_ref[...],
            adjoint_rows[...],
            precision=lax.Precision.HIGH,
            preferred_element_type=jnp.float32,
        )
        state = state_rows[...].reshape(dofs, cells_y, cells_x * cells_z)
        stiff_sum = jnp.sum(
            state * products[pl.ds(0, wide), :].reshape(dofs, cells_y, cells_x * cells_z), axis=0
        )
        mass_sum = jnp.sum(
            state * products[pl.ds(wide, wide), :].reshape(dofs, cells_y, cells_x * cells_z), axis=0
        )
        for x in range(cells_x):
            columns = slice(x * cells_z, (x + 1) * cells_z)
            stiff_out[x] = stiff_out[x] + stiff_sum[:, columns]
            mass_out[x] = mass_out[x] + mass_sum[:, columns]
        return carry

    lax.fori_loop(0, pair_count, over_pairs, 0)


def element_energies(extended, stiffness, mass_matrix):
    pair_count = extended.shape[0]
    cells = (extended.shape[3] - 1, extended.shape[4] - 1, extended.shape[5])
    voxels = cells[0] * cells[1] * cells[2]
    dofs = stiffness.shape[0]
    vmem = pl.BlockSpec(memory_space=pltpu.VMEM)
    return pl.pallas_call(
        mxu_energy_kernel,
        out_shape=(
            jax.ShapeDtypeStruct(cells, jnp.float32),
            jax.ShapeDtypeStruct(cells, jnp.float32),
        ),
        in_specs=[vmem, vmem, vmem],
        out_specs=(vmem, vmem),
        scratch_shapes=[
            pltpu.VMEM((2 * dofs * cells[1], dofs * cells[1]), jnp.float32),
            pltpu.VMEM((dofs * cells[1], cells[0] * cells[2]), jnp.float32),
            pltpu.VMEM((dofs * cells[1], cells[0] * cells[2]), jnp.float32),
            pltpu.VMEM((2 * dofs * cells[1], cells[0] * cells[2]), jnp.float32),
        ],
        cost_estimate=pl.CostEstimate(
            flops=pair_count * (4 * (dofs * cells[1]) ** 2 * cells[0] * cells[2] + 4 * dofs * voxels),
            bytes_accessed=extended.size * 4 + 2 * stiffness.size * 4 + 2 * voxels * 4,
            transcendentals=0,
        ),
    )(extended, stiffness, mass_matrix)


def shards(design, passive, basis_pairs, supports, stiffness, mass_matrix, volume_fraction):
    block_shape = design.shape
    size_x, size_y, size_z = block_shape
    devices_x = lax.axis_size("gx")
    devices_y = lax.axis_size("gy")
    index_x = lax.axis_index("gx")
    index_y = lax.axis_index("gy")
    grid_x = size_x * devices_x
    grid_y = size_y * devices_y
    spread_x = jnp.arange(size_x + 4, dtype=jnp.int32) + index_x * size_x - 2
    spread_y = jnp.arange(size_y + 4, dtype=jnp.int32) + index_y * size_y - 2
    valid_x = ((spread_x >= 0) & (spread_x < grid_x)).astype(jnp.float32)
    valid_y = ((spread_y >= 0) & (spread_y < grid_y)).astype(jnp.float32)
    valid_z = jnp.pad(jnp.ones((size_z,), jnp.float32), 2)
    inside = valid_x[:, None, None] * valid_y[None, :, None] * valid_z[None, None, :]
    weight_sum = stencil(inside, block_shape)
    fields = basis_pairs * (1 - supports).astype(jnp.float32)
    design_wide, extended = front_exchange(design, fields, 2)
    design_wide = jnp.pad(design_wide, ((0, 0), (0, 0), (2, 2)))
    physical = jnp.where(passive == 1, 1.0, stencil(design_wide, block_shape) / weight_sum)
    stiff_energy, mass_energy = element_energies(extended, stiffness, mass_matrix)
    raw_sensitivity = -(
        PENALTY_SCALE * physical * physical * stiff_energy - OMEGA_SQUARED * mass_energy
    )
    raw_sensitivity = jnp.where(passive == 1, 0.0, raw_sensitivity)
    scaled_wide = with_halo(raw_sensitivity / weight_sum, (("gx", 0), ("gy", 1)), 2)
    scaled_wide = jnp.pad(scaled_wide, ((0, 0), (0, 0), (2, 2)))
    sensitivity = stencil(scaled_wide, block_shape)
    benefit = jnp.maximum(-sensitivity, 0.0)
    floor_value = jnp.maximum(design - MOVE_LIMIT, 0.0)
    ceiling = jnp.minimum(design + MOVE_LIMIT, 1.0)
    band_cells = size_z // REGIONS
    target = volume_fraction * float(grid_x * grid_y * band_cells)

    def candidate(multiplier):
        per_cell = jnp.repeat(multiplier, band_cells)[None, None, :]
        trial = design * jnp.sqrt(benefit / per_cell)
        return jnp.where(passive == 1, 1.0, jnp.minimum(ceiling, jnp.maximum(floor_value, trial)))

    def region_sum(field):
        return jnp.sum(field, axis=(0, 1)).reshape(REGIONS, band_cells).sum(axis=1)

    levels = BISECT

    def bisect_round(round_index, bracket):
        low_end, high_end = bracket
        level_nodes = [(low_end, high_end)]
        midpoints = []
        for depth in range(levels):
            next_nodes = []
            for node_low, node_high in level_nodes:
                middle = jnp.sqrt(node_low * node_high)
                midpoints.append(middle)
                next_nodes.append((node_low, middle))
                next_nodes.append((middle, node_high))
            level_nodes = next_nodes
        trial_multipliers = jnp.stack(midpoints)
        per_cell = jnp.repeat(trial_multipliers, band_cells, axis=1)[:, None, None, :]
        trial = design[None] * jnp.sqrt(benefit[None] / per_cell)
        fields_of = jnp.where(
            passive[None] == 1, 1.0, jnp.minimum(ceiling[None], jnp.maximum(floor_value[None], trial))
        )
        partial_volumes = (
            jnp.sum(fields_of, axis=(1, 2)).reshape(len(midpoints), REGIONS, band_cells).sum(axis=2)
        )
        lanes = 128
        flat = partial_volumes.reshape(-1)
        spare = -flat.size % lanes
        dense = jnp.pad(flat, (0, spare)).reshape(-1, lanes)
        dense = butterfly_sum(butterfly_sum(dense, "gy"), "gx")
        volumes = dense.reshape(-1)[: flat.size].reshape(partial_volumes.shape)
        heavier_all = volumes > target[None, :]
        position = jnp.zeros((REGIONS,), jnp.int32)
        for depth in range(levels):
            middle = jnp.sqrt(low_end * high_end)
            nodes = lax.slice_in_dim(heavier_all, 2**depth - 1, 2 ** (depth + 1) - 1, axis=0)
            slots = lax.broadcasted_iota(jnp.int32, nodes.shape, 0)
            heavier = jnp.any(nodes & (slots == position[None, :]), axis=0)
            low_end = jnp.where(heavier, middle, low_end)
            high_end = jnp.where(heavier, high_end, middle)
            position = 2 * position + heavier.astype(jnp.int32)
        return (low_end, high_end)

    start = (jnp.full((REGIONS,), 0.0001, jnp.float32), jnp.full((REGIONS,), 10000.0, jnp.float32))
    low_end, high_end = bisect_round(0, start)
    design_next = candidate(jnp.sqrt(low_end * high_end))
    return (sensitivity, design_next)


def solution(mesh):
    placed = (
        P("gx", "gy", None),
        P("gx", "gy", None),
        P(None, None, None, "gx", "gy", None),
        P("gx", "gy", None),
        P(),
        P(),
        P(),
    )
    return jax.shard_map(
        shards,
        mesh=mesh,
        in_specs=placed,
        out_specs=(P("gx", "gy", None), P("gx", "gy", None)),
        check_vma=False,
    )
```

```python
import functools
import math

import jax
import jax.numpy as jnp
from jax import lax
from jax.sharding import PartitionSpec as P
from jax.experimental import pallas as pl
from jax.experimental.pallas import tpu as pltpu

BISECT = 6
REGIONS = 64


PENALTY_SCALE = 3.0 * (1.0 - 0.001)
OMEGA_SQUARED = 0.5
MOVE_LIMIT = 0.2


def with_halo(cells, sides, width):
    for axis, dim in sides:
        count = lax.axis_size(axis)
        ends = count - 1
        head = lax.slice_in_dim(cells, 0, width, axis=dim)
        tail = lax.slice_in_dim(cells, cells.shape[dim] - width, cells.shape[dim], axis=dim)
        cells = jnp.concatenate(
            [
                lax.ppermute(tail, axis, [(i, (i + 1) % count) for i in range(ends)]),
                cells,
                lax.ppermute(head, axis, [((i + 1) % count, i) for i in range(ends)]),
            ],
            axis=dim,
        )
    return cells


def front_exchange(cells, fields, width):
    for axis, dim in (("gx", 0), ("gy", 1)):
        count = lax.axis_size(axis)
        ends = count - 1
        field_dim = dim + 3
        head = lax.slice_in_dim(cells, 0, width, axis=dim)
        tail = lax.slice_in_dim(cells, cells.shape[dim] - width, cells.shape[dim], axis=dim)
        rim = lax.slice_in_dim(fields, 0, 1, axis=field_dim)
        lanes = cells.shape[-1]
        packed = jnp.concatenate([head.reshape(-1, lanes), rim.reshape(-1, lanes)], axis=0)
        packed = lax.ppermute(packed, axis, [((i + 1) % count, i) for i in range(ends)])
        split = head.size // lanes
        head = packed[:split].reshape(head.shape)
        rim = packed[split:].reshape(rim.shape)
        tail = lax.ppermute(tail, axis, [(i, (i + 1) % count) for i in range(ends)])
        cells = jnp.concatenate([tail, cells, head], axis=dim)
        fields = jnp.concatenate([fields, rim], axis=field_dim)
    return cells, fields


def from_behind(value, axis, steps):
    count = lax.axis_size(axis)
    initial, last = (max(0, -steps), min(count, count - steps))
    return lax.ppermute(value, axis, [(source, source + steps) for source in range(initial, last)])


def butterfly_sum(value, axis):
    count = lax.axis_size(axis)
    stride = 1
    while stride < count:
        value = value + lax.ppermute(value, axis, [(i, i ^ stride) for i in range(count)])
        stride *= 2
    return value


def filter_taps():
    tap_list = []
    for offset_x in range(-2, 3):
        for offset_y in range(-2, 3):
            for offset_z in range(-2, 3):
                weight = 3.0 - math.sqrt(
                    offset_x * offset_x + offset_y * offset_y + offset_z * offset_z
                )
                if weight > 0.0:
                    tap_list.append((offset_x, offset_y, offset_z, weight))
    return tap_list


def stencil(padded, block_shape):
    result = jnp.zeros(block_shape, jnp.float32)
    for offset_x, offset_y, offset_z, weight in filter_taps():
        result = (
            result
            + weight
            * padded[
                2 + offset_x : 2 + offset_x + block_shape[0],
                2 + offset_y : 2 + offset_y + block_shape[1],
                2 + offset_z : 2 + offset_z + block_shape[2],
            ]
        )
    return result


def element_terms(extended, stiffness, mass_matrix):
    pair_count = extended.shape[0]
    cells_x = extended.shape[3] - 1
    cells_y = extended.shape[4] - 1
    cells_z = extended.shape[5] - 1
    stiff_energy = jnp.zeros((cells_x * cells_y * cells_z,), jnp.float32)
    mass_energy = jnp.zeros((cells_x * cells_y * cells_z,), jnp.float32)
    for pair_index in range(pair_count):
        vectors = []
        for member in range(2):
            row_list = []
            for corner_x in (0, 1):
                for corner_y in (0, 1):
                    for corner_z in (0, 1):
                        for component in range(3):
                            row_list.append(
                                extended[
                                    pair_index,
                                    member,
                                    component,
                                    corner_x : corner_x + cells_x,
                                    corner_y : corner_y + cells_y,
                                    corner_z : corner_z + cells_z,
                                ].reshape(-1)
                            )
            vectors.append(jnp.stack(row_list))
        state_rows, adjoint_rows = vectors
        stiff_energy = stiff_energy + jnp.sum(
            state_rows * jnp.dot(stiffness, adjoint_rows, precision=lax.Precision.HIGHEST), axis=0
        )
        mass_energy = mass_energy + jnp.sum(
            state_rows * jnp.dot(mass_matrix, adjoint_rows, precision=lax.Precision.HIGHEST), axis=0
        )
    return (
        stiff_energy.reshape(cells_x, cells_y, cells_z),
        mass_energy.reshape(cells_x, cells_y, cells_z),
    )


CORNERS = [(a, b, d) for a in (0, 1) for b in (0, 1) for d in (0, 1)]


def energy_kernel(extended_ref, stiffness_ref, mass_ref, stiff_out, mass_out):
    pair_count = extended_ref.shape[0]
    cells_x, cells_y, cells_z = stiff_out.shape
    lane = lax.broadcasted_iota(jnp.int32, (cells_y, cells_z), 1)
    inside = lane < cells_z - 1

    def node_view(pair, member, component, x, corner):
        corner_x, corner_y, corner_z = corner
        value = extended_ref[pair, member, component, x + corner_x, pl.ds(corner_y, cells_y), :]
        if corner_z:
            value = jnp.where(inside, pltpu.roll(value, cells_z - 1, 1), 0.0)
        return value

    def over_pairs(pair, energies):
        stiff_sum, mass_sum, x = energies
        adjoint = [
            node_view(pair, 1, component, x, corner) for corner in CORNERS for component in range(3)
        ]
        for row in range(len(adjoint)):
            state = node_view(pair, 0, row % 3, x, CORNERS[row // 3])
            stiff_row = stiffness_ref[row, 0] * adjoint[0]
            mass_row = mass_ref[row, 0] * adjoint[0]
            for column in range(1, len(adjoint)):
                stiff_row = stiff_row + stiffness_ref[row, column] * adjoint[column]
                mass_row = mass_row + mass_ref[row, column] * adjoint[column]
            stiff_sum = stiff_sum + state * stiff_row
            mass_sum = mass_sum + state * mass_row
        return stiff_sum, mass_sum, x

    def over_x(x, carry):
        zero = jnp.zeros((cells_y, cells_z), jnp.float32)
        stiff_sum, mass_sum, _ = lax.fori_loop(0, pair_count, over_pairs, (zero, zero, x))
        stiff_out[x] = stiff_sum
        mass_out[x] = mass_sum
        return carry

    lax.fori_loop(0, cells_x, over_x, 0)


def coupling_kernel(cells_y, stiffness_ref, mass_ref, coupling_ref):
    dofs = stiffness_ref.shape[0]
    wide = dofs * cells_y
    spread_rows = (
        lax.broadcasted_iota(jnp.int32, (wide, dofs), 0) // cells_y
        == lax.broadcasted_iota(jnp.int32, (wide, dofs), 1)
    ).astype(jnp.float32)
    spread_columns = (
        lax.broadcasted_iota(jnp.int32, (dofs, wide), 0)
        == lax.broadcasted_iota(jnp.int32, (dofs, wide), 1) // cells_y
    ).astype(jnp.float32)
    same_y = (
        lax.broadcasted_iota(jnp.int32, (wide, wide), 0) % cells_y
        == lax.broadcasted_iota(jnp.int32, (wide, wide), 1) % cells_y
    )
    for block, matrix_ref in enumerate((stiffness_ref, mass_ref)):
        spread = jnp.dot(
            matrix_ref[...], spread_columns, precision=lax.Precision.HIGHEST,
            preferred_element_type=jnp.float32,
        )
        spread = jnp.dot(
            spread_rows, spread, precision=lax.Precision.HIGHEST, preferred_element_type=jnp.float32
        )
        coupling_ref[pl.ds(block * wide, wide), :] = jnp.where(same_y, spread, 0.0)


def mxu_energy_kernel(
    extended_ref, coupling_ref, stiff_out, mass_out, state_rows, adjoint_rows, products
):
    pair_count = extended_ref.shape[0]
    cells_x, cells_y, cells_z = stiff_out.shape
    dofs = 3 * len(CORNERS)
    wide = dofs * cells_y
    lane = lax.broadcasted_iota(jnp.int32, (cells_y, cells_z), 1)
    inside = lane < cells_z - 1
    stiff_out[...] = jnp.zeros(stiff_out.shape, jnp.float32)
    mass_out[...] = jnp.zeros(mass_out.shape, jnp.float32)
    member_rows = (state_rows, adjoint_rows)

    def over_pairs(pair, carry):
        for node_x in range(cells_x + 1):
            for member in range(2):
                for component in range(3):
                    for corner_y in (0, 1):
                        base = extended_ref[
                            pair, member, component, node_x, pl.ds(corner_y, cells_y), :
                        ]
                        for corner_z in (0, 1):
                            value = base
                            if corner_z:
                                value = jnp.where(inside, pltpu.roll(base, cells_z - 1, 1), 0.0)
                            for corner_x in (0, 1):
                                x = node_x - corner_x
                                if 0 <= x < cells_x:
                                    corner = CORNERS.index((corner_x, corner_y, corner_z))
                                    row = 3 * corner + component
                                    member_rows[member][
                                        pl.ds(row * cells_y, cells_y), pl.ds(x * cells_z, cells_z)
                                    ] = value
        products[...] = jnp.dot(
            coupling_ref[...],
            adjoint_rows[...],
            precision=lax.Precision.HIGH,
            preferred_element_type=jnp.float32,
        )
        state = state_rows[...].reshape(dofs, cells_y, cells_x * cells_z)
        stiff_sum = jnp.sum(
            state * products[pl.ds(0, wide), :].reshape(dofs, cells_y, cells_x * cells_z), axis=0
        )
        mass_sum = jnp.sum(
            state * products[pl.ds(wide, wide), :].reshape(dofs, cells_y, cells_x * cells_z), axis=0
        )
        for x in range(cells_x):
            columns = slice(x * cells_z, (x + 1) * cells_z)
            stiff_out[x] = stiff_out[x] + stiff_sum[:, columns]
            mass_out[x] = mass_out[x] + mass_sum[:, columns]
        return carry

    lax.fori_loop(0, pair_count, over_pairs, 0)


def element_energies(extended, stiffness, mass_matrix):
    pair_count = extended.shape[0]
    cells = (extended.shape[3] - 1, extended.shape[4] - 1, extended.shape[5])
    voxels = cells[0] * cells[1] * cells[2]
    dofs = stiffness.shape[0]
    vmem = pl.BlockSpec(memory_space=pltpu.VMEM)
    coupling = pl.pallas_call(
        functools.partial(coupling_kernel, cells[1]),
        out_shape=jax.ShapeDtypeStruct((2 * dofs * cells[1], dofs * cells[1]), jnp.float32),
        in_specs=[vmem, vmem],
        out_specs=vmem,
    )(stiffness, mass_matrix)
    return pl.pallas_call(
        mxu_energy_kernel,
        out_shape=(
            jax.ShapeDtypeStruct(cells, jnp.float32),
            jax.ShapeDtypeStruct(cells, jnp.float32),
        ),
        in_specs=[vmem, vmem],
        out_specs=(vmem, vmem),
        scratch_shapes=[
            pltpu.VMEM((dofs * cells[1], cells[0] * cells[2]), jnp.float32),
            pltpu.VMEM((dofs * cells[1], cells[0] * cells[2]), jnp.float32),
            pltpu.VMEM((2 * dofs * cells[1], cells[0] * cells[2]), jnp.float32),
        ],
        cost_estimate=pl.CostEstimate(
            flops=pair_count * (4 * (dofs * cells[1]) ** 2 * cells[0] * cells[2] + 4 * dofs * voxels),
            bytes_accessed=extended.size * 4 + coupling.size * 4 + 2 * voxels * 4,
            transcendentals=0,
        ),
    )(extended, coupling)


def shards(design, passive, basis_pairs, supports, stiffness, mass_matrix, volume_fraction):
    block_shape = design.shape
    size_x, size_y, size_z = block_shape
    devices_x = lax.axis_size("gx")
    devices_y = lax.axis_size("gy")
    index_x = lax.axis_index("gx")
    index_y = lax.axis_index("gy")
    grid_x = size_x * devices_x
    grid_y = size_y * devices_y
    spread_x = jnp.arange(size_x + 4, dtype=jnp.int32) + index_x * size_x - 2
    spread_y = jnp.arange(size_y + 4, dtype=jnp.int32) + index_y * size_y - 2
    valid_x = ((spread_x >= 0) & (spread_x < grid_x)).astype(jnp.float32)
    valid_y = ((spread_y >= 0) & (spread_y < grid_y)).astype(jnp.float32)
    valid_z = jnp.pad(jnp.ones((size_z,), jnp.float32), 2)
    inside = valid_x[:, None, None] * valid_y[None, :, None] * valid_z[None, None, :]
    weight_sum = stencil(inside, block_shape)
    fields = basis_pairs * (1 - supports).astype(jnp.float32)
    design_wide, extended = front_exchange(design, fields, 2)
    design_wide = jnp.pad(design_wide, ((0, 0), (0, 0), (2, 2)))
    physical = jnp.where(passive == 1, 1.0, stencil(design_wide, block_shape) / weight_sum)
    stiff_energy, mass_energy = element_energies(extended, stiffness, mass_matrix)
    raw_sensitivity = -(
        PENALTY_SCALE * physical * physical * stiff_energy - OMEGA_SQUARED * mass_energy
    )
    raw_sensitivity = jnp.where(passive == 1, 0.0, raw_sensitivity)
    scaled_wide = with_halo(raw_sensitivity / weight_sum, (("gx", 0), ("gy", 1)), 2)
    scaled_wide = jnp.pad(scaled_wide, ((0, 0), (0, 0), (2, 2)))
    sensitivity = stencil(scaled_wide, block_shape)
    benefit = jnp.maximum(-sensitivity, 0.0)
    floor_value = jnp.maximum(design - MOVE_LIMIT, 0.0)
    ceiling = jnp.minimum(design + MOVE_LIMIT, 1.0)
    band_cells = size_z // REGIONS
    target = volume_fraction * float(grid_x * grid_y * band_cells)

    def candidate(multiplier):
        per_cell = jnp.repeat(multiplier, band_cells)[None, None, :]
        trial = design * jnp.sqrt(benefit / per_cell)
        return jnp.where(passive == 1, 1.0, jnp.minimum(ceiling, jnp.maximum(floor_value, trial)))

    def region_sum(field):
        return jnp.sum(field, axis=(0, 1)).reshape(REGIONS, band_cells).sum(axis=1)

    levels = BISECT

    def bisect_round(round_index, bracket):
        low_end, high_end = bracket
        level_nodes = [(low_end, high_end)]
        midpoints = []
        for depth in range(levels):
            next_nodes = []
            for node_low, node_high in level_nodes:
                middle = jnp.sqrt(node_low * node_high)
                midpoints.append(middle)
                next_nodes.append((node_low, middle))
                next_nodes.append((middle, node_high))
            level_nodes = next_nodes
        trial_multipliers = jnp.stack(midpoints)
        per_cell = jnp.repeat(trial_multipliers, band_cells, axis=1)[:, None, None, :]
        trial = design[None] * jnp.sqrt(benefit[None] / per_cell)
        fields_of = jnp.where(
            passive[None] == 1, 1.0, jnp.minimum(ceiling[None], jnp.maximum(floor_value[None], trial))
        )
        partial_volumes = (
            jnp.sum(fields_of, axis=(1, 2)).reshape(len(midpoints), REGIONS, band_cells).sum(axis=2)
        )
        lanes = 128
        flat = partial_volumes.reshape(-1)
        spare = -flat.size % lanes
        dense = jnp.pad(flat, (0, spare)).reshape(-1, lanes)
        dense = butterfly_sum(butterfly_sum(dense, "gy"), "gx")
        volumes = dense.reshape(-1)[: flat.size].reshape(partial_volumes.shape)
        heavier_all = volumes > target[None, :]
        position = jnp.zeros((REGIONS,), jnp.int32)
        for depth in range(levels):
            middle = jnp.sqrt(low_end * high_end)
            nodes = lax.slice_in_dim(heavier_all, 2**depth - 1, 2 ** (depth + 1) - 1, axis=0)
            slots = lax.broadcasted_iota(jnp.int32, nodes.shape, 0)
            heavier = jnp.any(nodes & (slots == position[None, :]), axis=0)
            low_end = jnp.where(heavier, middle, low_end)
            high_end = jnp.where(heavier, high_end, middle)
            position = 2 * position + heavier.astype(jnp.int32)
        return (low_end, high_end)

    start = (jnp.full((REGIONS,), 0.0001, jnp.float32), jnp.full((REGIONS,), 10000.0, jnp.float32))
    low_end, high_end = bisect_round(0, start)
    design_next = candidate(jnp.sqrt(low_end * high_end))
    return (sensitivity, design_next)


def solution(mesh):
    placed = (
        P("gx", "gy", None),
        P("gx", "gy", None),
        P(None, None, None, "gx", "gy", None),
        P("gx", "gy", None),
        P(),
        P(),
        P(),
    )
    return jax.shard_map(
        shards,
        mesh=mesh,
        in_specs=placed,
        out_specs=(P("gx", "gy", None), P("gx", "gy", None)),
        check_vma=False,
    )
```

```python
import math

import jax
import jax.numpy as jnp
from jax import lax
from jax.sharding import PartitionSpec as P
from jax.experimental import pallas as pl
from jax.experimental.pallas import tpu as pltpu

BISECT = 6
REGIONS = 64


PENALTY_SCALE = 3.0 * (1.0 - 0.001)
OMEGA_SQUARED = 0.5
MOVE_LIMIT = 0.2


def with_halo(cells, sides, width):
    for axis, dim in sides:
        count = lax.axis_size(axis)
        ends = count - 1
        head = lax.slice_in_dim(cells, 0, width, axis=dim)
        tail = lax.slice_in_dim(cells, cells.shape[dim] - width, cells.shape[dim], axis=dim)
        cells = jnp.concatenate(
            [
                lax.ppermute(tail, axis, [(i, (i + 1) % count) for i in range(ends)]),
                cells,
                lax.ppermute(head, axis, [((i + 1) % count, i) for i in range(ends)]),
            ],
            axis=dim,
        )
    return cells


def front_exchange(cells, fields, width):
    for axis, dim in (("gx", 0), ("gy", 1)):
        count = lax.axis_size(axis)
        ends = count - 1
        field_dim = dim + 3
        head = lax.slice_in_dim(cells, 0, width, axis=dim)
        tail = lax.slice_in_dim(cells, cells.shape[dim] - width, cells.shape[dim], axis=dim)
        rim = lax.slice_in_dim(fields, 0, 1, axis=field_dim)
        lanes = cells.shape[-1]
        packed = jnp.concatenate([head.reshape(-1, lanes), rim.reshape(-1, lanes)], axis=0)
        packed = lax.ppermute(packed, axis, [((i + 1) % count, i) for i in range(ends)])
        split = head.size // lanes
        head = packed[:split].reshape(head.shape)
        rim = packed[split:].reshape(rim.shape)
        tail = lax.ppermute(tail, axis, [(i, (i + 1) % count) for i in range(ends)])
        cells = jnp.concatenate([tail, cells, head], axis=dim)
        fields = jnp.concatenate([fields, rim], axis=field_dim)
    return cells, fields


def from_behind(value, axis, steps):
    count = lax.axis_size(axis)
    initial, last = (max(0, -steps), min(count, count - steps))
    return lax.ppermute(value, axis, [(source, source + steps) for source in range(initial, last)])


def butterfly_sum(value, axis):
    count = lax.axis_size(axis)
    stride = 1
    while stride < count:
        value = value + lax.ppermute(value, axis, [(i, i ^ stride) for i in range(count)])
        stride *= 2
    return value


def filter_taps():
    tap_list = []
    for offset_x in range(-2, 3):
        for offset_y in range(-2, 3):
            for offset_z in range(-2, 3):
                weight = 3.0 - math.sqrt(
                    offset_x * offset_x + offset_y * offset_y + offset_z * offset_z
                )
                if weight > 0.0:
                    tap_list.append((offset_x, offset_y, offset_z, weight))
    return tap_list


def stencil(padded, block_shape):
    result = jnp.zeros(block_shape, jnp.float32)
    for offset_x, offset_y, offset_z, weight in filter_taps():
        result = (
            result
            + weight
            * padded[
                2 + offset_x : 2 + offset_x + block_shape[0],
                2 + offset_y : 2 + offset_y + block_shape[1],
                2 + offset_z : 2 + offset_z + block_shape[2],
            ]
        )
    return result


def element_terms(extended, stiffness, mass_matrix):
    pair_count = extended.shape[0]
    cells_x = extended.shape[3] - 1
    cells_y = extended.shape[4] - 1
    cells_z = extended.shape[5] - 1
    stiff_energy = jnp.zeros((cells_x * cells_y * cells_z,), jnp.float32)
    mass_energy = jnp.zeros((cells_x * cells_y * cells_z,), jnp.float32)
    for pair_index in range(pair_count):
        vectors = []
        for member in range(2):
            row_list = []
            for corner_x in (0, 1):
                for corner_y in (0, 1):
                    for corner_z in (0, 1):
                        for component in range(3):
                            row_list.append(
                                extended[
                                    pair_index,
                                    member,
                                    component,
                                    corner_x : corner_x + cells_x,
                                    corner_y : corner_y + cells_y,
                                    corner_z : corner_z + cells_z,
                                ].reshape(-1)
                            )
            vectors.append(jnp.stack(row_list))
        state_rows, adjoint_rows = vectors
        stiff_energy = stiff_energy + jnp.sum(
            state_rows * jnp.dot(stiffness, adjoint_rows, precision=lax.Precision.HIGHEST), axis=0
        )
        mass_energy = mass_energy + jnp.sum(
            state_rows * jnp.dot(mass_matrix, adjoint_rows, precision=lax.Precision.HIGHEST), axis=0
        )
    return (
        stiff_energy.reshape(cells_x, cells_y, cells_z),
        mass_energy.reshape(cells_x, cells_y, cells_z),
    )


CORNERS = [(a, b, d) for a in (0, 1) for b in (0, 1) for d in (0, 1)]


def energy_kernel(extended_ref, stiffness_ref, mass_ref, stiff_out, mass_out):
    pair_count = extended_ref.shape[0]
    cells_x, cells_y, cells_z = stiff_out.shape
    lane = lax.broadcasted_iota(jnp.int32, (cells_y, cells_z), 1)
    inside = lane < cells_z - 1

    def node_view(pair, member, component, x, corner):
        corner_x, corner_y, corner_z = corner
        value = extended_ref[pair, member, component, x + corner_x, pl.ds(corner_y, cells_y), :]
        if corner_z:
            value = jnp.where(inside, pltpu.roll(value, cells_z - 1, 1), 0.0)
        return value

    def over_pairs(pair, energies):
        stiff_sum, mass_sum, x = energies
        adjoint = [
            node_view(pair, 1, component, x, corner) for corner in CORNERS for component in range(3)
        ]
        for row in range(len(adjoint)):
            state = node_view(pair, 0, row % 3, x, CORNERS[row // 3])
            stiff_row = stiffness_ref[row, 0] * adjoint[0]
            mass_row = mass_ref[row, 0] * adjoint[0]
            for column in range(1, len(adjoint)):
                stiff_row = stiff_row + stiffness_ref[row, column] * adjoint[column]
                mass_row = mass_row + mass_ref[row, column] * adjoint[column]
            stiff_sum = stiff_sum + state * stiff_row
            mass_sum = mass_sum + state * mass_row
        return stiff_sum, mass_sum, x

    def over_x(x, carry):
        zero = jnp.zeros((cells_y, cells_z), jnp.float32)
        stiff_sum, mass_sum, _ = lax.fori_loop(0, pair_count, over_pairs, (zero, zero, x))
        stiff_out[x] = stiff_sum
        mass_out[x] = mass_sum
        return carry

    lax.fori_loop(0, cells_x, over_x, 0)


def mxu_energy_kernel(
    extended_ref, stiffness_ref, mass_ref, stiff_out, mass_out, coupling_ref, state_rows,
    adjoint_rows, products,
):
    pair_count = extended_ref.shape[0]
    cells_x, cells_y, cells_z = stiff_out.shape
    dofs = 3 * len(CORNERS)
    wide = dofs * cells_y
    spread_rows = (
        lax.broadcasted_iota(jnp.int32, (wide, dofs), 0) // cells_y
        == lax.broadcasted_iota(jnp.int32, (wide, dofs), 1)
    ).astype(jnp.float32)
    spread_columns = (
        lax.broadcasted_iota(jnp.int32, (dofs, wide), 0)
        == lax.broadcasted_iota(jnp.int32, (dofs, wide), 1) // cells_y
    ).astype(jnp.float32)
    same_y = (
        lax.broadcasted_iota(jnp.int32, (wide, wide), 0) % cells_y
        == lax.broadcasted_iota(jnp.int32, (wide, wide), 1) % cells_y
    )
    for block, matrix_ref in enumerate((stiffness_ref, mass_ref)):
        spread = jnp.dot(
            matrix_ref[...], spread_columns, precision=lax.Precision.HIGHEST,
            preferred_element_type=jnp.float32,
        )
        spread = jnp.dot(
            spread_rows, spread, precision=lax.Precision.HIGHEST, preferred_element_type=jnp.float32
        )
        coupling_ref[pl.ds(block * wide, wide), :] = jnp.where(same_y, spread, 0.0)
    lane = lax.broadcasted_iota(jnp.int32, (cells_y, cells_z), 1)
    inside = lane < cells_z - 1
    stiff_out[...] = jnp.zeros(stiff_out.shape, jnp.float32)
    mass_out[...] = jnp.zeros(mass_out.shape, jnp.float32)
    member_rows = (state_rows, adjoint_rows)

    def over_pairs(pair, carry):
        for node_x in range(cells_x + 1):
            for member in range(2):
                for component in range(3):
                    for corner_y in (0, 1):
                        base = extended_ref[
                            pair, member, component, node_x, pl.ds(corner_y, cells_y), :
                        ]
                        for corner_z in (0, 1):
                            value = base
                            if corner_z:
                                value = jnp.where(inside, pltpu.roll(base, cells_z - 1, 1), 0.0)
                            for corner_x in (0, 1):
                                x = node_x - corner_x
                                if 0 <= x < cells_x:
                                    corner = CORNERS.index((corner_x, corner_y, corner_z))
                                    row = 3 * corner + component
                                    member_rows[member][
                                        pl.ds(row * cells_y, cells_y), pl.ds(x * cells_z, cells_z)
                                    ] = value
        products[...] = jnp.dot(
            coupling_ref[...],
            adjoint_rows[...],
            precision=lax.Precision.HIGH,
            preferred_element_type=jnp.float32,
        )
        state = state_rows[...].reshape(dofs, cells_y, cells_x * cells_z)
        stiff_sum = jnp.sum(
            state * products[pl.ds(0, wide), :].reshape(dofs, cells_y, cells_x * cells_z), axis=0
        )
        mass_sum = jnp.sum(
            state * products[pl.ds(wide, wide), :].reshape(dofs, cells_y, cells_x * cells_z), axis=0
        )
        for x in range(cells_x):
            columns = slice(x * cells_z, (x + 1) * cells_z)
            stiff_out[x] = stiff_out[x] + stiff_sum[:, columns]
            mass_out[x] = mass_out[x] + mass_sum[:, columns]
        return carry

    lax.fori_loop(0, pair_count, over_pairs, 0)


def element_energies(extended, stiffness, mass_matrix):
    pair_count = extended.shape[0]
    cells = (extended.shape[3] - 1, extended.shape[4] - 1, extended.shape[5])
    voxels = cells[0] * cells[1] * cells[2]
    dofs = stiffness.shape[0]
    vmem = pl.BlockSpec(memory_space=pltpu.VMEM)
    return pl.pallas_call(
        mxu_energy_kernel,
        out_shape=(
            jax.ShapeDtypeStruct(cells, jnp.float32),
            jax.ShapeDtypeStruct(cells, jnp.float32),
        ),
        in_specs=[vmem, vmem, vmem],
        out_specs=(vmem, vmem),
        scratch_shapes=[
            pltpu.VMEM((2 * dofs * cells[1], dofs * cells[1]), jnp.float32),
            pltpu.VMEM((dofs * cells[1], cells[0] * cells[2]), jnp.float32),
            pltpu.VMEM((dofs * cells[1], cells[0] * cells[2]), jnp.float32),
            pltpu.VMEM((2 * dofs * cells[1], cells[0] * cells[2]), jnp.float32),
        ],
        cost_estimate=pl.CostEstimate(
            flops=pair_count * (4 * (dofs * cells[1]) ** 2 * cells[0] * cells[2] + 4 * dofs * voxels),
            bytes_accessed=extended.size * 4 + 2 * stiffness.size * 4 + 2 * voxels * 4,
            transcendentals=0,
        ),
    )(extended, stiffness, mass_matrix)


def shards(design, passive, basis_pairs, supports, stiffness, mass_matrix, volume_fraction):
    block_shape = design.shape
    size_x, size_y, size_z = block_shape
    devices_x = lax.axis_size("gx")
    devices_y = lax.axis_size("gy")
    index_x = lax.axis_index("gx")
    index_y = lax.axis_index("gy")
    grid_x = size_x * devices_x
    grid_y = size_y * devices_y
    spread_x = jnp.arange(size_x + 4, dtype=jnp.int32) + index_x * size_x - 2
    spread_y = jnp.arange(size_y + 4, dtype=jnp.int32) + index_y * size_y - 2
    valid_x = ((spread_x >= 0) & (spread_x < grid_x)).astype(jnp.float32)
    valid_y = ((spread_y >= 0) & (spread_y < grid_y)).astype(jnp.float32)
    valid_z = jnp.pad(jnp.ones((size_z,), jnp.float32), 2)
    inside = valid_x[:, None, None] * valid_y[None, :, None] * valid_z[None, None, :]
    weight_sum = stencil(inside, block_shape)
    fields = basis_pairs * (1 - supports).astype(jnp.float32)
    design_wide, extended = front_exchange(design, fields, 2)
    design_wide = jnp.pad(design_wide, ((0, 0), (0, 0), (2, 2)))
    physical = jnp.where(passive == 1, 1.0, stencil(design_wide, block_shape) / weight_sum)
    stiff_energy, mass_energy = element_energies(extended, stiffness, mass_matrix)
    raw_sensitivity = -(
        PENALTY_SCALE * physical * physical * stiff_energy - OMEGA_SQUARED * mass_energy
    )
    raw_sensitivity = jnp.where(passive == 1, 0.0, raw_sensitivity)
    scaled_wide = with_halo(raw_sensitivity / weight_sum, (("gy", 1), ("gx", 0)), 2)
    scaled_wide = jnp.pad(scaled_wide, ((0, 0), (0, 0), (2, 2)))
    sensitivity = stencil(scaled_wide, block_shape)
    benefit = jnp.maximum(-sensitivity, 0.0)
    floor_value = jnp.maximum(design - MOVE_LIMIT, 0.0)
    ceiling = jnp.minimum(design + MOVE_LIMIT, 1.0)
    band_cells = size_z // REGIONS
    target = volume_fraction * float(grid_x * grid_y * band_cells)

    def candidate(multiplier):
        per_cell = jnp.repeat(multiplier, band_cells)[None, None, :]
        trial = design * jnp.sqrt(benefit / per_cell)
        return jnp.where(passive == 1, 1.0, jnp.minimum(ceiling, jnp.maximum(floor_value, trial)))

    def region_sum(field):
        return jnp.sum(field, axis=(0, 1)).reshape(REGIONS, band_cells).sum(axis=1)

    levels = BISECT

    def bisect_round(round_index, bracket):
        low_end, high_end = bracket
        level_nodes = [(low_end, high_end)]
        midpoints = []
        for depth in range(levels):
            next_nodes = []
            for node_low, node_high in level_nodes:
                middle = jnp.sqrt(node_low * node_high)
                midpoints.append(middle)
                next_nodes.append((node_low, middle))
                next_nodes.append((middle, node_high))
            level_nodes = next_nodes
        trial_multipliers = jnp.stack(midpoints)
        per_cell = jnp.repeat(trial_multipliers, band_cells, axis=1)[:, None, None, :]
        trial = design[None] * jnp.sqrt(benefit[None] / per_cell)
        fields_of = jnp.where(
            passive[None] == 1, 1.0, jnp.minimum(ceiling[None], jnp.maximum(floor_value[None], trial))
        )
        partial_volumes = (
            jnp.sum(fields_of, axis=(1, 2)).reshape(len(midpoints), REGIONS, band_cells).sum(axis=2)
        )
        lanes = 128
        flat = partial_volumes.reshape(-1)
        spare = -flat.size % lanes
        dense = jnp.pad(flat, (0, spare)).reshape(-1, lanes)
        dense = butterfly_sum(butterfly_sum(dense, "gy"), "gx")
        volumes = dense.reshape(-1)[: flat.size].reshape(partial_volumes.shape)
        heavier_all = volumes > target[None, :]
        position = jnp.zeros((REGIONS,), jnp.int32)
        for depth in range(levels):
            middle = jnp.sqrt(low_end * high_end)
            nodes = lax.slice_in_dim(heavier_all, 2**depth - 1, 2 ** (depth + 1) - 1, axis=0)
            slots = lax.broadcasted_iota(jnp.int32, nodes.shape, 0)
            heavier = jnp.any(nodes & (slots == position[None, :]), axis=0)
            low_end = jnp.where(heavier, middle, low_end)
            high_end = jnp.where(heavier, high_end, middle)
            position = 2 * position + heavier.astype(jnp.int32)
        return (low_end, high_end)

    start = (jnp.full((REGIONS,), 0.0001, jnp.float32), jnp.full((REGIONS,), 10000.0, jnp.float32))
    low_end, high_end = bisect_round(0, start)
    design_next = candidate(jnp.sqrt(low_end * high_end))
    return (sensitivity, design_next)


def solution(mesh):
    placed = (
        P("gx", "gy", None),
        P("gx", "gy", None),
        P(None, None, None, "gx", "gy", None),
        P("gx", "gy", None),
        P(),
        P(),
        P(),
    )
    return jax.shard_map(
        shards,
        mesh=mesh,
        in_specs=placed,
        out_specs=(P("gx", "gy", None), P("gx", "gy", None)),
        check_vma=False,
    )
```

```python
import math

import jax
import jax.numpy as jnp
from jax import lax
from jax.sharding import PartitionSpec as P
from jax.experimental import pallas as pl
from jax.experimental.pallas import tpu as pltpu

BISECT = 6
REGIONS = 64


PENALTY_SCALE = 3.0 * (1.0 - 0.001)
OMEGA_SQUARED = 0.5
MOVE_LIMIT = 0.2


def with_halo(cells, sides, width):
    for axis, dim in sides:
        count = lax.axis_size(axis)
        ends = count - 1
        head = lax.slice_in_dim(cells, 0, width, axis=dim)
        tail = lax.slice_in_dim(cells, cells.shape[dim] - width, cells.shape[dim], axis=dim)
        cells = jnp.concatenate(
            [
                lax.ppermute(tail, axis, [(i, (i + 1) % count) for i in range(ends)]),
                cells,
                lax.ppermute(head, axis, [((i + 1) % count, i) for i in range(ends)]),
            ],
            axis=dim,
        )
    return cells


def front_exchange(cells, fields, width, first_rim):
    for axis, dim in (("gx", 0), ("gy", 1)):
        count = lax.axis_size(axis)
        ends = count - 1
        field_dim = dim + 3
        head = lax.slice_in_dim(cells, 0, width, axis=dim)
        tail = lax.slice_in_dim(cells, cells.shape[dim] - width, cells.shape[dim], axis=dim)
        rim = first_rim if axis == "gx" else lax.slice_in_dim(fields, 0, 1, axis=field_dim)
        lanes = cells.shape[-1]
        packed = jnp.concatenate([head.reshape(-1, lanes), rim.reshape(-1, lanes)], axis=0)
        packed = lax.ppermute(packed, axis, [((i + 1) % count, i) for i in range(ends)])
        split = head.size // lanes
        head = packed[:split].reshape(head.shape)
        rim = packed[split:].reshape(rim.shape)
        tail = lax.ppermute(tail, axis, [(i, (i + 1) % count) for i in range(ends)])
        cells = jnp.concatenate([tail, cells, head], axis=dim)
        fields = jnp.concatenate([fields, rim], axis=field_dim)
    return cells, fields


def from_behind(value, axis, steps):
    count = lax.axis_size(axis)
    initial, last = (max(0, -steps), min(count, count - steps))
    return lax.ppermute(value, axis, [(source, source + steps) for source in range(initial, last)])


def butterfly_sum(value, axis):
    count = lax.axis_size(axis)
    stride = 1
    while stride < count:
        value = value + lax.ppermute(value, axis, [(i, i ^ stride) for i in range(count)])
        stride *= 2
    return value


def filter_taps():
    tap_list = []
    for offset_x in range(-2, 3):
        for offset_y in range(-2, 3):
            for offset_z in range(-2, 3):
                weight = 3.0 - math.sqrt(
                    offset_x * offset_x + offset_y * offset_y + offset_z * offset_z
                )
                if weight > 0.0:
                    tap_list.append((offset_x, offset_y, offset_z, weight))
    return tap_list


def stencil(padded, block_shape):
    result = jnp.zeros(block_shape, jnp.float32)
    for offset_x, offset_y, offset_z, weight in filter_taps():
        result = (
            result
            + weight
            * padded[
                2 + offset_x : 2 + offset_x + block_shape[0],
                2 + offset_y : 2 + offset_y + block_shape[1],
                2 + offset_z : 2 + offset_z + block_shape[2],
            ]
        )
    return result


def element_terms(extended, stiffness, mass_matrix):
    pair_count = extended.shape[0]
    cells_x = extended.shape[3] - 1
    cells_y = extended.shape[4] - 1
    cells_z = extended.shape[5] - 1
    stiff_energy = jnp.zeros((cells_x * cells_y * cells_z,), jnp.float32)
    mass_energy = jnp.zeros((cells_x * cells_y * cells_z,), jnp.float32)
    for pair_index in range(pair_count):
        vectors = []
        for member in range(2):
            row_list = []
            for corner_x in (0, 1):
                for corner_y in (0, 1):
                    for corner_z in (0, 1):
                        for component in range(3):
                            row_list.append(
                                extended[
                                    pair_index,
                                    member,
                                    component,
                                    corner_x : corner_x + cells_x,
                                    corner_y : corner_y + cells_y,
                                    corner_z : corner_z + cells_z,
                                ].reshape(-1)
                            )
            vectors.append(jnp.stack(row_list))
        state_rows, adjoint_rows = vectors
        stiff_energy = stiff_energy + jnp.sum(
            state_rows * jnp.dot(stiffness, adjoint_rows, precision=lax.Precision.HIGHEST), axis=0
        )
        mass_energy = mass_energy + jnp.sum(
            state_rows * jnp.dot(mass_matrix, adjoint_rows, precision=lax.Precision.HIGHEST), axis=0
        )
    return (
        stiff_energy.reshape(cells_x, cells_y, cells_z),
        mass_energy.reshape(cells_x, cells_y, cells_z),
    )


CORNERS = [(a, b, d) for a in (0, 1) for b in (0, 1) for d in (0, 1)]


def energy_kernel(extended_ref, stiffness_ref, mass_ref, stiff_out, mass_out):
    pair_count = extended_ref.shape[0]
    cells_x, cells_y, cells_z = stiff_out.shape
    lane = lax.broadcasted_iota(jnp.int32, (cells_y, cells_z), 1)
    inside = lane < cells_z - 1

    def node_view(pair, member, component, x, corner):
        corner_x, corner_y, corner_z = corner
        value = extended_ref[pair, member, component, x + corner_x, pl.ds(corner_y, cells_y), :]
        if corner_z:
            value = jnp.where(inside, pltpu.roll(value, cells_z - 1, 1), 0.0)
        return value

    def over_pairs(pair, energies):
        stiff_sum, mass_sum, x = energies
        adjoint = [
            node_view(pair, 1, component, x, corner) for corner in CORNERS for component in range(3)
        ]
        for row in range(len(adjoint)):
            state = node_view(pair, 0, row % 3, x, CORNERS[row // 3])
            stiff_row = stiffness_ref[row, 0] * adjoint[0]
            mass_row = mass_ref[row, 0] * adjoint[0]
            for column in range(1, len(adjoint)):
                stiff_row = stiff_row + stiffness_ref[row, column] * adjoint[column]
                mass_row = mass_row + mass_ref[row, column] * adjoint[column]
            stiff_sum = stiff_sum + state * stiff_row
            mass_sum = mass_sum + state * mass_row
        return stiff_sum, mass_sum, x

    def over_x(x, carry):
        zero = jnp.zeros((cells_y, cells_z), jnp.float32)
        stiff_sum, mass_sum, _ = lax.fori_loop(0, pair_count, over_pairs, (zero, zero, x))
        stiff_out[x] = stiff_sum
        mass_out[x] = mass_sum
        return carry

    lax.fori_loop(0, cells_x, over_x, 0)


def mxu_energy_kernel(
    extended_ref, stiffness_ref, mass_ref, stiff_out, mass_out, coupling_ref, state_rows,
    adjoint_rows, products,
):
    pair_count = extended_ref.shape[0]
    cells_x, cells_y, cells_z = stiff_out.shape
    dofs = 3 * len(CORNERS)
    wide = dofs * cells_y
    spread_rows = (
        lax.broadcasted_iota(jnp.int32, (wide, dofs), 0) // cells_y
        == lax.broadcasted_iota(jnp.int32, (wide, dofs), 1)
    ).astype(jnp.float32)
    spread_columns = (
        lax.broadcasted_iota(jnp.int32, (dofs, wide), 0)
        == lax.broadcasted_iota(jnp.int32, (dofs, wide), 1) // cells_y
    ).astype(jnp.float32)
    same_y = (
        lax.broadcasted_iota(jnp.int32, (wide, wide), 0) % cells_y
        == lax.broadcasted_iota(jnp.int32, (wide, wide), 1) % cells_y
    )
    for block, matrix_ref in enumerate((stiffness_ref, mass_ref)):
        spread = jnp.dot(
            matrix_ref[...], spread_columns, precision=lax.Precision.HIGHEST,
            preferred_element_type=jnp.float32,
        )
        spread = jnp.dot(
            spread_rows, spread, precision=lax.Precision.HIGHEST, preferred_element_type=jnp.float32
        )
        coupling_ref[pl.ds(block * wide, wide), :] = jnp.where(same_y, spread, 0.0)
    lane = lax.broadcasted_iota(jnp.int32, (cells_y, cells_z), 1)
    inside = lane < cells_z - 1
    stiff_out[...] = jnp.zeros(stiff_out.shape, jnp.float32)
    mass_out[...] = jnp.zeros(mass_out.shape, jnp.float32)
    member_rows = (state_rows, adjoint_rows)

    def over_pairs(pair, carry):
        for node_x in range(cells_x + 1):
            for member in range(2):
                for component in range(3):
                    for corner_y in (0, 1):
                        base = extended_ref[
                            pair, member, component, node_x, pl.ds(corner_y, cells_y), :
                        ]
                        for corner_z in (0, 1):
                            value = base
                            if corner_z:
                                value = jnp.where(inside, pltpu.roll(base, cells_z - 1, 1), 0.0)
                            for corner_x in (0, 1):
                                x = node_x - corner_x
                                if 0 <= x < cells_x:
                                    corner = CORNERS.index((corner_x, corner_y, corner_z))
                                    row = 3 * corner + component
                                    member_rows[member][
                                        pl.ds(row * cells_y, cells_y), pl.ds(x * cells_z, cells_z)
                                    ] = value
        products[...] = jnp.dot(
            coupling_ref[...],
            adjoint_rows[...],
            precision=lax.Precision.HIGH,
            preferred_element_type=jnp.float32,
        )
        state = state_rows[...].reshape(dofs, cells_y, cells_x * cells_z)
        stiff_sum = jnp.sum(
            state * products[pl.ds(0, wide), :].reshape(dofs, cells_y, cells_x * cells_z), axis=0
        )
        mass_sum = jnp.sum(
            state * products[pl.ds(wide, wide), :].reshape(dofs, cells_y, cells_x * cells_z), axis=0
        )
        for x in range(cells_x):
            columns = slice(x * cells_z, (x + 1) * cells_z)
            stiff_out[x] = stiff_out[x] + stiff_sum[:, columns]
            mass_out[x] = mass_out[x] + mass_sum[:, columns]
        return carry

    lax.fori_loop(0, pair_count, over_pairs, 0)


def element_energies(extended, stiffness, mass_matrix):
    pair_count = extended.shape[0]
    cells = (extended.shape[3] - 1, extended.shape[4] - 1, extended.shape[5])
    voxels = cells[0] * cells[1] * cells[2]
    dofs = stiffness.shape[0]
    vmem = pl.BlockSpec(memory_space=pltpu.VMEM)
    return pl.pallas_call(
        mxu_energy_kernel,
        out_shape=(
            jax.ShapeDtypeStruct(cells, jnp.float32),
            jax.ShapeDtypeStruct(cells, jnp.float32),
        ),
        in_specs=[vmem, vmem, vmem],
        out_specs=(vmem, vmem),
        scratch_shapes=[
            pltpu.VMEM((2 * dofs * cells[1], dofs * cells[1]), jnp.float32),
            pltpu.VMEM((dofs * cells[1], cells[0] * cells[2]), jnp.float32),
            pltpu.VMEM((dofs * cells[1], cells[0] * cells[2]), jnp.float32),
            pltpu.VMEM((2 * dofs * cells[1], cells[0] * cells[2]), jnp.float32),
        ],
        cost_estimate=pl.CostEstimate(
            flops=pair_count * (4 * (dofs * cells[1]) ** 2 * cells[0] * cells[2] + 4 * dofs * voxels),
            bytes_accessed=extended.size * 4 + 2 * stiffness.size * 4 + 2 * voxels * 4,
            transcendentals=0,
        ),
    )(extended, stiffness, mass_matrix)


def shards(design, passive, basis_pairs, supports, stiffness, mass_matrix, volume_fraction):
    block_shape = design.shape
    size_x, size_y, size_z = block_shape
    devices_x = lax.axis_size("gx")
    devices_y = lax.axis_size("gy")
    index_x = lax.axis_index("gx")
    index_y = lax.axis_index("gy")
    grid_x = size_x * devices_x
    grid_y = size_y * devices_y
    spread_x = jnp.arange(size_x + 4, dtype=jnp.int32) + index_x * size_x - 2
    spread_y = jnp.arange(size_y + 4, dtype=jnp.int32) + index_y * size_y - 2
    valid_x = ((spread_x >= 0) & (spread_x < grid_x)).astype(jnp.float32)
    valid_y = ((spread_y >= 0) & (spread_y < grid_y)).astype(jnp.float32)
    valid_z = jnp.pad(jnp.ones((size_z,), jnp.float32), 2)
    inside = valid_x[:, None, None] * valid_y[None, :, None] * valid_z[None, None, :]
    weight_sum = stencil(inside, block_shape)
    fields = basis_pairs * (1 - supports).astype(jnp.float32)
    first_rim = basis_pairs[:, :, :, :1] * (1 - supports[:1]).astype(jnp.float32)
    design_wide, extended = front_exchange(design, fields, 2, first_rim)
    design_wide = jnp.pad(design_wide, ((0, 0), (0, 0), (2, 2)))
    physical = jnp.where(passive == 1, 1.0, stencil(design_wide, block_shape) / weight_sum)
    stiff_energy, mass_energy = element_energies(extended, stiffness, mass_matrix)
    raw_sensitivity = -(
        PENALTY_SCALE * physical * physical * stiff_energy - OMEGA_SQUARED * mass_energy
    )
    raw_sensitivity = jnp.where(passive == 1, 0.0, raw_sensitivity)
    scaled_wide = with_halo(raw_sensitivity / weight_sum, (("gx", 0), ("gy", 1)), 2)
    scaled_wide = jnp.pad(scaled_wide, ((0, 0), (0, 0), (2, 2)))
    sensitivity = stencil(scaled_wide, block_shape)
    benefit = jnp.maximum(-sensitivity, 0.0)
    floor_value = jnp.maximum(design - MOVE_LIMIT, 0.0)
    ceiling = jnp.minimum(design + MOVE_LIMIT, 1.0)
    band_cells = size_z // REGIONS
    target = volume_fraction * float(grid_x * grid_y * band_cells)

    def candidate(multiplier):
        per_cell = jnp.repeat(multiplier, band_cells)[None, None, :]
        trial = design * jnp.sqrt(benefit / per_cell)
        return jnp.where(passive == 1, 1.0, jnp.minimum(ceiling, jnp.maximum(floor_value, trial)))

    def region_sum(field):
        return jnp.sum(field, axis=(0, 1)).reshape(REGIONS, band_cells).sum(axis=1)

    levels = BISECT

    def bisect_round(round_index, bracket):
        low_end, high_end = bracket
        level_nodes = [(low_end, high_end)]
        midpoints = []
        for depth in range(levels):
            next_nodes = []
            for node_low, node_high in level_nodes:
                middle = jnp.sqrt(node_low * node_high)
                midpoints.append(middle)
                next_nodes.append((node_low, middle))
                next_nodes.append((middle, node_high))
            level_nodes = next_nodes
        trial_multipliers = jnp.stack(midpoints)
        per_cell = jnp.repeat(trial_multipliers, band_cells, axis=1)[:, None, None, :]
        trial = design[None] * jnp.sqrt(benefit[None] / per_cell)
        fields_of = jnp.where(
            passive[None] == 1, 1.0, jnp.minimum(ceiling[None], jnp.maximum(floor_value[None], trial))
        )
        partial_volumes = (
            jnp.sum(fields_of, axis=(1, 2)).reshape(len(midpoints), REGIONS, band_cells).sum(axis=2)
        )
        lanes = 128
        flat = partial_volumes.reshape(-1)
        spare = -flat.size % lanes
        dense = jnp.pad(flat, (0, spare)).reshape(-1, lanes)
        dense = butterfly_sum(butterfly_sum(dense, "gy"), "gx")
        volumes = dense.reshape(-1)[: flat.size].reshape(partial_volumes.shape)
        heavier_all = volumes > target[None, :]
        position = jnp.zeros((REGIONS,), jnp.int32)
        for depth in range(levels):
            middle = jnp.sqrt(low_end * high_end)
            nodes = lax.slice_in_dim(heavier_all, 2**depth - 1, 2 ** (depth + 1) - 1, axis=0)
            slots = lax.broadcasted_iota(jnp.int32, nodes.shape, 0)
            heavier = jnp.any(nodes & (slots == position[None, :]), axis=0)
            low_end = jnp.where(heavier, middle, low_end)
            high_end = jnp.where(heavier, high_end, middle)
            position = 2 * position + heavier.astype(jnp.int32)
        return (low_end, high_end)

    start = (jnp.full((REGIONS,), 0.0001, jnp.float32), jnp.full((REGIONS,), 10000.0, jnp.float32))
    low_end, high_end = bisect_round(0, start)
    design_next = candidate(jnp.sqrt(low_end * high_end))
    return (sensitivity, design_next)


def solution(mesh):
    placed = (
        P("gx", "gy", None),
        P("gx", "gy", None),
        P(None, None, None, "gx", "gy", None),
        P("gx", "gy", None),
        P(),
        P(),
        P(),
    )
    return jax.shard_map(
        shards,
        mesh=mesh,
        in_specs=placed,
        out_specs=(P("gx", "gy", None), P("gx", "gy", None)),
        check_vma=False,
    )
```
